32 devices in a mesh: groups: 2 (over y), context: 8 (over z, x), tensor: 2 (over core).
Axes of the slice: x: 2, y: 2, z: 4, core: 2. Of those that a mesh axis runs over, the one named last changes fastest.
Arguments:
- inputs: bfloat16 [8192, 2048], P('tensor', ('groups', 'context')), parts along dimension 1, may hold values from -12 to 12, as said below
- gate_medium: bfloat16 [8192, 2048], P('tensor', ('groups', 'context')), parts along dimension 1, may hold values from -6 to 6
- key_medium: bfloat16 [8192, 2048], P('tensor', ('groups', 'context')), parts along dimension 1, may hold values from -6 to 6
- gate_long: bfloat16 [8192, 2048], P('tensor', ('groups', 'context')), parts along dimension 1, may hold values from -6 to 6
- key_long: bfloat16 [8192, 2048], P('tensor', ('groups', 'context')), parts along dimension 1, may hold values from -6 to 6
- medium_taps: bfloat16 [512, 128], P('tensor'), may hold values from -0.5 to 0.5
- log_decay: float32 [8192, 16], P('tensor'), may hold values from 9.765625e-05 to 0.0768, as said below
- residues: float32 [8192, 16], P('tensor'), may hold values from -1.5 to 1.5
- norm_gain: float32 [8192], P('tensor'), may hold values from 0.1 to 1.9
Outputs:
- output: bfloat16 [8192, 2048], P('tensor', ('groups', 'context')), parts along dimension 1
The draws below stay inside these ranges and needn't reach their ends.
There are 2 independent parts, one for each index of `groups`. The reference program is written for one: setup_inputs(seed, part) draws one part's arguments, and reference() takes and returns one part's arrays. A program takes and returns all parts, laid end to end along the dimension named above; an argument that names none is the same for every part. Nothing has to cross between parts.
Inputs may be any that keep to these rules, and one draw needn't show every extreme that they name: `inputs`: block input; channel and token scales vary. `log_decay`: decay per token of each pole.
All inputs are finite; a program needn't handle non-finite values.
Results may differ from the reference program's by a relative error of at most 0.0045.
Values may be sent and summed in bfloat16 or wider, within the bound.
No kernel may reach another device: no remote copies, remote signals or barrier semaphores. Data moves between devices by JAX's collectives and lax.ppermute only.
A program may use at most 256 MiB of HBM per device.

```python
import math
import jax
import jax.numpy as jnp
from jax import lax

D = 8192
GROUP = 16
TAPS = 128
MODES = 16
STRING_POSITIONS = 1024


def draw_inputs(key, part):
    key_noise, key_chan, key_tok = jax.random.split(key, 3)
    ramp = 0.5 + jnp.arange(D, dtype=jnp.float32) / D
    chan_scale = jnp.exp(jax.random.uniform(key_chan, (D,), jnp.float32, math.log(0.3), math.log(3.0))) * ramp
    tok_scale = jnp.exp(jax.random.uniform(key_tok, (STRING_POSITIONS,), jnp.float32, math.log(0.5), math.log(2.0)))
    noise = jax.random.normal(key_noise, (D, STRING_POSITIONS), jnp.float32)
    return jnp.clip(noise * chan_scale[:, None] * tok_scale[None, :], -12.0, 12.0).astype(jnp.bfloat16)


def draw_log_decay(key, part):
    key_pick, key_slow, key_mid, key_fast = jax.random.split(key, 4)
    selector = jax.random.randint(key_pick, (D, MODES), 0, 16)
    slower = jnp.exp(jax.random.uniform(key_slow, (D, MODES), jnp.float32, math.log(0.1), math.log(2.3))) / STRING_POSITIONS
    middle_values = jnp.exp(jax.random.uniform(key_mid, (D, MODES), jnp.float32, math.log(2.3 / STRING_POSITIONS), math.log(0.046)))
    faster = jax.random.uniform(key_fast, (D, MODES), jnp.float32, 0.046, 0.0768)
    return jnp.where(selector < 8, slower, jnp.where(selector < 12, middle_values, faster))


def levels(stream_key, dims, cuts, smallest, top_value):
    def one(position, shards_of):
        draws = jax.random.uniform(jax.random.fold_in(jax.random.fold_in(stream_key, 6), position), (shards_of,), jnp.float32, smallest / len(cuts), top_value / len(cuts))
        return jnp.repeat(jnp.exp(draws), dims[position] // shards_of).reshape((-1,) + (1,) * (len(dims) - position - 1))

    gain = one(*cuts[0])
    for cut in cuts[1:]:
        gain = gain * one(*cut)
    return gain


def centred(key, extent, scale, reach, pieces=(), kind=jnp.bfloat16):
    drawn = jax.random.normal(key, extent, jnp.float32) * scale
    if len(pieces) > 0:
        drawn = levels(key, extent, pieces, -0.22, 0.18) * drawn
    return jnp.clip(drawn, min=-reach, max=reach).astype(kind)


def setup_inputs(seed: int = 0, part: int = 0) -> dict:
    seeds = jax.random.split(jax.random.key(seed), 10)
    part_keys = jax.random.split(jax.random.fold_in(seeds[9], part), 10)
    return {
        "inputs": draw_inputs(jax.random.fold_in(jax.random.fold_in(seeds[9], part), 71), part),
        "gate_medium": centred(part_keys[1], (D, STRING_POSITIONS), 1.0, 6.0, ((0, 2), (1, 8))),
        "key_medium": centred(part_keys[2], (D, STRING_POSITIONS), 1.0, 6.0, ((0, 2), (1, 8))),
        "gate_long": centred(part_keys[3], (D, STRING_POSITIONS), 1.0, 6.0, ((0, 2), (1, 8))),
        "key_long": centred(part_keys[4], (D, STRING_POSITIONS), 1.0, 6.0, ((0, 2), (1, 8))),
        "medium_taps": centred(seeds[5], (D // GROUP, TAPS), TAPS ** -0.5, 0.5, ((0, 2),)),
        "log_decay": draw_log_decay(jax.random.fold_in(seeds[9], 71), part),
        "residues": centred(seeds[7], (D, MODES), (MODES ** -0.5), 1.5, ((0, 2),), jnp.float32),
        "norm_gain": jnp.clip(1.0 + 0.18 * jax.random.normal(seeds[8], (D,), jnp.float32), 0.1, 1.9),
    }


def toeplitz_taps(taps):
    length = taps.shape[1]
    row_ids = jnp.arange(2 * length, dtype=jnp.int32)[:, None]
    col_ids = jnp.arange(length, dtype=jnp.int32)[None, :]
    lagged = col_ids + length - row_ids
    inside = (lagged >= 0) & (lagged < length)
    picked = jnp.take(taps, jnp.clip(lagged, 0, length - 1).astype(jnp.int32), axis=1)
    return jnp.where(inside[None], picked, jnp.zeros_like(picked))

def medium_conv(values, taps):
    padded = jnp.concatenate([jnp.zeros((D, TAPS), values.dtype), values], axis=1)
    tile_count = STRING_POSITIONS // TAPS
    leading = padded[:, :STRING_POSITIONS].reshape(D, tile_count, TAPS)
    trailing = padded[:, TAPS:].reshape(D, tile_count, TAPS)
    windows = jnp.concatenate([leading, trailing], axis=2).reshape(D // GROUP, GROUP, tile_count, 2 * TAPS)
    matrices = toeplitz_taps(taps)

    def one_group(pair):
        window, matrix = pair
        return jnp.einsum('jis,st->jit', window.astype(jnp.float32), matrix.astype(jnp.float32))
    result = lax.map(one_group, (windows, matrices))
    return result.reshape(D, STRING_POSITIONS)

def long_conv(values, log_decay, residues):
    block_size = math.gcd(D, 64)
    moment_indices = jnp.arange(STRING_POSITIONS, dtype=jnp.float32)

    def one_block(triple):
        signal, damping_ratios, weights = triple
        rescaled_entries = weights * jnp.sqrt(2.0 * damping_ratios)
        impulse_response = jnp.einsum('gj,gju->gu', rescaled_entries, jnp.exp(-damping_ratios[:, :, None] * moment_indices), precision=lax.Precision.HIGHEST)
        frequency_coefficients = jnp.fft.rfft(signal, n=2 * STRING_POSITIONS, axis=1) * jnp.fft.rfft(impulse_response, n=2 * STRING_POSITIONS, axis=1)
        return jnp.fft.irfft(frequency_coefficients, n=2 * STRING_POSITIONS, axis=1)[:, :STRING_POSITIONS]
    convolved = lax.map(one_block, (values.reshape(D // block_size, block_size, STRING_POSITIONS), log_decay.reshape(D // block_size, block_size, MODES), residues.reshape(D // block_size, block_size, MODES)))
    return convolved.reshape(D, STRING_POSITIONS)

def reference(inputs, gate_medium, key_medium, gate_long, key_long, medium_taps, log_decay, residues, norm_gain):
    source = inputs.astype(jnp.float32)
    values_medium = (key_medium.astype(jnp.float32) * source).astype(jnp.bfloat16)
    medium_out = medium_conv(values_medium, medium_taps)
    after_medium = source + gate_medium.astype(jnp.float32) * medium_out
    meansq = lax.optimization_barrier(jnp.mean(after_medium * after_medium, axis=0, keepdims=True))
    normed = after_medium * lax.rsqrt(meansq + 1e-05) * norm_gain[:, None]
    values_long = (key_long.astype(jnp.float32) * normed).astype(jnp.bfloat16)
    long_out = long_conv(values_long.astype(jnp.float32), log_decay, residues).astype(jnp.bfloat16)
    return (after_medium + gate_long.astype(jnp.float32) * long_out.astype(jnp.float32)).astype(jnp.bfloat16)
```

```python
import functools

import jax
import jax.numpy as jnp
from jax import lax
from jax.experimental import pallas as pl
from jax.experimental.pallas import tpu as pltpu
from jax.sharding import PartitionSpec as P

F32 = jnp.float32
BF16 = jnp.bfloat16
EPS = 1e-05
SUB, LANE = 8, 128
TILE = SUB * LANE


def shifted(block, axis, distance):
    devices = range(lax.axis_size(axis))
    route = [(i - distance, i) for i in devices if i - distance in devices]
    return lax.ppermute(block, axis, route)


def medium_kernel(x_ref, gm_ref, km_ref, rim_ref, taps_ref, am_ref, ss_ref):
    rows, length = x_ref.shape
    groups = taps_ref.shape[0]
    per_group = rows // groups
    row = lax.broadcasted_iota(jnp.int32, (length, length), 0)
    col = lax.broadcasted_iota(jnp.int32, (length, length), 1)
    upper = col >= row

    @pl.when(pl.program_id(0) == 0)
    def _():
        ss_ref[...] = jnp.zeros_like(ss_ref)

    acc = jnp.zeros((1, length), F32)
    for g in range(groups):
        lo, hi = g * per_group, (g + 1) * per_group
        taps = jnp.broadcast_to(taps_ref[g : g + 1, :].astype(F32), (length, length))
        rolled = pltpu.roll(taps, 0, 1, stride=1, stride_axis=0)
        t_cur = jnp.where(upper, rolled, 0.0).astype(BF16)
        t_rim = jnp.where(upper, 0.0, rolled).astype(BF16)
        x = x_ref[lo:hi, :].astype(F32)
        vm = (km_ref[lo:hi, :].astype(F32) * x).astype(BF16)
        conv = jnp.dot(vm, t_cur, preferred_element_type=F32) + jnp.dot(
            rim_ref[lo:hi, :], t_rim, preferred_element_type=F32
        )
        am = x + gm_ref[lo:hi, :].astype(F32) * conv
        am_ref[lo:hi, :] = am
        acc = acc + jnp.sum(am * am, axis=0, keepdims=True)
    ss_ref[...] += acc


def medium_call(inputs, gate_medium, key_medium, rim, taps):
    channels, length = inputs.shape
    per_group = channels // taps.shape[0]
    block = 256
    tap_block = block // per_group
    big = pl.BlockSpec((block, length), lambda b: (b, 0))
    return pl.pallas_call(
        medium_kernel,
        grid=(channels // block,),
        in_specs=[big, big, big, big, pl.BlockSpec((tap_block, length), lambda b: (b, 0))],
        out_specs=[big, pl.BlockSpec((1, length), lambda b: (0, 0))],
        out_shape=[
            jax.ShapeDtypeStruct((channels, length), F32),
            jax.ShapeDtypeStruct((1, length), F32),
        ],
        compiler_params=pltpu.CompilerParams(dimension_semantics=("arbitrary",)),
    )(inputs, gate_medium, key_medium, rim, taps)


def final_state_kernel(vt_ref, lam_ref, f_ref):
    modes = lam_ref.shape[0]
    length = vt_ref.shape[0]
    lam = [lam_ref[m] for m in range(modes)]

    def body(t, h):
        v = vt_ref[t].astype(F32)
        return tuple(lam[m] * h[m] + v for m in range(modes))

    h = lax.fori_loop(0, length, body, tuple(jnp.zeros((SUB, LANE), F32) for _ in range(modes)), unroll=8)
    for m in range(modes):
        f_ref[m] = h[m]


def output_kernel(vt_ref, lam_ref, w_ref, h0_ref, yt_ref):
    modes = lam_ref.shape[0]
    length = vt_ref.shape[0]
    lam = [lam_ref[m] for m in range(modes)]
    w = [w_ref[m] for m in range(modes)]

    def body(t, h):
        v = vt_ref[t].astype(F32)
        h = tuple(lam[m] * h[m] + v for m in range(modes))
        y = w[0] * h[0]
        for m in range(1, modes):
            y = y + w[m] * h[m]
        yt_ref[t] = y
        return h

    lax.fori_loop(0, length, body, tuple(h0_ref[m] for m in range(modes)), unroll=8)


def tiled_spec(lead):
    return pl.BlockSpec((lead, None, SUB, LANE), lambda b: (0, b, 0, 0))


def final_state_call(vt, lam):
    length, blocks = vt.shape[0], vt.shape[1]
    modes = lam.shape[0]
    return pl.pallas_call(
        final_state_kernel,
        grid=(blocks,),
        in_specs=[tiled_spec(length), tiled_spec(modes)],
        out_specs=tiled_spec(modes),
        out_shape=jax.ShapeDtypeStruct(lam.shape, F32),
    )(vt, lam)


def output_call(vt, lam, w, h0):
    length, blocks = vt.shape[0], vt.shape[1]
    modes = lam.shape[0]
    return pl.pallas_call(
        output_kernel,
        grid=(blocks,),
        in_specs=[tiled_spec(length), tiled_spec(modes), tiled_spec(modes), tiled_spec(modes)],
        out_specs=tiled_spec(length),
        out_shape=jax.ShapeDtypeStruct(vt.shape, F32),
    )(vt, lam, w, h0)


def to_tiles(a):
    channels, k = a.shape
    return a.T.reshape(k, channels // TILE, SUB, LANE)


def on_device(
    inputs,
    gate_medium,
    key_medium,
    gate_long,
    key_long,
    medium_taps,
    log_decay,
    residues,
    norm_gain,
):
    channels, length = inputs.shape
    assert length == medium_taps.shape[1]
    width = channels * lax.axis_size("tensor")
    source = inputs.astype(F32)
    values_medium = (key_medium.astype(F32) * source).astype(BF16)
    rim = shifted(values_medium, "context", 1)
    after_medium, partial = medium_call(inputs, gate_medium, key_medium, rim, medium_taps)
    totals = lax.psum(partial, "tensor")
    normed = after_medium * lax.rsqrt(totals / width + EPS) * norm_gain[:, None]
    values_long = (key_long.astype(F32) * normed).astype(BF16)

    vt = to_tiles(values_long)
    a_t = to_tiles(log_decay)
    lam = jnp.exp(-a_t)
    w = to_tiles(residues * jnp.sqrt(2.0 * log_decay))
    finals = final_state_call(vt, lam)

    carried = shifted(finals, "context", 1)
    distance = 1
    while distance < lax.axis_size("context"):
        decay = jnp.exp(-(length * distance) * a_t)
        carried = carried + decay * shifted(carried, "context", distance)
        distance *= 2

    yt = output_call(vt, lam, w, carried)
    long_out = yt.reshape(length, channels).T.astype(BF16)
    return (after_medium + gate_long.astype(F32) * long_out.astype(F32)).astype(BF16)


def solution(mesh):
    return jax.shard_map(
        on_device,
        mesh=mesh,
        in_specs=(
            P("tensor", ("groups", "context")),
            P("tensor", ("groups", "context")),
            P("tensor", ("groups", "context")),
            P("tensor", ("groups", "context")),
            P("tensor", ("groups", "context")),
            P("tensor", None),
            P("tensor", None),
            P("tensor", None),
            P("tensor"),
        ),
        out_specs=P("tensor", ("groups", "context")),
        check_vma=False,
    )
```

```python
import functools

import jax
import jax.numpy as jnp
from jax import lax
from jax.experimental import pallas as pl
from jax.experimental.pallas import tpu as pltpu
from jax.sharding import PartitionSpec as P

F32 = jnp.float32
BF16 = jnp.bfloat16
EPS = 1e-05
SUB, LANE = 8, 128
TILE = SUB * LANE


def shifted(block, axis, distance):
    devices = range(lax.axis_size(axis))
    route = [(i - distance, i) for i in devices if i - distance in devices]
    return lax.ppermute(block, axis, route)


def medium_kernel(x_ref, gm_ref, km_ref, rim_ref, taps_ref, am_ref, ss_ref):
    rows, length = x_ref.shape
    groups = taps_ref.shape[0]
    per_group = rows // groups
    row = lax.broadcasted_iota(jnp.int32, (length, length), 0)
    col = lax.broadcasted_iota(jnp.int32, (length, length), 1)
    upper = col >= row

    @pl.when(pl.program_id(0) == 0)
    def _():
        ss_ref[...] = jnp.zeros_like(ss_ref)

    acc = jnp.zeros((1, length), F32)
    for g in range(groups):
        lo, hi = g * per_group, (g + 1) * per_group
        taps = jnp.broadcast_to(taps_ref[g : g + 1, :].astype(F32), (length, length))
        rolled = pltpu.roll(taps, 0, 1, stride=1, stride_axis=0)
        t_cur = jnp.where(upper, rolled, 0.0).astype(BF16)
        t_rim = jnp.where(upper, 0.0, rolled).astype(BF16)
        x = x_ref[lo:hi, :].astype(F32)
        vm = (km_ref[lo:hi, :].astype(F32) * x).astype(BF16)
        conv = jnp.dot(vm, t_cur, preferred_element_type=F32) + jnp.dot(
            rim_ref[lo:hi, :], t_rim, preferred_element_type=F32
        )
        am = x + gm_ref[lo:hi, :].astype(F32) * conv
        am_ref[lo:hi, :] = am
        acc = acc + jnp.sum(am * am, axis=0, keepdims=True)
    ss_ref[...] += acc


def medium_call(inputs, gate_medium, key_medium, rim, taps):
    channels, length = inputs.shape
    per_group = channels // taps.shape[0]
    block = 256
    tap_block = block // per_group
    big = pl.BlockSpec((block, length), lambda b: (b, 0))
    return pl.pallas_call(
        medium_kernel,
        grid=(channels // block,),
        in_specs=[big, big, big, big, pl.BlockSpec((tap_block, length), lambda b: (b, 0))],
        out_specs=[big, pl.BlockSpec((1, length), lambda b: (0, 0))],
        out_shape=[
            jax.ShapeDtypeStruct((channels, length), F32),
            jax.ShapeDtypeStruct((1, length), F32),
        ],
        compiler_params=pltpu.CompilerParams(dimension_semantics=("arbitrary",)),
    )(inputs, gate_medium, key_medium, rim, taps)


def final_state_kernel(vt_ref, lam_ref, f_ref):
    modes = lam_ref.shape[0]
    length = vt_ref.shape[0]
    lam = [lam_ref[m] for m in range(modes)]

    def body(t, h):
        v = vt_ref[t].astype(F32)
        return tuple(lam[m] * h[m] + v for m in range(modes))

    h = lax.fori_loop(0, length, body, tuple(jnp.zeros((SUB, LANE), F32) for _ in range(modes)), unroll=8)
    for m in range(modes):
        f_ref[m] = h[m]


def output_kernel(vt_ref, lam_ref, w_ref, h0_ref, yt_ref):
    modes = lam_ref.shape[0]
    length = vt_ref.shape[0]
    lam = [lam_ref[m] for m in range(modes)]
    w = [w_ref[m] for m in range(modes)]

    def body(t, h):
        v = vt_ref[t].astype(F32)
        h = tuple(lam[m] * h[m] + v for m in range(modes))
        y = w[0] * h[0]
        for m in range(1, modes):
            y = y + w[m] * h[m]
        yt_ref[t] = y
        return h

    lax.fori_loop(0, length, body, tuple(h0_ref[m] for m in range(modes)), unroll=8)


def tiled_spec(lead):
    return pl.BlockSpec((lead, None, SUB, LANE), lambda b: (0, b, 0, 0))


def final_state_call(vt, lam):
    length, blocks = vt.shape[0], vt.shape[1]
    modes = lam.shape[0]
    return pl.pallas_call(
        final_state_kernel,
        grid=(blocks,),
        in_specs=[tiled_spec(length), tiled_spec(modes)],
        out_specs=tiled_spec(modes),
        out_shape=jax.ShapeDtypeStruct(lam.shape, F32),
    )(vt, lam)


def output_call(vt, lam, w, h0):
    length, blocks = vt.shape[0], vt.shape[1]
    modes = lam.shape[0]
    return pl.pallas_call(
        output_kernel,
        grid=(blocks,),
        in_specs=[tiled_spec(length), tiled_spec(modes), tiled_spec(modes), tiled_spec(modes)],
        out_specs=tiled_spec(length),
        out_shape=jax.ShapeDtypeStruct(vt.shape, F32),
    )(vt, lam, w, h0)


def to_tiles(a):
    channels, k = a.shape
    return a.T.reshape(k, channels // TILE, SUB, LANE)


def exclusive_scan(finals, a_t, length, count, first=4, radix=2):
    first = min(first, count)
    carried = shifted(finals, "context", 1)
    for j in range(2, first + 1):
        carried = carried + jnp.exp(-(length * (j - 1)) * a_t) * shifted(finals, "context", j)
    window = first
    while window < count:
        step = carried
        for j in range(1, radix):
            if j * window < count:
                decay = jnp.exp(-(length * j * window) * a_t)
                carried = carried + decay * shifted(step, "context", j * window)
        window *= radix
    return carried


def on_device(
    inputs,
    gate_medium,
    key_medium,
    gate_long,
    key_long,
    medium_taps,
    log_decay,
    residues,
    norm_gain,
):
    channels, length = inputs.shape
    assert length == medium_taps.shape[1]
    width = channels * lax.axis_size("tensor")
    source = inputs.astype(F32)
    values_medium = (key_medium.astype(F32) * source).astype(BF16)
    rim = shifted(values_medium, "context", 1)
    after_medium, partial = medium_call(inputs, gate_medium, key_medium, rim, medium_taps)
    totals = lax.psum(partial, "tensor")
    normed = after_medium * lax.rsqrt(totals / width + EPS) * norm_gain[:, None]
    values_long = (key_long.astype(F32) * normed).astype(BF16)

    vt = to_tiles(values_long)
    a_t = to_tiles(log_decay)
    lam = jnp.exp(-a_t)
    w = to_tiles(residues * jnp.sqrt(2.0 * log_decay))
    finals = final_state_call(vt, lam)

    carried = exclusive_scan(finals, a_t, length, lax.axis_size("context"))

    yt = output_call(vt, lam, w, carried)
    long_out = yt.reshape(length, channels).T.astype(BF16)
    return (after_medium + gate_long.astype(F32) * long_out.astype(F32)).astype(BF16)


def solution(mesh):
    return jax.shard_map(
        on_device,
        mesh=mesh,
        in_specs=(
            P("tensor", ("groups", "context")),
            P("tensor", ("groups", "context")),
            P("tensor", ("groups", "context")),
            P("tensor", ("groups", "context")),
            P("tensor", ("groups", "context")),
            P("tensor", None),
            P("tensor", None),
            P("tensor", None),
            P("tensor"),
        ),
        out_specs=P("tensor", ("groups", "context")),
        check_vma=False,
    )
```

```python
import functools

import jax
import jax.numpy as jnp
from jax import lax
from jax.experimental import pallas as pl
from jax.experimental.pallas import tpu as pltpu
from jax.sharding import PartitionSpec as P

F32 = jnp.float32
BF16 = jnp.bfloat16
EPS = 1e-05
SUB, LANE = 8, 128
TILE = SUB * LANE


def shifted(block, axis, distance):
    devices = range(lax.axis_size(axis))
    route = [(i - distance, i) for i in devices if i - distance in devices]
    return lax.ppermute(block, axis, route)


def medium_kernel(x_ref, gm_ref, km_ref, rim_ref, taps_ref, am_ref, ss_ref):
    rows, length = x_ref.shape
    groups = taps_ref.shape[0]
    per_group = rows // groups
    row = lax.broadcasted_iota(jnp.int32, (length, length), 0)
    col = lax.broadcasted_iota(jnp.int32, (length, length), 1)
    upper = col >= row

    @pl.when(pl.program_id(0) == 0)
    def _():
        ss_ref[...] = jnp.zeros_like(ss_ref)

    acc = jnp.zeros((1, length), F32)
    for g in range(groups):
        lo, hi = g * per_group, (g + 1) * per_group
        taps = jnp.broadcast_to(taps_ref[g : g + 1, :].astype(F32), (length, length))
        rolled = pltpu.roll(taps, 0, 1, stride=1, stride_axis=0)
        t_cur = jnp.where(upper, rolled, 0.0).astype(BF16)
        t_rim = jnp.where(upper, 0.0, rolled).astype(BF16)
        x = x_ref[lo:hi, :].astype(F32)
        vm = (km_ref[lo:hi, :].astype(F32) * x).astype(BF16)
        conv = jnp.dot(vm, t_cur, preferred_element_type=F32) + jnp.dot(
            rim_ref[lo:hi, :], t_rim, preferred_element_type=F32
        )
        am = x + gm_ref[lo:hi, :].astype(F32) * conv
        am_ref[lo:hi, :] = am
        acc = acc + jnp.sum(am * am, axis=0, keepdims=True)
    ss_ref[...] += acc


def medium_call(inputs, gate_medium, key_medium, rim, taps):
    channels, length = inputs.shape
    per_group = channels // taps.shape[0]
    block = 256
    tap_block = block // per_group
    big = pl.BlockSpec((block, length), lambda b: (b, 0))
    return pl.pallas_call(
        medium_kernel,
        grid=(channels // block,),
        in_specs=[big, big, big, big, pl.BlockSpec((tap_block, length), lambda b: (b, 0))],
        out_specs=[big, pl.BlockSpec((1, length), lambda b: (0, 0))],
        out_shape=[
            jax.ShapeDtypeStruct((channels, length), F32),
            jax.ShapeDtypeStruct((1, length), F32),
        ],
        compiler_params=pltpu.CompilerParams(dimension_semantics=("arbitrary",)),
    )(inputs, gate_medium, key_medium, rim, taps)


def final_state_kernel(vt_ref, lam_ref, f_ref):
    modes = lam_ref.shape[0]
    length = vt_ref.shape[0]
    lam = [lam_ref[m] for m in range(modes)]

    def body(t, h):
        v = vt_ref[t].astype(F32)
        return tuple(lam[m] * h[m] + v for m in range(modes))

    h = lax.fori_loop(0, length, body, tuple(jnp.zeros((SUB, LANE), F32) for _ in range(modes)), unroll=8)
    for m in range(modes):
        f_ref[m] = h[m]


def output_kernel(vt_ref, lam_ref, w_ref, h0_ref, yt_ref):
    modes = lam_ref.shape[0]
    length = vt_ref.shape[0]
    lam = [lam_ref[m] for m in range(modes)]
    w = [w_ref[m] for m in range(modes)]

    def body(t, h):
        v = vt_ref[t].astype(F32)
        h = tuple(lam[m] * h[m] + v for m in range(modes))
        y = w[0] * h[0]
        for m in range(1, modes):
            y = y + w[m] * h[m]
        yt_ref[t] = y
        return h

    lax.fori_loop(0, length, body, tuple(h0_ref[m] for m in range(modes)), unroll=8)


def tiled_spec(lead):
    return pl.BlockSpec((lead, None, SUB, LANE), lambda b: (0, b, 0, 0))


def final_state_call(vt, lam):
    length, blocks = vt.shape[0], vt.shape[1]
    modes = lam.shape[0]
    return pl.pallas_call(
        final_state_kernel,
        grid=(blocks,),
        in_specs=[tiled_spec(length), tiled_spec(modes)],
        out_specs=tiled_spec(modes),
        out_shape=jax.ShapeDtypeStruct(lam.shape, F32),
    )(vt, lam)


def output_call(vt, lam, w, h0):
    length, blocks = vt.shape[0], vt.shape[1]
    modes = lam.shape[0]
    return pl.pallas_call(
        output_kernel,
        grid=(blocks,),
        in_specs=[tiled_spec(length), tiled_spec(modes), tiled_spec(modes), tiled_spec(modes)],
        out_specs=tiled_spec(length),
        out_shape=jax.ShapeDtypeStruct(vt.shape, F32),
    )(vt, lam, w, h0)


def to_tiles(a):
    channels, k = a.shape
    return a.T.reshape(k, channels // TILE, SUB, LANE)


def exclusive_scan(finals, a_t, length, count, first=4, radix=2):
    first = min(first, count)
    carried = shifted(finals, "context", 1)
    for j in range(2, first + 1):
        carried = carried + jnp.exp(-(length * (j - 1)) * a_t) * shifted(finals, "context", j)
    window = first
    while window < count:
        step = carried
        for j in range(1, radix):
            if j * window < count:
                decay = jnp.exp(-(length * j * window) * a_t)
                carried = carried + decay * shifted(step, "context", j * window)
        window *= radix
    return carried


def gathered_scan(finals, a_t, length):
    count = lax.axis_size("context")
    everyone = lax.all_gather(finals, "context")
    gap = lax.axis_index("context") - 1 - jnp.arange(count)
    inside = (gap >= 0).reshape((count,) + (1,) * a_t.ndim)
    distance = (length * jnp.maximum(gap, 0)).astype(F32).reshape(inside.shape)
    decay = jnp.where(inside, jnp.exp(-distance * a_t[None]), 0.0)
    return jnp.sum(decay * everyone, axis=0)


def on_device(
    inputs,
    gate_medium,
    key_medium,
    gate_long,
    key_long,
    medium_taps,
    log_decay,
    residues,
    norm_gain,
):
    channels, length = inputs.shape
    assert length == medium_taps.shape[1]
    width = channels * lax.axis_size("tensor")
    source = inputs.astype(F32)
    values_medium = (key_medium.astype(F32) * source).astype(BF16)
    rim = shifted(values_medium, "context", 1)
    after_medium, partial = medium_call(inputs, gate_medium, key_medium, rim, medium_taps)
    totals = lax.psum(partial, "tensor")
    normed = after_medium * lax.rsqrt(totals / width + EPS) * norm_gain[:, None]
    values_long = (key_long.astype(F32) * normed).astype(BF16)

    vt = to_tiles(values_long)
    a_t = to_tiles(log_decay)
    lam = jnp.exp(-a_t)
    w = to_tiles(residues * jnp.sqrt(2.0 * log_decay))
    finals = final_state_call(vt, lam)

    carried = gathered_scan(finals, a_t, length)

    yt = output_call(vt, lam, w, carried)
    long_out = yt.reshape(length, channels).T.astype(BF16)
    return (after_medium + gate_long.astype(F32) * long_out.astype(F32)).astype(BF16)


def solution(mesh):
    return jax.shard_map(
        on_device,
        mesh=mesh,
        in_specs=(
            P("tensor", ("groups", "context")),
            P("tensor", ("groups", "context")),
            P("tensor", ("groups", "context")),
            P("tensor", ("groups", "context")),
            P("tensor", ("groups", "context")),
            P("tensor", None),
            P("tensor", None),
            P("tensor", None),
            P("tensor"),
        ),
        out_specs=P("tensor", ("groups", "context")),
        check_vma=False,
    )
```

```python
import functools

import jax
import jax.numpy as jnp
from jax import lax
from jax.experimental import pallas as pl
from jax.experimental.pallas import tpu as pltpu
from jax.sharding import PartitionSpec as P

F32 = jnp.float32
BF16 = jnp.bfloat16
EPS = 1e-05
SUB, LANE = 8, 128
TILE = SUB * LANE


def shifted(block, axis, distance):
    devices = range(lax.axis_size(axis))
    route = [(i - distance, i) for i in devices if i - distance in devices]
    return lax.ppermute(block, axis, route)


def medium_kernel(x_ref, gm_ref, km_ref, rim_ref, taps_ref, am_ref, ss_ref):
    rows, length = x_ref.shape
    groups = taps_ref.shape[0]
    per_group = rows // groups
    row = lax.broadcasted_iota(jnp.int32, (length, length), 0)
    col = lax.broadcasted_iota(jnp.int32, (length, length), 1)
    upper = col >= row

    @pl.when(pl.program_id(0) == 0)
    def _():
        ss_ref[...] = jnp.zeros_like(ss_ref)

    acc = jnp.zeros((1, length), F32)
    for g in range(groups):
        lo, hi = g * per_group, (g + 1) * per_group
        taps = jnp.broadcast_to(taps_ref[g : g + 1, :].astype(F32), (length, length))
        rolled = pltpu.roll(taps, 0, 1, stride=1, stride_axis=0)
        t_cur = jnp.where(upper, rolled, 0.0).astype(BF16)
        t_rim = jnp.where(upper, 0.0, rolled).astype(BF16)
        x = x_ref[lo:hi, :].astype(F32)
        vm = (km_ref[lo:hi, :].astype(F32) * x).astype(BF16)
        ext = jnp.concatenate([rim_ref[lo:hi, :], vm], axis=1)
        conv = jnp.dot(ext, jnp.concatenate([t_rim, t_cur], axis=0), preferred_element_type=F32)
        am = x + gm_ref[lo:hi, :].astype(F32) * conv
        am_ref[lo:hi, :] = am
        acc = acc + jnp.sum(am * am, axis=0, keepdims=True)
    ss_ref[...] += acc


def medium_call(inputs, gate_medium, key_medium, rim, taps):
    channels, length = inputs.shape
    per_group = channels // taps.shape[0]
    block = 256
    tap_block = block // per_group
    big = pl.BlockSpec((block, length), lambda b: (b, 0))
    return pl.pallas_call(
        medium_kernel,
        grid=(channels // block,),
        in_specs=[big, big, big, big, pl.BlockSpec((tap_block, length), lambda b: (b, 0))],
        out_specs=[big, pl.BlockSpec((1, length), lambda b: (0, 0))],
        out_shape=[
            jax.ShapeDtypeStruct((channels, length), F32),
            jax.ShapeDtypeStruct((1, length), F32),
        ],
        compiler_params=pltpu.CompilerParams(dimension_semantics=("arbitrary",)),
    )(inputs, gate_medium, key_medium, rim, taps)


def load_values(am_ref, kl_ref, g_ref, r_ref, vt_ref):
    r = r_ref[...]
    for i in range(SUB):
        rows = slice(i * LANE, (i + 1) * LANE)
        normed = am_ref[rows, :] * r * g_ref[rows, :]
        v = (kl_ref[rows, :].astype(F32) * normed).astype(BF16).astype(F32)
        vt_ref[pl.ds(i, LANE, stride=SUB), :] = v.T


def token_tile(ref, t):
    return ref[pl.ds(pl.multiple_of(t * SUB, SUB), SUB), :]


def final_state_kernel(am_ref, kl_ref, g_ref, r_ref, lam_ref, f_ref, vt_ref):
    modes = lam_ref.shape[0]
    length = am_ref.shape[1]
    load_values(am_ref, kl_ref, g_ref, r_ref, vt_ref)
    lam = [lam_ref[m] for m in range(modes)]

    def body(t, h):
        v = token_tile(vt_ref, t)
        return tuple(lam[m] * h[m] + v for m in range(modes))

    h = lax.fori_loop(0, length, body, tuple(jnp.zeros((SUB, LANE), F32) for _ in range(modes)), unroll=8)
    for m in range(modes):
        f_ref[m] = h[m]


def output_kernel(am_ref, kl_ref, gl_ref, g_ref, r_ref, lam_ref, w_ref, h0_ref, out_ref, vt_ref, yt_ref):
    modes = lam_ref.shape[0]
    length = am_ref.shape[1]
    load_values(am_ref, kl_ref, g_ref, r_ref, vt_ref)
    lam = [lam_ref[m] for m in range(modes)]
    w = [w_ref[m] for m in range(modes)]

    def body(t, h):
        v = token_tile(vt_ref, t)
        h = tuple(lam[m] * h[m] + v for m in range(modes))
        y = w[0] * h[0]
        for m in range(1, modes):
            y = y + w[m] * h[m]
        yt_ref[pl.ds(pl.multiple_of(t * SUB, SUB), SUB), :] = y
        return h

    lax.fori_loop(0, length, body, tuple(h0_ref[m] for m in range(modes)), unroll=8)
    for i in range(SUB):
        rows = slice(i * LANE, (i + 1) * LANE)
        long_out = yt_ref[pl.ds(i, LANE, stride=SUB), :].T.astype(BF16).astype(F32)
        out_ref[rows, :] = (am_ref[rows, :] + gl_ref[rows, :].astype(F32) * long_out).astype(BF16)


def tiled_spec(lead):
    return pl.BlockSpec((lead, None, SUB, LANE), lambda b: (0, b, 0, 0))


def final_state_call(am, kl, gain, r, lam):
    channels, length = am.shape
    modes = lam.shape[0]
    big = pl.BlockSpec((TILE, length), lambda b: (b, 0))
    return pl.pallas_call(
        final_state_kernel,
        grid=(channels // TILE,),
        in_specs=[big, big, pl.BlockSpec((TILE, 1), lambda b: (b, 0)), pl.BlockSpec((1, length), lambda b: (0, 0)), tiled_spec(modes)],
        out_specs=tiled_spec(modes),
        out_shape=jax.ShapeDtypeStruct(lam.shape, F32),
        scratch_shapes=[pltpu.VMEM((length * SUB, LANE), F32)],
    )(am, kl, gain, r, lam)


def output_call(am, kl, gl, gain, r, lam, w, h0):
    channels, length = am.shape
    modes = lam.shape[0]
    big = pl.BlockSpec((TILE, length), lambda b: (b, 0))
    return pl.pallas_call(
        output_kernel,
        grid=(channels // TILE,),
        in_specs=[big, big, big, pl.BlockSpec((TILE, 1), lambda b: (b, 0)), pl.BlockSpec((1, length), lambda b: (0, 0)), tiled_spec(modes), tiled_spec(modes), tiled_spec(modes)],
        out_specs=big,
        out_shape=jax.ShapeDtypeStruct((channels, length), BF16),
        scratch_shapes=[pltpu.VMEM((length * SUB, LANE), F32), pltpu.VMEM((length * SUB, LANE), F32)],
    )(am, kl, gl, gain, r, lam, w, h0)


def to_tiles(a):
    channels, k = a.shape
    return a.T.reshape(k, channels // TILE, SUB, LANE)


def on_device(
    inputs,
    gate_medium,
    key_medium,
    gate_long,
    key_long,
    medium_taps,
    log_decay,
    residues,
    norm_gain,
):
    channels, length = inputs.shape
    assert length == medium_taps.shape[1]
    width = channels * lax.axis_size("tensor")
    source = inputs.astype(F32)
    values_medium = (key_medium.astype(F32) * source).astype(BF16)
    rim = shifted(values_medium, "context", 1)
    after_medium, partial = medium_call(inputs, gate_medium, key_medium, rim, medium_taps)
    totals = lax.psum(partial, "tensor")
    r = lax.rsqrt(totals / width + EPS)
    gain = norm_gain[:, None]
    a_t = to_tiles(log_decay)
    lam = jnp.exp(-a_t)
    w = to_tiles(residues * jnp.sqrt(2.0 * log_decay))
    finals = final_state_call(after_medium, key_long, gain, r, lam)

    carried = shifted(finals, "context", 1)
    distance = 1
    while distance < lax.axis_size("context"):
        decay = jnp.exp(-(length * distance) * a_t)
        carried = carried + decay * shifted(carried, "context", distance)
        distance *= 2

    return output_call(after_medium, key_long, gate_long, gain, r, lam, w, carried)


def solution(mesh):
    return jax.shard_map(
        on_device,
        mesh=mesh,
        in_specs=(
            P("tensor", ("groups", "context")),
            P("tensor", ("groups", "context")),
            P("tensor", ("groups", "context")),
            P("tensor", ("groups", "context")),
            P("tensor", ("groups", "context")),
            P("tensor", None),
            P("tensor", None),
            P("tensor", None),
            P("tensor"),
        ),
        out_specs=P("tensor", ("groups", "context")),
        check_vma=False,
    )
```

```python
import functools

import jax
import jax.numpy as jnp
from jax import lax
from jax.experimental import pallas as pl
from jax.experimental.pallas import tpu as pltpu
from jax.sharding import PartitionSpec as P

F32 = jnp.float32
BF16 = jnp.bfloat16
EPS = 1e-05
SUB, LANE = 8, 128
TILE = SUB * LANE


def shifted(block, axis, distance):
    devices = range(lax.axis_size(axis))
    route = [(i - distance, i) for i in devices if i - distance in devices]
    return lax.ppermute(block, axis, route)


def tap_toeplitz(taps_ref, g, length, upper):
    taps = jnp.broadcast_to(taps_ref[g : g + 1, :].astype(F32), (length, length))
    rolled = pltpu.roll(taps, 0, 1, stride=1, stride_axis=0)
    if upper:
        return jnp.where(tap_mask(length), rolled, 0.0).astype(BF16)
    return jnp.where(tap_mask(length), 0.0, rolled).astype(BF16)


def tap_mask(length):
    row = lax.broadcasted_iota(jnp.int32, (length, length), 0)
    col = lax.broadcasted_iota(jnp.int32, (length, length), 1)
    return col >= row


def current_kernel(x_ref, km_ref, taps_ref, conv_ref):
    rows, length = x_ref.shape
    groups = taps_ref.shape[0]
    per_group = rows // groups
    for g in range(groups):
        lo, hi = g * per_group, (g + 1) * per_group
        vm = (km_ref[lo:hi, :].astype(F32) * x_ref[lo:hi, :].astype(F32)).astype(BF16)
        conv_ref[lo:hi, :] = jnp.dot(vm, tap_toeplitz(taps_ref, g, length, True), preferred_element_type=F32)


def rim_kernel(conv_ref, x_ref, gm_ref, rim_ref, taps_ref, am_ref, ss_ref):
    rows, length = x_ref.shape
    groups = taps_ref.shape[0]
    per_group = rows // groups

    @pl.when(pl.program_id(0) == 0)
    def _():
        ss_ref[...] = jnp.zeros_like(ss_ref)

    acc = jnp.zeros((1, length), F32)
    for g in range(groups):
        lo, hi = g * per_group, (g + 1) * per_group
        conv = conv_ref[lo:hi, :] + jnp.dot(
            rim_ref[lo:hi, :], tap_toeplitz(taps_ref, g, length, False), preferred_element_type=F32
        )
        am = x_ref[lo:hi, :].astype(F32) + gm_ref[lo:hi, :].astype(F32) * conv
        am_ref[lo:hi, :] = am
        acc = acc + jnp.sum(am * am, axis=0, keepdims=True)
    ss_ref[...] += acc


def medium_call(inputs, gate_medium, key_medium, rim, taps):
    channels, length = inputs.shape
    per_group = channels // taps.shape[0]
    block = 256
    tap_block = block // per_group
    big = pl.BlockSpec((block, length), lambda b: (b, 0))
    tap_spec = pl.BlockSpec((tap_block, length), lambda b: (b, 0))
    conv = pl.pallas_call(
        current_kernel,
        grid=(channels // block,),
        in_specs=[big, big, tap_spec],
        out_specs=big,
        out_shape=jax.ShapeDtypeStruct((channels, length), F32),
    )(inputs, key_medium, taps)
    return pl.pallas_call(
        rim_kernel,
        grid=(channels // block,),
        in_specs=[big, big, big, big, tap_spec],
        out_specs=[big, pl.BlockSpec((1, length), lambda b: (0, 0))],
        out_shape=[
            jax.ShapeDtypeStruct((channels, length), F32),
            jax.ShapeDtypeStruct((1, length), F32),
        ],
        compiler_params=pltpu.CompilerParams(dimension_semantics=("arbitrary",)),
    )(conv, inputs, gate_medium, rim, taps)


def load_values(am_ref, kl_ref, g_ref, r_ref, vt_ref):
    r = r_ref[...]
    for i in range(SUB):
        rows = slice(i * LANE, (i + 1) * LANE)
        normed = am_ref[rows, :] * r * g_ref[rows, :]
        v = (kl_ref[rows, :].astype(F32) * normed).astype(BF16).astype(F32)
        vt_ref[pl.ds(i, LANE, stride=SUB), :] = v.T


def token_tile(ref, t):
    return ref[pl.ds(pl.multiple_of(t * SUB, SUB), SUB), :]


def final_state_kernel(am_ref, kl_ref, g_ref, r_ref, lam_ref, f_ref, vt_ref):
    modes = lam_ref.shape[0]
    length = am_ref.shape[1]
    load_values(am_ref, kl_ref, g_ref, r_ref, vt_ref)
    lam = [lam_ref[m] for m in range(modes)]

    def body(t, h):
        v = token_tile(vt_ref, t)
        return tuple(lam[m] * h[m] + v for m in range(modes))

    h = lax.fori_loop(0, length, body, tuple(jnp.zeros((SUB, LANE), F32) for _ in range(modes)), unroll=8)
    for m in range(modes):
        f_ref[m] = h[m]


def output_kernel(am_ref, kl_ref, gl_ref, g_ref, r_ref, lam_ref, w_ref, h0_ref, out_ref, vt_ref, yt_ref):
    modes = lam_ref.shape[0]
    length = am_ref.shape[1]
    load_values(am_ref, kl_ref, g_ref, r_ref, vt_ref)
    lam = [lam_ref[m] for m in range(modes)]
    w = [w_ref[m] for m in range(modes)]

    def body(t, h):
        v = token_tile(vt_ref, t)
        h = tuple(lam[m] * h[m] + v for m in range(modes))
        y = w[0] * h[0]
        for m in range(1, modes):
            y = y + w[m] * h[m]
        yt_ref[pl.ds(pl.multiple_of(t * SUB, SUB), SUB), :] = y
        return h

    lax.fori_loop(0, length, body, tuple(h0_ref[m] for m in range(modes)), unroll=8)
    for i in range(SUB):
        rows = slice(i * LANE, (i + 1) * LANE)
        long_out = yt_ref[pl.ds(i, LANE, stride=SUB), :].T.astype(BF16).astype(F32)
        out_ref[rows, :] = (am_ref[rows, :] + gl_ref[rows, :].astype(F32) * long_out).astype(BF16)


def tiled_spec(lead):
    return pl.BlockSpec((lead, None, SUB, LANE), lambda b: (0, b, 0, 0))


def final_state_call(am, kl, gain, r, lam):
    channels, length = am.shape
    modes = lam.shape[0]
    big = pl.BlockSpec((TILE, length), lambda b: (b, 0))
    return pl.pallas_call(
        final_state_kernel,
        grid=(channels // TILE,),
        in_specs=[big, big, pl.BlockSpec((TILE, 1), lambda b: (b, 0)), pl.BlockSpec((1, length), lambda b: (0, 0)), tiled_spec(modes)],
        out_specs=tiled_spec(modes),
        out_shape=jax.ShapeDtypeStruct(lam.shape, F32),
        scratch_shapes=[pltpu.VMEM((length * SUB, LANE), F32)],
    )(am, kl, gain, r, lam)


def output_call(am, kl, gl, gain, r, lam, w, h0):
    channels, length = am.shape
    modes = lam.shape[0]
    big = pl.BlockSpec((TILE, length), lambda b: (b, 0))
    return pl.pallas_call(
        output_kernel,
        grid=(channels // TILE,),
        in_specs=[big, big, big, pl.BlockSpec((TILE, 1), lambda b: (b, 0)), pl.BlockSpec((1, length), lambda b: (0, 0)), tiled_spec(modes), tiled_spec(modes), tiled_spec(modes)],
        out_specs=big,
        out_shape=jax.ShapeDtypeStruct((channels, length), BF16),
        scratch_shapes=[pltpu.VMEM((length * SUB, LANE), F32), pltpu.VMEM((length * SUB, LANE), F32)],
    )(am, kl, gl, gain, r, lam, w, h0)


def to_tiles(a):
    channels, k = a.shape
    return a.T.reshape(k, channels // TILE, SUB, LANE)


def on_device(
    inputs,
    gate_medium,
    key_medium,
    gate_long,
    key_long,
    medium_taps,
    log_decay,
    residues,
    norm_gain,
):
    channels, length = inputs.shape
    assert length == medium_taps.shape[1]
    width = channels * lax.axis_size("tensor")
    source = inputs.astype(F32)
    values_medium = (key_medium.astype(F32) * source).astype(BF16)
    rim = shifted(values_medium, "context", 1)
    after_medium, partial = medium_call(inputs, gate_medium, key_medium, rim, medium_taps)
    totals = lax.psum(partial, "tensor")
    r = lax.rsqrt(totals / width + EPS)
    gain = norm_gain[:, None]
    a_t = to_tiles(log_decay)
    lam = jnp.exp(-a_t)
    w = to_tiles(residues * jnp.sqrt(2.0 * log_decay))
    finals = final_state_call(after_medium, key_long, gain, r, lam)

    carried = shifted(finals, "context", 1)
    distance = 1
    while distance < lax.axis_size("context"):
        decay = jnp.exp(-(length * distance) * a_t)
        carried = carried + decay * shifted(carried, "context", distance)
        distance *= 2

    return output_call(after_medium, key_long, gate_long, gain, r, lam, w, carried)


def solution(mesh):
    return jax.shard_map(
        on_device,
        mesh=mesh,
        in_specs=(
            P("tensor", ("groups", "context")),
            P("tensor", ("groups", "context")),
            P("tensor", ("groups", "context")),
            P("tensor", ("groups", "context")),
            P("tensor", ("groups", "context")),
            P("tensor", None),
            P("tensor", None),
            P("tensor", None),
            P("tensor"),
        ),
        out_specs=P("tensor", ("groups", "context")),
        check_vma=False,
    )
```

```python
import functools

import jax
import jax.numpy as jnp
from jax import lax
from jax.experimental import pallas as pl
from jax.experimental.pallas import tpu as pltpu
from jax.sharding import PartitionSpec as P

F32 = jnp.float32
BF16 = jnp.bfloat16
EPS = 1e-05
SUB, LANE = 8, 128
TILE = SUB * LANE


def shifted(block, axis, distance):
    devices = range(lax.axis_size(axis))
    route = [(i - distance, i) for i in devices if i - distance in devices]
    return lax.ppermute(block, axis, route)


def tap_mask(length):
    row = lax.broadcasted_iota(jnp.int32, (length, length), 0)
    col = lax.broadcasted_iota(jnp.int32, (length, length), 1)
    return col >= row


def current_kernel(x_ref, km_ref, taps_ref, conv_ref, t_rim_ref):
    rows, length = x_ref.shape
    groups = taps_ref.shape[0]
    per_group = rows // groups
    upper = tap_mask(length)
    for g in range(groups):
        lo, hi = g * per_group, (g + 1) * per_group
        taps = jnp.broadcast_to(taps_ref[g : g + 1, :].astype(F32), (length, length))
        rolled = pltpu.roll(taps, 0, 1, stride=1, stride_axis=0)
        t_cur = jnp.where(upper, rolled, 0.0).astype(BF16)
        t_rim_ref[g * length : (g + 1) * length, :] = jnp.where(upper, 0.0, rolled).astype(BF16)
        vm = (km_ref[lo:hi, :].astype(F32) * x_ref[lo:hi, :].astype(F32)).astype(BF16)
        conv_ref[lo:hi, :] = jnp.dot(vm, t_cur, preferred_element_type=F32)


def rim_kernel(conv_ref, x_ref, gm_ref, rim_ref, t_rim_ref, am_ref, ss_ref):
    rows, length = x_ref.shape
    groups = t_rim_ref.shape[0] // length
    per_group = rows // groups

    @pl.when(pl.program_id(0) == 0)
    def _():
        ss_ref[...] = jnp.zeros_like(ss_ref)

    acc = jnp.zeros((1, length), F32)
    for g in range(groups):
        lo, hi = g * per_group, (g + 1) * per_group
        conv = conv_ref[lo:hi, :] + jnp.dot(
            rim_ref[lo:hi, :], t_rim_ref[g * length : (g + 1) * length, :], preferred_element_type=F32
        )
        am = x_ref[lo:hi, :].astype(F32) + gm_ref[lo:hi, :].astype(F32) * conv
        am_ref[lo:hi, :] = am
        acc = acc + jnp.sum(am * am, axis=0, keepdims=True)
    ss_ref[...] += acc


def medium_call(inputs, gate_medium, key_medium, rim, taps):
    channels, length = inputs.shape
    filters = taps.shape[0]
    per_group = channels // filters
    block = 256
    tap_block = block // per_group
    big = pl.BlockSpec((block, length), lambda b: (b, 0))
    t_spec = pl.BlockSpec((tap_block * length, length), lambda b: (b, 0))
    conv, t_rim = pl.pallas_call(
        current_kernel,
        grid=(channels // block,),
        in_specs=[big, big, pl.BlockSpec((tap_block, length), lambda b: (b, 0))],
        out_specs=[big, t_spec],
        out_shape=[
            jax.ShapeDtypeStruct((channels, length), F32),
            jax.ShapeDtypeStruct((filters * length, length), BF16),
        ],
    )(inputs, key_medium, taps)
    return pl.pallas_call(
        rim_kernel,
        grid=(channels // block,),
        in_specs=[big, big, big, big, t_spec],
        out_specs=[big, pl.BlockSpec((1, length), lambda b: (0, 0))],
        out_shape=[
            jax.ShapeDtypeStruct((channels, length), F32),
            jax.ShapeDtypeStruct((1, length), F32),
        ],
        compiler_params=pltpu.CompilerParams(dimension_semantics=("arbitrary",)),
    )(conv, inputs, gate_medium, rim, t_rim)


def load_values(am_ref, kl_ref, g_ref, r_ref, vt_ref):
    r = r_ref[...]
    for i in range(SUB):
        rows = slice(i * LANE, (i + 1) * LANE)
        normed = am_ref[rows, :] * r * g_ref[rows, :]
        v = (kl_ref[rows, :].astype(F32) * normed).astype(BF16).astype(F32)
        vt_ref[pl.ds(i, LANE, stride=SUB), :] = v.T


def token_tile(ref, t):
    return ref[pl.ds(pl.multiple_of(t * SUB, SUB), SUB), :]


def final_state_kernel(am_ref, kl_ref, g_ref, r_ref, lam_ref, f_ref, vt_ref):
    modes = lam_ref.shape[0]
    length = am_ref.shape[1]
    load_values(am_ref, kl_ref, g_ref, r_ref, vt_ref)
    lam = [lam_ref[m] for m in range(modes)]

    def body(t, h):
        v = token_tile(vt_ref, t)
        return tuple(lam[m] * h[m] + v for m in range(modes))

    h = lax.fori_loop(0, length, body, tuple(jnp.zeros((SUB, LANE), F32) for _ in range(modes)), unroll=8)
    for m in range(modes):
        f_ref[m] = h[m]


def output_kernel(am_ref, kl_ref, gl_ref, g_ref, r_ref, lam_ref, w_ref, h0_ref, out_ref, vt_ref, yt_ref):
    modes = lam_ref.shape[0]
    length = am_ref.shape[1]
    load_values(am_ref, kl_ref, g_ref, r_ref, vt_ref)
    lam = [lam_ref[m] for m in range(modes)]
    w = [w_ref[m] for m in range(modes)]

    def body(t, h):
        v = token_tile(vt_ref, t)
        h = tuple(lam[m] * h[m] + v for m in range(modes))
        y = w[0] * h[0]
        for m in range(1, modes):
            y = y + w[m] * h[m]
        yt_ref[pl.ds(pl.multiple_of(t * SUB, SUB), SUB), :] = y
        return h

    lax.fori_loop(0, length, body, tuple(h0_ref[m] for m in range(modes)), unroll=8)
    for i in range(SUB):
        rows = slice(i * LANE, (i + 1) * LANE)
        long_out = yt_ref[pl.ds(i, LANE, stride=SUB), :].T.astype(BF16).astype(F32)
        out_ref[rows, :] = (am_ref[rows, :] + gl_ref[rows, :].astype(F32) * long_out).astype(BF16)


def tiled_spec(lead):
    return pl.BlockSpec((lead, None, SUB, LANE), lambda b: (0, b, 0, 0))


def final_state_call(am, kl, gain, r, lam):
    channels, length = am.shape
    modes = lam.shape[0]
    big = pl.BlockSpec((TILE, length), lambda b: (b, 0))
    return pl.pallas_call(
        final_state_kernel,
        grid=(channels // TILE,),
        in_specs=[big, big, pl.BlockSpec((TILE, 1), lambda b: (b, 0)), pl.BlockSpec((1, length), lambda b: (0, 0)), tiled_spec(modes)],
        out_specs=tiled_spec(modes),
        out_shape=jax.ShapeDtypeStruct(lam.shape, F32),
        scratch_shapes=[pltpu.VMEM((length * SUB, LANE), F32)],
    )(am, kl, gain, r, lam)


def output_call(am, kl, gl, gain, r, lam, w, h0):
    channels, length = am.shape
    modes = lam.shape[0]
    big = pl.BlockSpec((TILE, length), lambda b: (b, 0))
    return pl.pallas_call(
        output_kernel,
        grid=(channels // TILE,),
        in_specs=[big, big, big, pl.BlockSpec((TILE, 1), lambda b: (b, 0)), pl.BlockSpec((1, length), lambda b: (0, 0)), tiled_spec(modes), tiled_spec(modes), tiled_spec(modes)],
        out_specs=big,
        out_shape=jax.ShapeDtypeStruct((channels, length), BF16),
        scratch_shapes=[pltpu.VMEM((length * SUB, LANE), F32), pltpu.VMEM((length * SUB, LANE), F32)],
    )(am, kl, gl, gain, r, lam, w, h0)


def to_tiles(a):
    channels, k = a.shape
    return a.T.reshape(k, channels // TILE, SUB, LANE)


def on_device(
    inputs,
    gate_medium,
    key_medium,
    gate_long,
    key_long,
    medium_taps,
    log_decay,
    residues,
    norm_gain,
):
    channels, length = inputs.shape
    assert length == medium_taps.shape[1]
    width = channels * lax.axis_size("tensor")
    source = inputs.astype(F32)
    values_medium = (key_medium.astype(F32) * source).astype(BF16)
    rim = shifted(values_medium, "context", 1)
    after_medium, partial = medium_call(inputs, gate_medium, key_medium, rim, medium_taps)
    totals = lax.psum(partial, "tensor")
    r = lax.rsqrt(totals / width + EPS)
    gain = norm_gain[:, None]
    a_t = to_tiles(log_decay)
    lam = jnp.exp(-a_t)
    w = to_tiles(residues * jnp.sqrt(2.0 * log_decay))
    finals = final_state_call(after_medium, key_long, gain, r, lam)

    carried = shifted(finals, "context", 1)
    distance = 1
    while distance < lax.axis_size("context"):
        decay = jnp.exp(-(length * distance) * a_t)
        carried = carried + decay * shifted(carried, "context", distance)
        distance *= 2

    return output_call(after_medium, key_long, gate_long, gain, r, lam, w, carried)


def solution(mesh):
    return jax.shard_map(
        on_device,
        mesh=mesh,
        in_specs=(
            P("tensor", ("groups", "context")),
            P("tensor", ("groups", "context")),
            P("tensor", ("groups", "context")),
            P("tensor", ("groups", "context")),
            P("tensor", ("groups", "context")),
            P("tensor", None),
            P("tensor", None),
            P("tensor", None),
            P("tensor"),
        ),
        out_specs=P("tensor", ("groups", "context")),
        check_vma=False,
    )
```

```python
import functools

import jax
import jax.numpy as jnp
from jax import lax
from jax.experimental import pallas as pl
from jax.experimental.pallas import tpu as pltpu
from jax.sharding import PartitionSpec as P

F32 = jnp.float32
BF16 = jnp.bfloat16
EPS = 1e-05
SUB, LANE = 8, 128
TILE = SUB * LANE


def shifted(block, axis, distance):
    devices = range(lax.axis_size(axis))
    route = [(i - distance, i) for i in devices if i - distance in devices]
    return lax.ppermute(block, axis, route)


def medium_kernel(x_ref, gm_ref, km_ref, rim_ref, taps_ref, am_ref, ss_ref):
    rows, length = x_ref.shape
    groups = taps_ref.shape[0]
    per_group = rows // groups
    row = lax.broadcasted_iota(jnp.int32, (length, length), 0)
    col = lax.broadcasted_iota(jnp.int32, (length, length), 1)
    upper = col >= row

    @pl.when(pl.program_id(0) == 0)
    def _():
        ss_ref[...] = jnp.zeros_like(ss_ref)

    acc = jnp.zeros((1, length), F32)
    for g in range(groups):
        lo, hi = g * per_group, (g + 1) * per_group
        taps = jnp.broadcast_to(taps_ref[g : g + 1, :].astype(F32), (length, length))
        rolled = pltpu.roll(taps, 0, 1, stride=1, stride_axis=0)
        t_cur = jnp.where(upper, rolled, 0.0).astype(BF16)
        t_rim = jnp.where(upper, 0.0, rolled).astype(BF16)
        x = x_ref[lo:hi, :].astype(F32)
        vm = (km_ref[lo:hi, :].astype(F32) * x).astype(BF16)
        ext = jnp.concatenate([rim_ref[lo:hi, :], vm], axis=1)
        conv = jnp.dot(ext, jnp.concatenate([t_rim, t_cur], axis=0), preferred_element_type=F32)
        am = x + gm_ref[lo:hi, :].astype(F32) * conv
        am_ref[lo:hi, :] = am
        acc = acc + jnp.sum(am * am, axis=0, keepdims=True)
    ss_ref[...] += acc


def medium_call(inputs, gate_medium, key_medium, rim, taps):
    channels, length = inputs.shape
    per_group = channels // taps.shape[0]
    block = 256
    tap_block = block // per_group
    big = pl.BlockSpec((block, length), lambda b: (b, 0))
    return pl.pallas_call(
        medium_kernel,
        grid=(channels // block,),
        in_specs=[big, big, big, big, pl.BlockSpec((tap_block, length), lambda b: (b, 0))],
        out_specs=[big, pl.BlockSpec((1, length), lambda b: (0, 0))],
        out_shape=[
            jax.ShapeDtypeStruct((channels, length), F32),
            jax.ShapeDtypeStruct((1, length), F32),
        ],
        compiler_params=pltpu.CompilerParams(dimension_semantics=("arbitrary",)),
    )(inputs, gate_medium, key_medium, rim, taps)


def load_values(am_ref, kl_ref, g_ref, r_ref, vt_ref):
    r = r_ref[...]
    for i in range(SUB):
        rows = slice(i * LANE, (i + 1) * LANE)
        normed = am_ref[rows, :] * r * g_ref[rows, :]
        v = (kl_ref[rows, :].astype(F32) * normed).astype(BF16).astype(F32)
        vt_ref[pl.ds(i, LANE, stride=SUB), :] = v.T


def token_tile(ref, t):
    return ref[pl.ds(pl.multiple_of(t * SUB, SUB), SUB), :]


def final_state_kernel(am_ref, kl_ref, g_ref, r_ref, lam_ref, f_ref, vt_ref):
    modes = lam_ref.shape[0]
    length = am_ref.shape[1]
    load_values(am_ref, kl_ref, g_ref, r_ref, vt_ref)
    lam = [lam_ref[m] for m in range(modes)]

    def body(t, h):
        v = token_tile(vt_ref, t)
        return tuple(lam[m] * h[m] + v for m in range(modes))

    h = lax.fori_loop(0, length, body, tuple(jnp.zeros((SUB, LANE), F32) for _ in range(modes)), unroll=8)
    for m in range(modes):
        f_ref[m] = h[m]


def output_kernel(am_ref, kl_ref, gl_ref, g_ref, r_ref, lam_ref, w_ref, h0_ref, out_ref, vt_ref, yt_ref):
    modes = lam_ref.shape[0]
    length = am_ref.shape[1]
    load_values(am_ref, kl_ref, g_ref, r_ref, vt_ref)
    lam = [lam_ref[m] for m in range(modes)]
    w = [w_ref[m] for m in range(modes)]

    def body(t, h):
        v = token_tile(vt_ref, t)
        h = tuple(lam[m] * h[m] + v for m in range(modes))
        y = w[0] * h[0]
        for m in range(1, modes):
            y = y + w[m] * h[m]
        yt_ref[pl.ds(pl.multiple_of(t * SUB, SUB), SUB), :] = y
        return h

    lax.fori_loop(0, length, body, tuple(h0_ref[m] for m in range(modes)), unroll=8)
    for i in range(SUB):
        rows = slice(i * LANE, (i + 1) * LANE)
        long_out = yt_ref[pl.ds(i, LANE, stride=SUB), :].T.astype(BF16).astype(F32)
        out_ref[rows, :] = (am_ref[rows, :] + gl_ref[rows, :].astype(F32) * long_out).astype(BF16)


def tiled_spec(lead):
    return pl.BlockSpec((lead, None, SUB, LANE), lambda b: (0, b, 0, 0))


def final_state_call(am, kl, gain, r, lam):
    channels, length = am.shape
    modes = lam.shape[0]
    big = pl.BlockSpec((TILE, length), lambda b: (b, 0))
    return pl.pallas_call(
        final_state_kernel,
        grid=(channels // TILE,),
        in_specs=[big, big, pl.BlockSpec((TILE, 1), lambda b: (b, 0)), pl.BlockSpec((1, length), lambda b: (0, 0)), tiled_spec(modes)],
        out_specs=tiled_spec(modes),
        out_shape=jax.ShapeDtypeStruct(lam.shape, F32),
        scratch_shapes=[pltpu.VMEM((length * SUB, LANE), F32)],
    )(am, kl, gain, r, lam)


def output_call(am, kl, gl, gain, r, lam, w, h0):
    channels, length = am.shape
    modes = lam.shape[0]
    big = pl.BlockSpec((TILE, length), lambda b: (b, 0))
    return pl.pallas_call(
        output_kernel,
        grid=(channels // TILE,),
        in_specs=[big, big, big, pl.BlockSpec((TILE, 1), lambda b: (b, 0)), pl.BlockSpec((1, length), lambda b: (0, 0)), tiled_spec(modes), tiled_spec(modes), tiled_spec(modes)],
        out_specs=big,
        out_shape=jax.ShapeDtypeStruct((channels, length), BF16),
        scratch_shapes=[pltpu.VMEM((length * SUB, LANE), F32), pltpu.VMEM((length * SUB, LANE), F32)],
    )(am, kl, gl, gain, r, lam, w, h0)


def to_tiles(a):
    channels, k = a.shape
    return a.T.reshape(k, channels // TILE, SUB, LANE)


def on_device(
    inputs,
    gate_medium,
    key_medium,
    gate_long,
    key_long,
    medium_taps,
    log_decay,
    residues,
    norm_gain,
):
    channels, length = inputs.shape
    assert length == medium_taps.shape[1]
    width = channels * lax.axis_size("tensor")
    source = inputs.astype(F32)
    values_medium = (key_medium.astype(F32) * source).astype(BF16)
    rim = shifted(values_medium, "context", 1)
    after_medium, partial = medium_call(inputs, gate_medium, key_medium, rim, medium_taps)
    totals = lax.psum(partial, "tensor")
    r = lax.rsqrt(totals / width + EPS)
    gain = norm_gain[:, None]
    a_t = to_tiles(log_decay)
    lam = jnp.exp(-a_t)
    w = to_tiles(residues * jnp.sqrt(2.0 * log_decay))
    finals = final_state_call(after_medium, key_long, gain, r, lam)

    carried = shifted(finals.astype(BF16), "context", 1).astype(F32)
    distance = 1
    while distance < lax.axis_size("context"):
        decay = jnp.exp(-(length * distance) * a_t)
        carried = carried + decay * shifted(carried.astype(BF16), "context", distance).astype(F32)
        distance *= 2

    return output_call(after_medium, key_long, gate_long, gain, r, lam, w, carried)


def solution(mesh):
    return jax.shard_map(
        on_device,
        mesh=mesh,
        in_specs=(
            P("tensor", ("groups", "context")),
            P("tensor", ("groups", "context")),
            P("tensor", ("groups", "context")),
            P("tensor", ("groups", "context")),
            P("tensor", ("groups", "context")),
            P("tensor", None),
            P("tensor", None),
            P("tensor", None),
            P("tensor"),
        ),
        out_specs=P("tensor", ("groups", "context")),
        check_vma=False,
    )
```

```python
import functools

import jax
import jax.numpy as jnp
from jax import lax
from jax.experimental import pallas as pl
from jax.experimental.pallas import tpu as pltpu
from jax.sharding import PartitionSpec as P

F32 = jnp.float32
BF16 = jnp.bfloat16
EPS = 1e-05
SUB, LANE = 8, 128
TILE = SUB * LANE


def shifted(block, axis, distance):
    devices = range(lax.axis_size(axis))
    route = [(i - distance, i) for i in devices if i - distance in devices]
    return lax.ppermute(block, axis, route)


def medium_kernel(x_ref, gm_ref, km_ref, rim_ref, taps_ref, am_ref, ss_ref):
    rows, length = x_ref.shape
    groups = taps_ref.shape[0]
    per_group = rows // groups
    row = lax.broadcasted_iota(jnp.int32, (length, length), 0)
    col = lax.broadcasted_iota(jnp.int32, (length, length), 1)
    upper = col >= row

    @pl.when(pl.program_id(0) == 0)
    def _():
        ss_ref[...] = jnp.zeros_like(ss_ref)

    acc = jnp.zeros((1, length), F32)
    for g in range(groups):
        lo, hi = g * per_group, (g + 1) * per_group
        taps = jnp.broadcast_to(taps_ref[g : g + 1, :].astype(F32), (length, length))
        rolled = pltpu.roll(taps, 0, 1, stride=1, stride_axis=0)
        t_cur = jnp.where(upper, rolled, 0.0).astype(BF16)
        t_rim = jnp.where(upper, 0.0, rolled).astype(BF16)
        x = x_ref[lo:hi, :].astype(F32)
        vm = (km_ref[lo:hi, :].astype(F32) * x).astype(BF16)
        ext = jnp.concatenate([rim_ref[lo:hi, :], vm], axis=1)
        conv = jnp.dot(ext, jnp.concatenate([t_rim, t_cur], axis=0), preferred_element_type=F32)
        am = x + gm_ref[lo:hi, :].astype(F32) * conv
        am_ref[lo:hi, :] = am
        acc = acc + jnp.sum(am * am, axis=0, keepdims=True)
    ss_ref[...] += acc


def medium_call(inputs, gate_medium, key_medium, rim, taps):
    channels, length = inputs.shape
    per_group = channels // taps.shape[0]
    block = 256
    tap_block = block // per_group
    big = pl.BlockSpec((block, length), lambda b: (b, 0))
    return pl.pallas_call(
        medium_kernel,
        grid=(channels // block,),
        in_specs=[big, big, big, big, pl.BlockSpec((tap_block, length), lambda b: (b, 0))],
        out_specs=[big, pl.BlockSpec((1, length), lambda b: (0, 0))],
        out_shape=[
            jax.ShapeDtypeStruct((channels, length), F32),
            jax.ShapeDtypeStruct((1, length), F32),
        ],
        compiler_params=pltpu.CompilerParams(dimension_semantics=("arbitrary",)),
    )(inputs, gate_medium, key_medium, rim, taps)


def load_values(am_ref, kl_ref, g_ref, r_ref, vt_ref):
    r = r_ref[...]
    for i in range(SUB):
        rows = slice(i * LANE, (i + 1) * LANE)
        normed = am_ref[rows, :] * r * g_ref[rows, :]
        v = (kl_ref[rows, :].astype(F32) * normed).astype(BF16).astype(F32)
        vt_ref[pl.ds(i, LANE, stride=SUB), :] = v.T


def token_tile(ref, t):
    return ref[pl.ds(pl.multiple_of(t * SUB, SUB), SUB), :]


def final_state_kernel(am_ref, kl_ref, g_ref, r_ref, lam_ref, f_ref, vt_ref):
    modes = lam_ref.shape[0]
    length = am_ref.shape[1]
    load_values(am_ref, kl_ref, g_ref, r_ref, vt_ref)
    lam = [lam_ref[m] for m in range(modes)]

    def body(t, h):
        v = token_tile(vt_ref, t)
        return tuple(lam[m] * h[m] + v for m in range(modes))

    h = lax.fori_loop(0, length, body, tuple(jnp.zeros((SUB, LANE), F32) for _ in range(modes)), unroll=8)
    for m in range(modes):
        f_ref[m] = h[m]


def output_kernel(am_ref, kl_ref, gl_ref, g_ref, r_ref, lam_ref, w_ref, h0_ref, out_ref, vt_ref, yt_ref):
    modes = lam_ref.shape[0]
    length = am_ref.shape[1]
    load_values(am_ref, kl_ref, g_ref, r_ref, vt_ref)
    lam = [lam_ref[m] for m in range(modes)]
    w = [w_ref[m] for m in range(modes)]

    def body(t, h):
        v = token_tile(vt_ref, t)
        h = tuple(lam[m] * h[m] + v for m in range(modes))
        y = w[0] * h[0]
        for m in range(1, modes):
            y = y + w[m] * h[m]
        yt_ref[pl.ds(pl.multiple_of(t * SUB, SUB), SUB), :] = y
        return h

    lax.fori_loop(0, length, body, tuple(h0_ref[m] for m in range(modes)), unroll=8)
    for i in range(SUB):
        rows = slice(i * LANE, (i + 1) * LANE)
        long_out = yt_ref[pl.ds(i, LANE, stride=SUB), :].T.astype(BF16).astype(F32)
        out_ref[rows, :] = (am_ref[rows, :] + gl_ref[rows, :].astype(F32) * long_out).astype(BF16)


def tiled_spec(lead):
    return pl.BlockSpec((lead, None, SUB, LANE), lambda b: (0, b, 0, 0))


def final_state_call(am, kl, gain, r, lam):
    channels, length = am.shape
    modes = lam.shape[0]
    big = pl.BlockSpec((TILE, length), lambda b: (b, 0))
    return pl.pallas_call(
        final_state_kernel,
        grid=(channels // TILE,),
        in_specs=[big, big, pl.BlockSpec((TILE, 1), lambda b: (b, 0)), pl.BlockSpec((1, length), lambda b: (0, 0)), tiled_spec(modes)],
        out_specs=tiled_spec(modes),
        out_shape=jax.ShapeDtypeStruct(lam.shape, F32),
        scratch_shapes=[pltpu.VMEM((length * SUB, LANE), F32)],
    )(am, kl, gain, r, lam)


def output_call(am, kl, gl, gain, r, lam, w, h0):
    channels, length = am.shape
    modes = lam.shape[0]
    big = pl.BlockSpec((TILE, length), lambda b: (b, 0))
    return pl.pallas_call(
        output_kernel,
        grid=(channels // TILE,),
        in_specs=[big, big, big, pl.BlockSpec((TILE, 1), lambda b: (b, 0)), pl.BlockSpec((1, length), lambda b: (0, 0)), tiled_spec(modes), tiled_spec(modes), tiled_spec(modes)],
        out_specs=big,
        out_shape=jax.ShapeDtypeStruct((channels, length), BF16),
        scratch_shapes=[pltpu.VMEM((length * SUB, LANE), F32), pltpu.VMEM((length * SUB, LANE), F32)],
    )(am, kl, gl, gain, r, lam, w, h0)


def to_tiles(a):
    channels, k = a.shape
    return a.T.reshape(k, channels // TILE, SUB, LANE)


def on_device(
    inputs,
    gate_medium,
    key_medium,
    gate_long,
    key_long,
    medium_taps,
    log_decay,
    residues,
    norm_gain,
):
    channels, length = inputs.shape
    assert length == medium_taps.shape[1]
    width = channels * lax.axis_size("tensor")
    source = inputs.astype(F32)
    values_medium = (key_medium.astype(F32) * source).astype(BF16)
    rim = shifted(values_medium, "context", 1)
    after_medium, partial = medium_call(inputs, gate_medium, key_medium, rim, medium_taps)
    totals = lax.psum(partial, "tensor")
    r = lax.rsqrt(totals / width + EPS)
    gain = norm_gain[:, None]
    a_t = to_tiles(log_decay)
    lam = jnp.exp(-a_t)
    w = to_tiles(residues * jnp.sqrt(2.0 * log_decay))
    finals = final_state_call(after_medium, key_long, gain, r, lam)

    sent = finals.astype(BF16)
    carried = shifted(sent, "context", 1).astype(F32)
    distance = 1
    if lax.axis_size("context") > 2:
        decay = jnp.exp(-length * a_t)
        carried = carried + decay * shifted(sent, "context", 2).astype(F32)
        distance = 2
    while distance < lax.axis_size("context"):
        decay = jnp.exp(-(length * distance) * a_t)
        carried = carried + decay * shifted(carried.astype(BF16), "context", distance).astype(F32)
        distance *= 2

    return output_call(after_medium, key_long, gate_long, gain, r, lam, w, carried)


def solution(mesh):
    return jax.shard_map(
        on_device,
        mesh=mesh,
        in_specs=(
            P("tensor", ("groups", "context")),
            P("tensor", ("groups", "context")),
            P("tensor", ("groups", "context")),
            P("tensor", ("groups", "context")),
            P("tensor", ("groups", "context")),
            P("tensor", None),
            P("tensor", None),
            P("tensor", None),
            P("tensor"),
        ),
        out_specs=P("tensor", ("groups", "context")),
        check_vma=False,
    )
```

```python
import functools

import jax
import jax.numpy as jnp
from jax import lax
from jax.experimental import pallas as pl
from jax.experimental.pallas import tpu as pltpu
from jax.sharding import PartitionSpec as P

F32 = jnp.float32
BF16 = jnp.bfloat16
EPS = 1e-05
SUB, LANE = 8, 128
TILE = SUB * LANE


def shifted(block, axis, distance):
    devices = range(lax.axis_size(axis))
    route = [(i - distance, i) for i in devices if i - distance in devices]
    return lax.ppermute(block, axis, route)


def medium_kernel(x_ref, gm_ref, km_ref, rim_ref, taps_ref, am_ref, ss_ref):
    rows, length = x_ref.shape
    groups = taps_ref.shape[0]
    per_group = rows // groups
    row = lax.broadcasted_iota(jnp.int32, (length, length), 0)
    col = lax.broadcasted_iota(jnp.int32, (length, length), 1)
    upper = col >= row

    @pl.when(pl.program_id(0) == 0)
    def _():
        ss_ref[...] = jnp.zeros_like(ss_ref)

    acc = jnp.zeros((1, length), F32)
    for g in range(groups):
        lo, hi = g * per_group, (g + 1) * per_group
        taps = jnp.broadcast_to(taps_ref[g : g + 1, :].astype(F32), (length, length))
        rolled = pltpu.roll(taps, 0, 1, stride=1, stride_axis=0)
        t_cur = jnp.where(upper, rolled, 0.0).astype(BF16)
        t_rim = jnp.where(upper, 0.0, rolled).astype(BF16)
        x = x_ref[lo:hi, :].astype(F32)
        vm = (km_ref[lo:hi, :].astype(F32) * x).astype(BF16)
        ext = jnp.concatenate([rim_ref[lo:hi, :], vm], axis=1)
        conv = jnp.dot(ext, jnp.concatenate([t_rim, t_cur], axis=0), preferred_element_type=F32)
        am = x + gm_ref[lo:hi, :].astype(F32) * conv
        am_ref[lo:hi, :] = am
        acc = acc + jnp.sum(am * am, axis=0, keepdims=True)
    ss_ref[...] += acc


def medium_call(inputs, gate_medium, key_medium, rim, taps):
    channels, length = inputs.shape
    per_group = channels // taps.shape[0]
    block = 256
    tap_block = block // per_group
    big = pl.BlockSpec((block, length), lambda b: (b, 0))
    return pl.pallas_call(
        medium_kernel,
        grid=(channels // block,),
        in_specs=[big, big, big, big, pl.BlockSpec((tap_block, length), lambda b: (b, 0))],
        out_specs=[big, pl.BlockSpec((1, length), lambda b: (0, 0))],
        out_shape=[
            jax.ShapeDtypeStruct((channels, length), F32),
            jax.ShapeDtypeStruct((1, length), F32),
        ],
        compiler_params=pltpu.CompilerParams(dimension_semantics=("arbitrary",)),
    )(inputs, gate_medium, key_medium, rim, taps)


def load_values(am_ref, kl_ref, g_ref, r_ref, vt_ref):
    r = r_ref[...]
    for i in range(SUB):
        rows = slice(i * LANE, (i + 1) * LANE)
        normed = am_ref[rows, :] * r * g_ref[rows, :]
        v = (kl_ref[rows, :].astype(F32) * normed).astype(BF16).astype(F32)
        vt_ref[pl.ds(i, LANE, stride=SUB), :] = v.T


def token_tile(ref, t):
    return ref[pl.ds(pl.multiple_of(t * SUB, SUB), SUB), :]


def final_state_kernel(am_ref, kl_ref, g_ref, r_ref, lam_ref, f_ref, vt_ref):
    modes = lam_ref.shape[0]
    length = am_ref.shape[1]
    load_values(am_ref, kl_ref, g_ref, r_ref, vt_ref)
    lam = [lam_ref[m] for m in range(modes)]

    def body(t, h):
        v = token_tile(vt_ref, t)
        return tuple(lam[m] * h[m] + v for m in range(modes))

    h = lax.fori_loop(0, length, body, tuple(jnp.zeros((SUB, LANE), F32) for _ in range(modes)), unroll=8)
    for m in range(modes):
        f_ref[m] = h[m]


def output_kernel(am_ref, kl_ref, gl_ref, g_ref, r_ref, lam_ref, w_ref, h0_ref, out_ref, vt_ref, yt_ref):
    modes = lam_ref.shape[0]
    length = am_ref.shape[1]
    load_values(am_ref, kl_ref, g_ref, r_ref, vt_ref)
    lam = [lam_ref[m] for m in range(modes)]
    w = [w_ref[m] for m in range(modes)]

    def body(t, h):
        v = token_tile(vt_ref, t)
        h = tuple(lam[m] * h[m] + v for m in range(modes))
        y = w[0] * h[0]
        for m in range(1, modes):
            y = y + w[m] * h[m]
        yt_ref[pl.ds(pl.multiple_of(t * SUB, SUB), SUB), :] = y
        return h

    lax.fori_loop(0, length, body, tuple(h0_ref[m] for m in range(modes)), unroll=8)
    for i in range(SUB):
        rows = slice(i * LANE, (i + 1) * LANE)
        long_out = yt_ref[pl.ds(i, LANE, stride=SUB), :].T.astype(BF16).astype(F32)
        out_ref[rows, :] = (am_ref[rows, :] + gl_ref[rows, :].astype(F32) * long_out).astype(BF16)


def tiled_spec(lead):
    return pl.BlockSpec((lead, None, SUB, LANE), lambda b: (0, b, 0, 0))


def final_state_call(am, kl, gain, r, lam):
    channels, length = am.shape
    modes = lam.shape[0]
    big = pl.BlockSpec((TILE, length), lambda b: (b, 0))
    return pl.pallas_call(
        final_state_kernel,
        grid=(channels // TILE,),
        in_specs=[big, big, pl.BlockSpec((TILE, 1), lambda b: (b, 0)), pl.BlockSpec((1, length), lambda b: (0, 0)), tiled_spec(modes)],
        out_specs=tiled_spec(modes),
        out_shape=jax.ShapeDtypeStruct(lam.shape, F32),
        scratch_shapes=[pltpu.VMEM((length * SUB, LANE), F32)],
    )(am, kl, gain, r, lam)


def output_call(am, kl, gl, gain, r, lam, w, h0):
    channels, length = am.shape
    modes = lam.shape[0]
    big = pl.BlockSpec((TILE, length), lambda b: (b, 0))
    return pl.pallas_call(
        output_kernel,
        grid=(channels // TILE,),
        in_specs=[big, big, big, pl.BlockSpec((TILE, 1), lambda b: (b, 0)), pl.BlockSpec((1, length), lambda b: (0, 0)), tiled_spec(modes), tiled_spec(modes), tiled_spec(modes)],
        out_specs=big,
        out_shape=jax.ShapeDtypeStruct((channels, length), BF16),
        scratch_shapes=[pltpu.VMEM((length * SUB, LANE), F32), pltpu.VMEM((length * SUB, LANE), F32)],
    )(am, kl, gl, gain, r, lam, w, h0)


def to_tiles(a):
    channels, k = a.shape
    return a.T.reshape(k, channels // TILE, SUB, LANE)


def decayed_scan(finals, a_t, length, count, radix=3):
    sent = finals.astype(BF16)
    carried = shifted(sent, "context", 1).astype(F32)
    for j in range(2, min(radix, count) + 1):
        decay = jnp.exp(-(length * (j - 1)) * a_t)
        carried = carried + decay * shifted(sent, "context", j).astype(F32)
    window = radix
    while window < count:
        sent = carried.astype(BF16)
        for j in range(1, radix):
            if j * window < count:
                decay = jnp.exp(-(length * j * window) * a_t)
                carried = carried + decay * shifted(sent, "context", j * window).astype(F32)
        window *= radix
    return carried


def on_device(
    inputs,
    gate_medium,
    key_medium,
    gate_long,
    key_long,
    medium_taps,
    log_decay,
    residues,
    norm_gain,
):
    channels, length = inputs.shape
    assert length == medium_taps.shape[1]
    width = channels * lax.axis_size("tensor")
    source = inputs.astype(F32)
    values_medium = (key_medium.astype(F32) * source).astype(BF16)
    rim = shifted(values_medium, "context", 1)
    after_medium, partial = medium_call(inputs, gate_medium, key_medium, rim, medium_taps)
    totals = lax.psum(partial, "tensor")
    r = lax.rsqrt(totals / width + EPS)
    gain = norm_gain[:, None]
    a_t = to_tiles(log_decay)
    lam = jnp.exp(-a_t)
    w = to_tiles(residues * jnp.sqrt(2.0 * log_decay))
    finals = final_state_call(after_medium, key_long, gain, r, lam)

    carried = decayed_scan(finals, a_t, length, lax.axis_size("context"))

    return output_call(after_medium, key_long, gate_long, gain, r, lam, w, carried)


def solution(mesh):
    return jax.shard_map(
        on_device,
        mesh=mesh,
        in_specs=(
            P("tensor", ("groups", "context")),
            P("tensor", ("groups", "context")),
            P("tensor", ("groups", "context")),
            P("tensor", ("groups", "context")),
            P("tensor", ("groups", "context")),
            P("tensor", None),
            P("tensor", None),
            P("tensor", None),
            P("tensor"),
        ),
        out_specs=P("tensor", ("groups", "context")),
        check_vma=False,
    )
```

```python
import functools

import jax
import jax.numpy as jnp
from jax import lax
from jax.experimental import pallas as pl
from jax.experimental.pallas import tpu as pltpu
from jax.sharding import PartitionSpec as P

F32 = jnp.float32
BF16 = jnp.bfloat16
EPS = 1e-05
SUB, LANE = 8, 128
TILE = SUB * LANE


def shifted(block, axis, distance):
    devices = range(lax.axis_size(axis))
    route = [(i - distance, i) for i in devices if i - distance in devices]
    return lax.ppermute(block, axis, route)


def medium_kernel(x_ref, gm_ref, km_ref, rim_ref, taps_ref, am_ref, ss_ref):
    rows, length = x_ref.shape
    groups = taps_ref.shape[0]
    per_group = rows // groups
    row = lax.broadcasted_iota(jnp.int32, (length, length), 0)
    col = lax.broadcasted_iota(jnp.int32, (length, length), 1)
    upper = col >= row

    @pl.when(pl.program_id(0) == 0)
    def _():
        ss_ref[...] = jnp.zeros_like(ss_ref)

    acc = jnp.zeros((1, length), F32)
    for g in range(groups):
        lo, hi = g * per_group, (g + 1) * per_group
        taps = jnp.broadcast_to(taps_ref[g : g + 1, :].astype(F32), (length, length))
        rolled = pltpu.roll(taps, 0, 1, stride=1, stride_axis=0)
        t_cur = jnp.where(upper, rolled, 0.0).astype(BF16)
        t_rim = jnp.where(upper, 0.0, rolled).astype(BF16)
        x = x_ref[lo:hi, :].astype(F32)
        vm = (km_ref[lo:hi, :].astype(F32) * x).astype(BF16)
        ext = jnp.concatenate([rim_ref[lo:hi, :], vm], axis=1)
        conv = jnp.dot(ext, jnp.concatenate([t_rim, t_cur], axis=0), preferred_element_type=F32)
        am = x + gm_ref[lo:hi, :].astype(F32) * conv
        am_ref[lo:hi, :] = am
        acc = acc + jnp.sum(am * am, axis=0, keepdims=True)
    ss_ref[...] += acc


def medium_call(inputs, gate_medium, key_medium, rim, taps):
    channels, length = inputs.shape
    per_group = channels // taps.shape[0]
    block = 256
    tap_block = block // per_group
    big = pl.BlockSpec((block, length), lambda b: (b, 0))
    return pl.pallas_call(
        medium_kernel,
        grid=(channels // block,),
        in_specs=[big, big, big, big, pl.BlockSpec((tap_block, length), lambda b: (b, 0))],
        out_specs=[big, pl.BlockSpec((1, length), lambda b: (0, 0))],
        out_shape=[
            jax.ShapeDtypeStruct((channels, length), F32),
            jax.ShapeDtypeStruct((1, length), F32),
        ],
        compiler_params=pltpu.CompilerParams(dimension_semantics=("arbitrary",)),
    )(inputs, gate_medium, key_medium, rim, taps)


def load_values(am_ref, kl_ref, g_ref, r_ref, vt_ref):
    r = r_ref[...]
    for i in range(SUB):
        rows = slice(i * LANE, (i + 1) * LANE)
        normed = am_ref[rows, :] * r * g_ref[rows, :]
        v = (kl_ref[rows, :].astype(F32) * normed).astype(BF16).astype(F32)
        vt_ref[pl.ds(i, LANE, stride=SUB), :] = v.T


def token_tile(ref, t):
    return ref[pl.ds(pl.multiple_of(t * SUB, SUB), SUB), :]


def final_state_kernel(am_ref, kl_ref, g_ref, r_ref, lam_ref, f_ref, vt_ref):
    modes = lam_ref.shape[0]
    length = am_ref.shape[1]
    load_values(am_ref, kl_ref, g_ref, r_ref, vt_ref)
    lam = [lam_ref[m] for m in range(modes)]

    def body(t, h):
        v = token_tile(vt_ref, t)
        return tuple(lam[m] * h[m] + v for m in range(modes))

    h = lax.fori_loop(0, length, body, tuple(jnp.zeros((SUB, LANE), F32) for _ in range(modes)), unroll=8)
    for m in range(modes):
        f_ref[m] = h[m].astype(f_ref.dtype)


def output_kernel(am_ref, vt_ref, gl_ref, lam_ref, w_ref, h0_ref, out_ref, yt_ref):
    modes = lam_ref.shape[0]
    length = am_ref.shape[1]
    lam = [lam_ref[m] for m in range(modes)]
    w = [w_ref[m] for m in range(modes)]

    def body(t, h):
        v = token_tile(vt_ref, t)
        h = tuple(lam[m] * h[m] + v for m in range(modes))
        y = w[0] * h[0]
        for m in range(1, modes):
            y = y + w[m] * h[m]
        yt_ref[pl.ds(pl.multiple_of(t * SUB, SUB), SUB), :] = y
        return h

    lax.fori_loop(0, length, body, tuple(h0_ref[m] for m in range(modes)), unroll=8)
    for i in range(SUB):
        rows = slice(i * LANE, (i + 1) * LANE)
        long_out = yt_ref[pl.ds(i, LANE, stride=SUB), :].T.astype(BF16).astype(F32)
        out_ref[rows, :] = (am_ref[rows, :] + gl_ref[rows, :].astype(F32) * long_out).astype(BF16)


def tiled_spec(lead):
    return pl.BlockSpec((lead, None, SUB, LANE), lambda b: (0, b, 0, 0))


def final_state_call(am, kl, gain, r, lam):
    channels, length = am.shape
    modes = lam.shape[0]
    big = pl.BlockSpec((TILE, length), lambda b: (b, 0))
    return pl.pallas_call(
        final_state_kernel,
        grid=(channels // TILE,),
        in_specs=[big, big, pl.BlockSpec((TILE, 1), lambda b: (b, 0)), pl.BlockSpec((1, length), lambda b: (0, 0)), tiled_spec(modes)],
        out_specs=[tiled_spec(modes), pl.BlockSpec((length * SUB, LANE), lambda b: (b, 0))],
        out_shape=[
            jax.ShapeDtypeStruct(lam.shape, BF16),
            jax.ShapeDtypeStruct((channels // TILE * length * SUB, LANE), F32),
        ],
    )(am, kl, gain, r, lam)


def output_call(am, vt, gl, lam, w, h0):
    channels, length = am.shape
    modes = lam.shape[0]
    big = pl.BlockSpec((TILE, length), lambda b: (b, 0))
    return pl.pallas_call(
        output_kernel,
        grid=(channels // TILE,),
        in_specs=[big, pl.BlockSpec((length * SUB, LANE), lambda b: (b, 0)), big, tiled_spec(modes), tiled_spec(modes), tiled_spec(modes)],
        out_specs=big,
        out_shape=jax.ShapeDtypeStruct((channels, length), BF16),
        scratch_shapes=[pltpu.VMEM((length * SUB, LANE), F32)],
    )(am, vt, gl, lam, w, h0)


def to_tiles(a):
    channels, k = a.shape
    return a.T.reshape(k, channels // TILE, SUB, LANE)


def on_device(
    inputs,
    gate_medium,
    key_medium,
    gate_long,
    key_long,
    medium_taps,
    log_decay,
    residues,
    norm_gain,
):
    channels, length = inputs.shape
    assert length == medium_taps.shape[1]
    width = channels * lax.axis_size("tensor")
    source = inputs.astype(F32)
    values_medium = (key_medium.astype(F32) * source).astype(BF16)
    rim = shifted(values_medium, "context", 1)
    after_medium, partial = medium_call(inputs, gate_medium, key_medium, rim, medium_taps)
    totals = lax.psum(partial, "tensor")
    r = lax.rsqrt(totals / width + EPS)
    gain = norm_gain[:, None]
    a_t = to_tiles(log_decay)
    lam = jnp.exp(-a_t)
    w = to_tiles(residues * jnp.sqrt(2.0 * log_decay))
    finals, vt = final_state_call(after_medium, key_long, gain, r, lam)

    sent = finals
    carried = shifted(sent, "context", 1).astype(F32)
    distance = 1
    if lax.axis_size("context") > 2:
        decay = jnp.exp(-length * a_t)
        carried = carried + decay * shifted(sent, "context", 2).astype(F32)
        distance = 2
    while distance < lax.axis_size("context"):
        decay = jnp.exp(-(length * distance) * a_t)
        carried = carried + decay * shifted(carried.astype(BF16), "context", distance).astype(F32)
        distance *= 2

    return output_call(after_medium, vt, gate_long, lam, w, carried)


def solution(mesh):
    return jax.shard_map(
        on_device,
        mesh=mesh,
        in_specs=(
            P("tensor", ("groups", "context")),
            P("tensor", ("groups", "context")),
            P("tensor", ("groups", "context")),
            P("tensor", ("groups", "context")),
            P("tensor", ("groups", "context")),
            P("tensor", None),
            P("tensor", None),
            P("tensor", None),
            P("tensor"),
        ),
        out_specs=P("tensor", ("groups", "context")),
        check_vma=False,
    )
```

```python
import functools

import jax
import jax.numpy as jnp
from jax import lax
from jax.experimental import pallas as pl
from jax.experimental.pallas import tpu as pltpu
from jax.sharding import PartitionSpec as P

F32 = jnp.float32
BF16 = jnp.bfloat16
EPS = 1e-05
SUB, LANE = 8, 128
TILE = SUB * LANE


def shifted(block, axis, distance):
    devices = range(lax.axis_size(axis))
    route = [(i - distance, i) for i in devices if i - distance in devices]
    return lax.ppermute(block, axis, route)


def medium_kernel(x_ref, gm_ref, km_ref, rim_ref, taps_ref, am_ref, ss_ref):
    rows, length = x_ref.shape
    groups = taps_ref.shape[0]
    per_group = rows // groups
    row = lax.broadcasted_iota(jnp.int32, (length, length), 0)
    col = lax.broadcasted_iota(jnp.int32, (length, length), 1)
    upper = col >= row

    @pl.when(pl.program_id(0) == 0)
    def _():
        ss_ref[...] = jnp.zeros_like(ss_ref)

    acc = jnp.zeros((1, length), F32)
    for g in range(groups):
        lo, hi = g * per_group, (g + 1) * per_group
        taps = jnp.broadcast_to(taps_ref[g : g + 1, :].astype(F32), (length, length))
        rolled = pltpu.roll(taps, 0, 1, stride=1, stride_axis=0)
        t_cur = jnp.where(upper, rolled, 0.0).astype(BF16)
        t_rim = jnp.where(upper, 0.0, rolled).astype(BF16)
        x = x_ref[lo:hi, :].astype(F32)
        vm = (km_ref[lo:hi, :].astype(F32) * x).astype(BF16)
        ext = jnp.concatenate([rim_ref[lo:hi, :], vm], axis=1)
        conv = jnp.dot(ext, jnp.concatenate([t_rim, t_cur], axis=0), preferred_element_type=F32)
        am = x + gm_ref[lo:hi, :].astype(F32) * conv
        am_ref[lo:hi, :] = am
        acc = acc + jnp.sum(am * am, axis=0, keepdims=True)
    ss_ref[...] += acc


def medium_call(inputs, gate_medium, key_medium, rim, taps):
    channels, length = inputs.shape
    per_group = channels // taps.shape[0]
    block = 512
    tap_block = block // per_group
    big = pl.BlockSpec((block, length), lambda b: (b, 0))
    return pl.pallas_call(
        medium_kernel,
        grid=(channels // block,),
        in_specs=[big, big, big, big, pl.BlockSpec((tap_block, length), lambda b: (b, 0))],
        out_specs=[big, pl.BlockSpec((1, length), lambda b: (0, 0))],
        out_shape=[
            jax.ShapeDtypeStruct((channels, length), F32),
            jax.ShapeDtypeStruct((1, length), F32),
        ],
        compiler_params=pltpu.CompilerParams(dimension_semantics=("arbitrary",)),
    )(inputs, gate_medium, key_medium, rim, taps)


def load_values(am_ref, kl_ref, g_ref, r_ref, vt_ref):
    r = r_ref[...]
    for i in range(SUB):
        rows = slice(i * LANE, (i + 1) * LANE)
        normed = am_ref[rows, :] * r * g_ref[rows, :]
        v = (kl_ref[rows, :].astype(F32) * normed).astype(BF16).astype(F32)
        vt_ref[pl.ds(i, LANE, stride=SUB), :] = v.T


def token_tile(ref, t):
    return ref[pl.ds(pl.multiple_of(t * SUB, SUB), SUB), :]


def final_state_kernel(am_ref, kl_ref, g_ref, r_ref, lam_ref, f_ref, vt_ref):
    modes = lam_ref.shape[0]
    length = am_ref.shape[1]
    load_values(am_ref, kl_ref, g_ref, r_ref, vt_ref)
    lam = [lam_ref[m] for m in range(modes)]

    def body(t, h):
        v = token_tile(vt_ref, t)
        return tuple(lam[m] * h[m] + v for m in range(modes))

    h = lax.fori_loop(0, length, body, tuple(jnp.zeros((SUB, LANE), F32) for _ in range(modes)), unroll=8)
    for m in range(modes):
        f_ref[m] = h[m].astype(f_ref.dtype)


def output_kernel(am_ref, vt_ref, gl_ref, lam_ref, w_ref, h0_ref, out_ref, yt_ref):
    modes = lam_ref.shape[0]
    length = am_ref.shape[1]
    lam = [lam_ref[m] for m in range(modes)]
    w = [w_ref[m] for m in range(modes)]

    def body(t, h):
        v = token_tile(vt_ref, t)
        h = tuple(lam[m] * h[m] + v for m in range(modes))
        y = w[0] * h[0]
        for m in range(1, modes):
            y = y + w[m] * h[m]
        yt_ref[pl.ds(pl.multiple_of(t * SUB, SUB), SUB), :] = y
        return h

    lax.fori_loop(0, length, body, tuple(h0_ref[m] for m in range(modes)), unroll=8)
    for i in range(SUB):
        rows = slice(i * LANE, (i + 1) * LANE)
        long_out = yt_ref[pl.ds(i, LANE, stride=SUB), :].T.astype(BF16).astype(F32)
        out_ref[rows, :] = (am_ref[rows, :] + gl_ref[rows, :].astype(F32) * long_out).astype(BF16)


def tiled_spec(lead):
    return pl.BlockSpec((lead, None, SUB, LANE), lambda b: (0, b, 0, 0))


def final_state_call(am, kl, gain, r, lam):
    channels, length = am.shape
    modes = lam.shape[0]
    big = pl.BlockSpec((TILE, length), lambda b: (b, 0))
    return pl.pallas_call(
        final_state_kernel,
        grid=(channels // TILE,),
        in_specs=[big, big, pl.BlockSpec((TILE, 1), lambda b: (b, 0)), pl.BlockSpec((1, length), lambda b: (0, 0)), tiled_spec(modes)],
        out_specs=[tiled_spec(modes), pl.BlockSpec((length * SUB, LANE), lambda b: (b, 0))],
        out_shape=[
            jax.ShapeDtypeStruct(lam.shape, BF16),
            jax.ShapeDtypeStruct((channels // TILE * length * SUB, LANE), F32),
        ],
    )(am, kl, gain, r, lam)


def output_call(am, vt, gl, lam, w, h0):
    channels, length = am.shape
    modes = lam.shape[0]
    big = pl.BlockSpec((TILE, length), lambda b: (b, 0))
    return pl.pallas_call(
        output_kernel,
        grid=(channels // TILE,),
        in_specs=[big, pl.BlockSpec((length * SUB, LANE), lambda b: (b, 0)), big, tiled_spec(modes), tiled_spec(modes), tiled_spec(modes)],
        out_specs=big,
        out_shape=jax.ShapeDtypeStruct((channels, length), BF16),
        scratch_shapes=[pltpu.VMEM((length * SUB, LANE), F32)],
    )(am, vt, gl, lam, w, h0)


def to_tiles(a):
    channels, k = a.shape
    return a.T.reshape(k, channels // TILE, SUB, LANE)


def on_device(
    inputs,
    gate_medium,
    key_medium,
    gate_long,
    key_long,
    medium_taps,
    log_decay,
    residues,
    norm_gain,
):
    channels, length = inputs.shape
    assert length == medium_taps.shape[1]
    width = channels * lax.axis_size("tensor")
    source = inputs.astype(F32)
    values_medium = (key_medium.astype(F32) * source).astype(BF16)
    rim = shifted(values_medium, "context", 1)
    after_medium, partial = medium_call(inputs, gate_medium, key_medium, rim, medium_taps)
    totals = lax.psum(partial, "tensor")
    r = lax.rsqrt(totals / width + EPS)
    gain = norm_gain[:, None]
    a_t = to_tiles(log_decay)
    lam = jnp.exp(-a_t)
    w = to_tiles(residues * jnp.sqrt(2.0 * log_decay))
    finals, vt = final_state_call(after_medium, key_long, gain, r, lam)

    sent = finals
    carried = shifted(sent, "context", 1).astype(F32)
    distance = 1
    if lax.axis_size("context") > 2:
        decay = jnp.exp(-length * a_t)
        carried = carried + decay * shifted(sent, "context", 2).astype(F32)
        distance = 2
    while distance < lax.axis_size("context"):
        decay = jnp.exp(-(length * distance) * a_t)
        carried = carried + decay * shifted(carried.astype(BF16), "context", distance).astype(F32)
        distance *= 2

    return output_call(after_medium, vt, gate_long, lam, w, carried)


def solution(mesh):
    return jax.shard_map(
        on_device,
        mesh=mesh,
        in_specs=(
            P("tensor", ("groups", "context")),
            P("tensor", ("groups", "context")),
            P("tensor", ("groups", "context")),
            P("tensor", ("groups", "context")),
            P("tensor", ("groups", "context")),
            P("tensor", None),
            P("tensor", None),
            P("tensor", None),
            P("tensor"),
        ),
        out_specs=P("tensor", ("groups", "context")),
        check_vma=False,
    )
```

```python
import functools

import jax
import jax.numpy as jnp
from jax import lax
from jax.experimental import pallas as pl
from jax.experimental.pallas import tpu as pltpu
from jax.sharding import PartitionSpec as P

F32 = jnp.float32
BF16 = jnp.bfloat16
EPS = 1e-05
SUB, LANE = 8, 128
TILE = SUB * LANE


def shifted(block, axis, distance):
    devices = range(lax.axis_size(axis))
    route = [(i - distance, i) for i in devices if i - distance in devices]
    return lax.ppermute(block, axis, route)


def medium_kernel(x_ref, gm_ref, km_ref, rim_ref, taps_ref, am_ref, ss_ref):
    rows, length = x_ref.shape
    groups = taps_ref.shape[0]
    per_group = rows // groups
    row = lax.broadcasted_iota(jnp.int32, (length, length), 0)
    col = lax.broadcasted_iota(jnp.int32, (length, length), 1)
    upper = col >= row

    @pl.when(pl.program_id(0) == 0)
    def _():
        ss_ref[...] = jnp.zeros_like(ss_ref)

    acc = jnp.zeros((1, length), F32)
    for g in range(groups):
        lo, hi = g * per_group, (g + 1) * per_group
        taps = jnp.broadcast_to(taps_ref[g : g + 1, :].astype(F32), (length, length))
        rolled = pltpu.roll(taps, 0, 1, stride=1, stride_axis=0)
        t_cur = jnp.where(upper, rolled, 0.0).astype(BF16)
        t_rim = jnp.where(upper, 0.0, rolled).astype(BF16)
        x = x_ref[lo:hi, :].astype(F32)
        vm = (km_ref[lo:hi, :].astype(F32) * x).astype(BF16)
        ext = jnp.concatenate([rim_ref[lo:hi, :], vm], axis=1)
        conv = jnp.dot(ext, jnp.concatenate([t_rim, t_cur], axis=0), preferred_element_type=F32)
        am = x + gm_ref[lo:hi, :].astype(F32) * conv
        am_ref[lo:hi, :] = am
        acc = acc + jnp.sum(am * am, axis=0, keepdims=True)
    ss_ref[...] += acc


def medium_call(inputs, gate_medium, key_medium, rim, taps):
    channels, length = inputs.shape
    per_group = channels // taps.shape[0]
    block = 1024
    tap_block = block // per_group
    big = pl.BlockSpec((block, length), lambda b: (b, 0))
    return pl.pallas_call(
        medium_kernel,
        grid=(channels // block,),
        in_specs=[big, big, big, big, pl.BlockSpec((tap_block, length), lambda b: (b, 0))],
        out_specs=[big, pl.BlockSpec((1, length), lambda b: (0, 0))],
        out_shape=[
            jax.ShapeDtypeStruct((channels, length), F32),
            jax.ShapeDtypeStruct((1, length), F32),
        ],
        compiler_params=pltpu.CompilerParams(dimension_semantics=("arbitrary",)),
    )(inputs, gate_medium, key_medium, rim, taps)


def load_values(am_ref, kl_ref, g_ref, r_ref, vt_ref):
    r = r_ref[...]
    for i in range(SUB):
        rows = slice(i * LANE, (i + 1) * LANE)
        normed = am_ref[rows, :] * r * g_ref[rows, :]
        v = (kl_ref[rows, :].astype(F32) * normed).astype(BF16).astype(F32)
        vt_ref[pl.ds(i, LANE, stride=SUB), :] = v.T


def token_tile(ref, t):
    return ref[pl.ds(pl.multiple_of(t * SUB, SUB), SUB), :]


def final_state_kernel(am_ref, kl_ref, g_ref, r_ref, lam_ref, f_ref, vt_ref):
    modes = lam_ref.shape[0]
    length = am_ref.shape[1]
    load_values(am_ref, kl_ref, g_ref, r_ref, vt_ref)
    lam = [lam_ref[m] for m in range(modes)]

    def body(t, h):
        v = token_tile(vt_ref, t)
        return tuple(lam[m] * h[m] + v for m in range(modes))

    h = lax.fori_loop(0, length, body, tuple(jnp.zeros((SUB, LANE), F32) for _ in range(modes)), unroll=8)
    for m in range(modes):
        f_ref[m] = h[m].astype(f_ref.dtype)


def output_kernel(am_ref, vt_ref, gl_ref, lam_ref, w_ref, h0_ref, out_ref, yt_ref):
    modes = lam_ref.shape[0]
    length = am_ref.shape[1]
    lam = [lam_ref[m] for m in range(modes)]
    w = [w_ref[m] for m in range(modes)]

    def body(t, h):
        v = token_tile(vt_ref, t)
        h = tuple(lam[m] * h[m] + v for m in range(modes))
        y = w[0] * h[0]
        for m in range(1, modes):
            y = y + w[m] * h[m]
        yt_ref[pl.ds(pl.multiple_of(t * SUB, SUB), SUB), :] = y
        return h

    lax.fori_loop(0, length, body, tuple(h0_ref[m] for m in range(modes)), unroll=8)
    for i in range(SUB):
        rows = slice(i * LANE, (i + 1) * LANE)
        long_out = yt_ref[pl.ds(i, LANE, stride=SUB), :].T.astype(BF16).astype(F32)
        out_ref[rows, :] = (am_ref[rows, :] + gl_ref[rows, :].astype(F32) * long_out).astype(BF16)


def tiled_spec(lead):
    return pl.BlockSpec((lead, None, SUB, LANE), lambda b: (0, b, 0, 0))


def final_state_call(am, kl, gain, r, lam):
    channels, length = am.shape
    modes = lam.shape[0]
    big = pl.BlockSpec((TILE, length), lambda b: (b, 0))
    return pl.pallas_call(
        final_state_kernel,
        grid=(channels // TILE,),
        in_specs=[big, big, pl.BlockSpec((TILE, 1), lambda b: (b, 0)), pl.BlockSpec((1, length), lambda b: (0, 0)), tiled_spec(modes)],
        out_specs=[tiled_spec(modes), pl.BlockSpec((length * SUB, LANE), lambda b: (b, 0))],
        out_shape=[
            jax.ShapeDtypeStruct(lam.shape, BF16),
            jax.ShapeDtypeStruct((channels // TILE * length * SUB, LANE), F32),
        ],
    )(am, kl, gain, r, lam)


def output_call(am, vt, gl, lam, w, h0):
    channels, length = am.shape
    modes = lam.shape[0]
    big = pl.BlockSpec((TILE, length), lambda b: (b, 0))
    return pl.pallas_call(
        output_kernel,
        grid=(channels // TILE,),
        in_specs=[big, pl.BlockSpec((length * SUB, LANE), lambda b: (b, 0)), big, tiled_spec(modes), tiled_spec(modes), tiled_spec(modes)],
        out_specs=big,
        out_shape=jax.ShapeDtypeStruct((channels, length), BF16),
        scratch_shapes=[pltpu.VMEM((length * SUB, LANE), F32)],
    )(am, vt, gl, lam, w, h0)


def to_tiles(a):
    channels, k = a.shape
    return a.T.reshape(k, channels // TILE, SUB, LANE)


def on_device(
    inputs,
    gate_medium,
    key_medium,
    gate_long,
    key_long,
    medium_taps,
    log_decay,
    residues,
    norm_gain,
):
    channels, length = inputs.shape
    assert length == medium_taps.shape[1]
    width = channels * lax.axis_size("tensor")
    source = inputs.astype(F32)
    values_medium = (key_medium.astype(F32) * source).astype(BF16)
    rim = shifted(values_medium, "context", 1)
    after_medium, partial = medium_call(inputs, gate_medium, key_medium, rim, medium_taps)
    totals = lax.psum(partial, "tensor")
    r = lax.rsqrt(totals / width + EPS)
    gain = norm_gain[:, None]
    a_t = to_tiles(log_decay)
    lam = jnp.exp(-a_t)
    w = to_tiles(residues * jnp.sqrt(2.0 * log_decay))
    finals, vt = final_state_call(after_medium, key_long, gain, r, lam)

    sent = finals
    carried = shifted(sent, "context", 1).astype(F32)
    distance = 1
    if lax.axis_size("context") > 2:
        decay = jnp.exp(-length * a_t)
        carried = carried + decay * shifted(sent, "context", 2).astype(F32)
        distance = 2
    while distance < lax.axis_size("context"):
        decay = jnp.exp(-(length * distance) * a_t)
        carried = carried + decay * shifted(carried.astype(BF16), "context", distance).astype(F32)
        distance *= 2

    return output_call(after_medium, vt, gate_long, lam, w, carried)


def solution(mesh):
    return jax.shard_map(
        on_device,
        mesh=mesh,
        in_specs=(
            P("tensor", ("groups", "context")),
            P("tensor", ("groups", "context")),
            P("tensor", ("groups", "context")),
            P("tensor", ("groups", "context")),
            P("tensor", ("groups", "context")),
            P("tensor", None),
            P("tensor", None),
            P("tensor", None),
            P("tensor"),
        ),
        out_specs=P("tensor", ("groups", "context")),
        check_vma=False,
    )
```

```python
import functools

import jax
import jax.numpy as jnp
from jax import lax
from jax.experimental import pallas as pl
from jax.experimental.pallas import tpu as pltpu
from jax.sharding import PartitionSpec as P

F32 = jnp.float32
BF16 = jnp.bfloat16
EPS = 1e-05
SUB, LANE = 8, 128
TILE = SUB * LANE


def shifted(block, axis, distance):
    devices = range(lax.axis_size(axis))
    route = [(i - distance, i) for i in devices if i - distance in devices]
    return lax.ppermute(block, axis, route)


def medium_kernel(x_ref, gm_ref, km_ref, rim_ref, taps_ref, am_ref, ss_ref):
    rows, length = x_ref.shape
    groups = taps_ref.shape[0]
    per_group = rows // groups
    row = lax.broadcasted_iota(jnp.int32, (length, length), 0)
    col = lax.broadcasted_iota(jnp.int32, (length, length), 1)
    upper = col >= row

    @pl.when(pl.program_id(0) == 0)
    def _():
        ss_ref[...] = jnp.zeros_like(ss_ref)

    acc = jnp.zeros((1, length), F32)
    for g in range(groups):
        lo, hi = g * per_group, (g + 1) * per_group
        taps = jnp.broadcast_to(taps_ref[g : g + 1, :].astype(F32), (length, length))
        rolled = pltpu.roll(taps, 0, 1, stride=1, stride_axis=0)
        t_cur = jnp.where(upper, rolled, 0.0).astype(BF16)
        t_rim = jnp.where(upper, 0.0, rolled).astype(BF16)
        x = x_ref[lo:hi, :].astype(F32)
        vm = (km_ref[lo:hi, :].astype(F32) * x).astype(BF16)
        ext = jnp.concatenate([rim_ref[lo:hi, :], vm], axis=1)
        conv = jnp.dot(ext, jnp.concatenate([t_rim, t_cur], axis=0), preferred_element_type=F32)
        am = x + gm_ref[lo:hi, :].astype(F32) * conv
        am_ref[lo:hi, :] = am
        acc = acc + jnp.sum(am * am, axis=0, keepdims=True)
    ss_ref[...] += acc


def medium_call(inputs, gate_medium, key_medium, rim, taps):
    channels, length = inputs.shape
    per_group = channels // taps.shape[0]
    block = 2048
    tap_block = block // per_group
    big = pl.BlockSpec((block, length), lambda b: (b, 0))
    return pl.pallas_call(
        medium_kernel,
        grid=(channels // block,),
        in_specs=[big, big, big, big, pl.BlockSpec((tap_block, length), lambda b: (b, 0))],
        out_specs=[big, pl.BlockSpec((1, length), lambda b: (0, 0))],
        out_shape=[
            jax.ShapeDtypeStruct((channels, length), F32),
            jax.ShapeDtypeStruct((1, length), F32),
        ],
        compiler_params=pltpu.CompilerParams(dimension_semantics=("arbitrary",)),
    )(inputs, gate_medium, key_medium, rim, taps)


def load_values(am_ref, kl_ref, g_ref, r_ref, vt_ref):
    r = r_ref[...]
    for i in range(SUB):
        rows = slice(i * LANE, (i + 1) * LANE)
        normed = am_ref[rows, :] * r * g_ref[rows, :]
        v = (kl_ref[rows, :].astype(F32) * normed).astype(BF16).astype(F32)
        vt_ref[pl.ds(i, LANE, stride=SUB), :] = v.T


def token_tile(ref, t):
    return ref[pl.ds(pl.multiple_of(t * SUB, SUB), SUB), :]


def final_state_kernel(am_ref, kl_ref, g_ref, r_ref, lam_ref, f_ref, vt_ref):
    modes = lam_ref.shape[0]
    length = am_ref.shape[1]
    load_values(am_ref, kl_ref, g_ref, r_ref, vt_ref)
    lam = [lam_ref[m] for m in range(modes)]

    def body(t, h):
        v = token_tile(vt_ref, t)
        return tuple(lam[m] * h[m] + v for m in range(modes))

    h = lax.fori_loop(0, length, body, tuple(jnp.zeros((SUB, LANE), F32) for _ in range(modes)), unroll=8)
    for m in range(modes):
        f_ref[m] = h[m].astype(f_ref.dtype)


def output_kernel(am_ref, vt_ref, gl_ref, lam_ref, w_ref, h0_ref, out_ref, yt_ref):
    modes = lam_ref.shape[0]
    length = am_ref.shape[1]
    lam = [lam_ref[m] for m in range(modes)]
    w = [w_ref[m] for m in range(modes)]

    def body(t, h):
        v = token_tile(vt_ref, t)
        h = tuple(lam[m] * h[m] + v for m in range(modes))
        y = w[0] * h[0]
        for m in range(1, modes):
            y = y + w[m] * h[m]
        yt_ref[pl.ds(pl.multiple_of(t * SUB, SUB), SUB), :] = y
        return h

    lax.fori_loop(0, length, body, tuple(h0_ref[m] for m in range(modes)), unroll=8)
    for i in range(SUB):
        rows = slice(i * LANE, (i + 1) * LANE)
        long_out = yt_ref[pl.ds(i, LANE, stride=SUB), :].T.astype(BF16).astype(F32)
        out_ref[rows, :] = (am_ref[rows, :] + gl_ref[rows, :].astype(F32) * long_out).astype(BF16)


def tiled_spec(lead):
    return pl.BlockSpec((lead, None, SUB, LANE), lambda b: (0, b, 0, 0))


def final_state_call(am, kl, gain, r, lam):
    channels, length = am.shape
    modes = lam.shape[0]
    big = pl.BlockSpec((TILE, length), lambda b: (b, 0))
    return pl.pallas_call(
        final_state_kernel,
        grid=(channels // TILE,),
        in_specs=[big, big, pl.BlockSpec((TILE, 1), lambda b: (b, 0)), pl.BlockSpec((1, length), lambda b: (0, 0)), tiled_spec(modes)],
        out_specs=[tiled_spec(modes), pl.BlockSpec((length * SUB, LANE), lambda b: (b, 0))],
        out_shape=[
            jax.ShapeDtypeStruct(lam.shape, BF16),
            jax.ShapeDtypeStruct((channels // TILE * length * SUB, LANE), F32),
        ],
    )(am, kl, gain, r, lam)


def output_call(am, vt, gl, lam, w, h0):
    channels, length = am.shape
    modes = lam.shape[0]
    big = pl.BlockSpec((TILE, length), lambda b: (b, 0))
    return pl.pallas_call(
        output_kernel,
        grid=(channels // TILE,),
        in_specs=[big, pl.BlockSpec((length * SUB, LANE), lambda b: (b, 0)), big, tiled_spec(modes), tiled_spec(modes), tiled_spec(modes)],
        out_specs=big,
        out_shape=jax.ShapeDtypeStruct((channels, length), BF16),
        scratch_shapes=[pltpu.VMEM((length * SUB, LANE), F32)],
    )(am, vt, gl, lam, w, h0)


def to_tiles(a):
    channels, k = a.shape
    return a.T.reshape(k, channels // TILE, SUB, LANE)


def on_device(
    inputs,
    gate_medium,
    key_medium,
    gate_long,
    key_long,
    medium_taps,
    log_decay,
    residues,
    norm_gain,
):
    channels, length = inputs.shape
    assert length == medium_taps.shape[1]
    width = channels * lax.axis_size("tensor")
    source = inputs.astype(F32)
    values_medium = (key_medium.astype(F32) * source).astype(BF16)
    rim = shifted(values_medium, "context", 1)
    after_medium, partial = medium_call(inputs, gate_medium, key_medium, rim, medium_taps)
    totals = lax.psum(partial, "tensor")
    r = lax.rsqrt(totals / width + EPS)
    gain = norm_gain[:, None]
    a_t = to_tiles(log_decay)
    lam = jnp.exp(-a_t)
    w = to_tiles(residues * jnp.sqrt(2.0 * log_decay))
    finals, vt = final_state_call(after_medium, key_long, gain, r, lam)

    sent = finals
    carried = shifted(sent, "context", 1).astype(F32)
    distance = 1
    if lax.axis_size("context") > 2:
        decay = jnp.exp(-length * a_t)
        carried = carried + decay * shifted(sent, "context", 2).astype(F32)
        distance = 2
    while distance < lax.axis_size("context"):
        decay = jnp.exp(-(length * distance) * a_t)
        carried = carried + decay * shifted(carried.astype(BF16), "context", distance).astype(F32)
        distance *= 2

    return output_call(after_medium, vt, gate_long, lam, w, carried)


def solution(mesh):
    return jax.shard_map(
        on_device,
        mesh=mesh,
        in_specs=(
            P("tensor", ("groups", "context")),
            P("tensor", ("groups", "context")),
            P("tensor", ("groups", "context")),
            P("tensor", ("groups", "context")),
            P("tensor", ("groups", "context")),
            P("tensor", None),
            P("tensor", None),
            P("tensor", None),
            P("tensor"),
        ),
        out_specs=P("tensor", ("groups", "context")),
        check_vma=False,
    )
```

```python
import functools

import jax
import jax.numpy as jnp
from jax import lax
from jax.experimental import pallas as pl
from jax.experimental.pallas import tpu as pltpu
from jax.sharding import PartitionSpec as P

F32 = jnp.float32
BF16 = jnp.bfloat16
EPS = 1e-05
SUB, LANE = 8, 128
TILE = SUB * LANE


def shifted(block, axis, distance):
    devices = range(lax.axis_size(axis))
    route = [(i - distance, i) for i in devices if i - distance in devices]
    return lax.ppermute(block, axis, route)


def medium_kernel(x_ref, gm_ref, km_ref, rim_ref, taps_ref, am_ref, ss_ref):
    rows, length = x_ref.shape
    groups = taps_ref.shape[0]
    per_group = rows // groups
    row = lax.broadcasted_iota(jnp.int32, (length, length), 0)
    col = lax.broadcasted_iota(jnp.int32, (length, length), 1)
    upper = col >= row

    @pl.when(pl.program_id(0) == 0)
    def _():
        ss_ref[...] = jnp.zeros_like(ss_ref)

    acc = jnp.zeros((1, length), F32)
    for g in range(groups):
        lo, hi = g * per_group, (g + 1) * per_group
        taps = jnp.broadcast_to(taps_ref[g : g + 1, :].astype(F32), (length, length))
        rolled = pltpu.roll(taps, 0, 1, stride=1, stride_axis=0)
        t_cur = jnp.where(upper, rolled, 0.0).astype(BF16)
        t_rim = jnp.where(upper, 0.0, rolled).astype(BF16)
        x = x_ref[lo:hi, :].astype(F32)
        vm = (km_ref[lo:hi, :].astype(F32) * x).astype(BF16)
        ext = jnp.concatenate([rim_ref[lo:hi, :], vm], axis=1)
        conv = jnp.dot(ext, jnp.concatenate([t_rim, t_cur], axis=0), preferred_element_type=F32)
        am = x + gm_ref[lo:hi, :].astype(F32) * conv
        am_ref[lo:hi, :] = am
        acc = acc + jnp.sum(am * am, axis=0, keepdims=True)
    ss_ref[...] += acc


def medium_call(inputs, gate_medium, key_medium, rim, taps):
    channels, length = inputs.shape
    per_group = channels // taps.shape[0]
    block = 2048
    tap_block = block // per_group
    big = pl.BlockSpec((block, length), lambda b: (b, 0))
    return pl.pallas_call(
        medium_kernel,
        grid=(channels // block,),
        in_specs=[big, big, big, big, pl.BlockSpec((tap_block, length), lambda b: (b, 0))],
        out_specs=[big, pl.BlockSpec((1, length), lambda b: (0, 0))],
        out_shape=[
            jax.ShapeDtypeStruct((channels, length), F32),
            jax.ShapeDtypeStruct((1, length), F32),
        ],
        compiler_params=pltpu.CompilerParams(dimension_semantics=("arbitrary",)),
    )(inputs, gate_medium, key_medium, rim, taps)


def load_values(am_ref, kl_ref, g_ref, r_ref, vt_ref, sb):
    r = r_ref[...]
    length = am_ref.shape[1]
    for i in range(SUB):
        rows = slice(sb * TILE + i * LANE, sb * TILE + (i + 1) * LANE)
        normed = am_ref[rows, :] * r * g_ref[rows, :]
        v = (kl_ref[rows, :].astype(F32) * normed).astype(BF16).astype(F32)
        vt_ref[pl.ds(sb * length * SUB + i, LANE, stride=SUB), :] = v.T


def token_tile(ref, base, t):
    return ref[pl.ds(pl.multiple_of(base + t * SUB, SUB), SUB), :]


def final_state_kernel(am_ref, kl_ref, g_ref, r_ref, lam_ref, f_ref, vt_ref):
    modes, subs = lam_ref.shape[0], lam_ref.shape[1]
    length = am_ref.shape[1]
    for sb in range(subs):
        load_values(am_ref, kl_ref, g_ref, r_ref, vt_ref, sb)
        lam = [lam_ref[m, sb] for m in range(modes)]
        base = sb * length * SUB

        def body(t, h):
            v = token_tile(vt_ref, base, t)
            return tuple(lam[m] * h[m] + v for m in range(modes))

        h = lax.fori_loop(0, length, body, tuple(jnp.zeros((SUB, LANE), F32) for _ in range(modes)), unroll=8)
        for m in range(modes):
            f_ref[m, sb] = h[m].astype(f_ref.dtype)


def output_kernel(am_ref, vt_ref, gl_ref, lam_ref, w_ref, h0_ref, out_ref, yt_ref):
    modes, subs = lam_ref.shape[0], lam_ref.shape[1]
    length = am_ref.shape[1]
    for sb in range(subs):
        lam = [lam_ref[m, sb] for m in range(modes)]
        w = [w_ref[m, sb] for m in range(modes)]
        base = sb * length * SUB

        def body(t, h):
            v = token_tile(vt_ref, base, t)
            h = tuple(lam[m] * h[m] + v for m in range(modes))
            y = w[0] * h[0]
            for m in range(1, modes):
                y = y + w[m] * h[m]
            yt_ref[pl.ds(pl.multiple_of(t * SUB, SUB), SUB), :] = y
            return h

        lax.fori_loop(0, length, body, tuple(h0_ref[m, sb] for m in range(modes)), unroll=8)
        for i in range(SUB):
            rows = slice(sb * TILE + i * LANE, sb * TILE + (i + 1) * LANE)
            long_out = yt_ref[pl.ds(i, LANE, stride=SUB), :].T.astype(BF16).astype(F32)
            out_ref[rows, :] = (am_ref[rows, :] + gl_ref[rows, :].astype(F32) * long_out).astype(BF16)


SUBS = 2


def tiled_spec(lead, subs):
    return pl.BlockSpec((lead, subs, SUB, LANE), lambda b: (0, b, 0, 0))


def final_state_call(am, kl, gain, r, lam):
    channels, length = am.shape
    modes = lam.shape[0]
    subs = min(SUBS, channels // TILE)
    rows = subs * TILE
    big = pl.BlockSpec((rows, length), lambda b: (b, 0))
    return pl.pallas_call(
        final_state_kernel,
        grid=(channels // rows,),
        in_specs=[big, big, pl.BlockSpec((rows, 1), lambda b: (b, 0)), pl.BlockSpec((1, length), lambda b: (0, 0)), tiled_spec(modes, subs)],
        out_specs=[tiled_spec(modes, subs), pl.BlockSpec((subs * length * SUB, LANE), lambda b: (b, 0))],
        out_shape=[
            jax.ShapeDtypeStruct(lam.shape, BF16),
            jax.ShapeDtypeStruct((channels // TILE * length * SUB, LANE), F32),
        ],
    )(am, kl, gain, r, lam)


def output_call(am, vt, gl, lam, w, h0):
    channels, length = am.shape
    modes = lam.shape[0]
    subs = min(SUBS, channels // TILE)
    rows = subs * TILE
    big = pl.BlockSpec((rows, length), lambda b: (b, 0))
    tiles = tiled_spec(modes, subs)
    return pl.pallas_call(
        output_kernel,
        grid=(channels // rows,),
        in_specs=[big, pl.BlockSpec((subs * length * SUB, LANE), lambda b: (b, 0)), big, tiles, tiles, tiles],
        out_specs=big,
        out_shape=jax.ShapeDtypeStruct((channels, length), BF16),
        scratch_shapes=[pltpu.VMEM((length * SUB, LANE), F32)],
    )(am, vt, gl, lam, w, h0)


def to_tiles(a):
    channels, k = a.shape
    return a.T.reshape(k, channels // TILE, SUB, LANE)


def on_device(
    inputs,
    gate_medium,
    key_medium,
    gate_long,
    key_long,
    medium_taps,
    log_decay,
    residues,
    norm_gain,
):
    channels, length = inputs.shape
    assert length == medium_taps.shape[1]
    width = channels * lax.axis_size("tensor")
    source = inputs.astype(F32)
    values_medium = (key_medium.astype(F32) * source).astype(BF16)
    rim = shifted(values_medium, "context", 1)
    after_medium, partial = medium_call(inputs, gate_medium, key_medium, rim, medium_taps)
    totals = lax.psum(partial, "tensor")
    r = lax.rsqrt(totals / width + EPS)
    gain = norm_gain[:, None]
    a_t = to_tiles(log_decay)
    lam = jnp.exp(-a_t)
    w = to_tiles(residues * jnp.sqrt(2.0 * log_decay))
    finals, vt = final_state_call(after_medium, key_long, gain, r, lam)

    sent = finals
    carried = shifted(sent, "context", 1).astype(F32)
    distance = 1
    if lax.axis_size("context") > 2:
        decay = jnp.exp(-length * a_t)
        carried = carried + decay * shifted(sent, "context", 2).astype(F32)
        distance = 2
    while distance < lax.axis_size("context"):
        decay = jnp.exp(-(length * distance) * a_t)
        carried = carried + decay * shifted(carried.astype(BF16), "context", distance).astype(F32)
        distance *= 2

    return output_call(after_medium, vt, gate_long, lam, w, carried)


def solution(mesh):
    return jax.shard_map(
        on_device,
        mesh=mesh,
        in_specs=(
            P("tensor", ("groups", "context")),
            P("tensor", ("groups", "context")),
            P("tensor", ("groups", "context")),
            P("tensor", ("groups", "context")),
            P("tensor", ("groups", "context")),
            P("tensor", None),
            P("tensor", None),
            P("tensor", None),
            P("tensor"),
        ),
        out_specs=P("tensor", ("groups", "context")),
        check_vma=False,
    )
```

```python
import functools

import jax
import jax.numpy as jnp
from jax import lax
from jax.experimental import pallas as pl
from jax.experimental.pallas import tpu as pltpu
from jax.sharding import PartitionSpec as P

F32 = jnp.float32
BF16 = jnp.bfloat16
EPS = 1e-05
SUB, LANE = 8, 128
TILE = SUB * LANE


def shifted(block, axis, distance):
    devices = range(lax.axis_size(axis))
    route = [(i - distance, i) for i in devices if i - distance in devices]
    return lax.ppermute(block, axis, route)


def medium_kernel(x_ref, gm_ref, km_ref, rim_ref, taps_ref, am_ref, ss_ref):
    rows, length = x_ref.shape
    groups = taps_ref.shape[0]
    per_group = rows // groups
    row = lax.broadcasted_iota(jnp.int32, (length, length), 0)
    col = lax.broadcasted_iota(jnp.int32, (length, length), 1)
    upper = col >= row

    @pl.when(pl.program_id(0) == 0)
    def _():
        ss_ref[...] = jnp.zeros_like(ss_ref)

    acc = jnp.zeros((1, length), F32)
    for g in range(groups):
        lo, hi = g * per_group, (g + 1) * per_group
        taps = jnp.broadcast_to(taps_ref[g : g + 1, :].astype(F32), (length, length))
        rolled = pltpu.roll(taps, 0, 1, stride=1, stride_axis=0)
        t_cur = jnp.where(upper, rolled, 0.0).astype(BF16)
        t_rim = jnp.where(upper, 0.0, rolled).astype(BF16)
        x = x_ref[lo:hi, :].astype(F32)
        vm = (km_ref[lo:hi, :].astype(F32) * x).astype(BF16)
        ext = jnp.concatenate([rim_ref[lo:hi, :], vm], axis=1)
        conv = jnp.dot(ext, jnp.concatenate([t_rim, t_cur], axis=0), preferred_element_type=F32)
        am = x + gm_ref[lo:hi, :].astype(F32) * conv
        am_ref[lo:hi, :] = am
        acc = acc + jnp.sum(am * am, axis=0, keepdims=True)
    ss_ref[...] += acc


def medium_call(inputs, gate_medium, key_medium, rim, taps):
    channels, length = inputs.shape
    per_group = channels // taps.shape[0]
    block = 2048
    tap_block = block // per_group
    big = pl.BlockSpec((block, length), lambda b: (b, 0))
    return pl.pallas_call(
        medium_kernel,
        grid=(channels // block,),
        in_specs=[big, big, big, big, pl.BlockSpec((tap_block, length), lambda b: (b, 0))],
        out_specs=[big, pl.BlockSpec((1, length), lambda b: (0, 0))],
        out_shape=[
            jax.ShapeDtypeStruct((channels, length), F32),
            jax.ShapeDtypeStruct((1, length), F32),
        ],
        compiler_params=pltpu.CompilerParams(dimension_semantics=("arbitrary",)),
    )(inputs, gate_medium, key_medium, rim, taps)


def load_values(am_ref, kl_ref, g_ref, r_ref, vt_ref):
    r = r_ref[...]
    for i in range(SUB):
        rows = slice(i * LANE, (i + 1) * LANE)
        normed = am_ref[rows, :] * r * g_ref[rows, :]
        v = (kl_ref[rows, :].astype(F32) * normed).astype(BF16).astype(F32)
        vt_ref[pl.ds(i, LANE, stride=SUB), :] = v.T


def token_tile(ref, t):
    return ref[pl.ds(pl.multiple_of(t * SUB, SUB), SUB), :]


def final_state_kernel(am_ref, kl_ref, g_ref, r_ref, lam_ref, f_ref, vt_ref):
    modes = lam_ref.shape[0]
    length = am_ref.shape[1]
    load_values(am_ref, kl_ref, g_ref, r_ref, vt_ref)
    lam = [lam_ref[m] for m in range(modes)]

    def body(t, h):
        v = token_tile(vt_ref, t)
        return tuple(lam[m] * h[m] + v for m in range(modes))

    h = lax.fori_loop(0, length, body, tuple(jnp.zeros((SUB, LANE), F32) for _ in range(modes)), unroll=8)
    for m in range(modes):
        f_ref[m] = h[m].astype(f_ref.dtype)


def output_kernel(am_ref, vt_ref, gl_ref, lam_ref, w_ref, base_ref, decay_ref, recv_ref, out_ref, yt_ref):
    modes = lam_ref.shape[0]
    length = am_ref.shape[1]
    lam = [lam_ref[m] for m in range(modes)]
    w = [w_ref[m] for m in range(modes)]

    def body(t, h):
        v = token_tile(vt_ref, t)
        h = tuple(lam[m] * h[m] + v for m in range(modes))
        y = w[0] * h[0]
        for m in range(1, modes):
            y = y + w[m] * h[m]
        yt_ref[pl.ds(pl.multiple_of(t * SUB, SUB), SUB), :] = y
        return h

    h0 = tuple(base_ref[m] + decay_ref[m] * recv_ref[m].astype(F32) for m in range(modes))
    lax.fori_loop(0, length, body, h0, unroll=8)
    for i in range(SUB):
        rows = slice(i * LANE, (i + 1) * LANE)
        long_out = yt_ref[pl.ds(i, LANE, stride=SUB), :].T.astype(BF16).astype(F32)
        out_ref[rows, :] = (am_ref[rows, :] + gl_ref[rows, :].astype(F32) * long_out).astype(BF16)


def tiled_spec(lead):
    return pl.BlockSpec((lead, None, SUB, LANE), lambda b: (0, b, 0, 0))


def final_state_call(am, kl, gain, r, lam):
    channels, length = am.shape
    modes = lam.shape[0]
    big = pl.BlockSpec((TILE, length), lambda b: (b, 0))
    return pl.pallas_call(
        final_state_kernel,
        grid=(channels // TILE,),
        in_specs=[big, big, pl.BlockSpec((TILE, 1), lambda b: (b, 0)), pl.BlockSpec((1, length), lambda b: (0, 0)), tiled_spec(modes)],
        out_specs=[tiled_spec(modes), pl.BlockSpec((length * SUB, LANE), lambda b: (b, 0))],
        out_shape=[
            jax.ShapeDtypeStruct(lam.shape, BF16),
            jax.ShapeDtypeStruct((channels // TILE * length * SUB, LANE), F32),
        ],
    )(am, kl, gain, r, lam)


def output_call(am, vt, gl, lam, w, base, decay, recv):
    channels, length = am.shape
    modes = lam.shape[0]
    big = pl.BlockSpec((TILE, length), lambda b: (b, 0))
    return pl.pallas_call(
        output_kernel,
        grid=(channels // TILE,),
        in_specs=[big, pl.BlockSpec((length * SUB, LANE), lambda b: (b, 0)), big] + [tiled_spec(modes)] * 5,
        out_specs=big,
        out_shape=jax.ShapeDtypeStruct((channels, length), BF16),
        scratch_shapes=[pltpu.VMEM((length * SUB, LANE), F32)],
    )(am, vt, gl, lam, w, base, decay, recv)


def to_tiles(a):
    channels, k = a.shape
    return a.T.reshape(k, channels // TILE, SUB, LANE)


def on_device(
    inputs,
    gate_medium,
    key_medium,
    gate_long,
    key_long,
    medium_taps,
    log_decay,
    residues,
    norm_gain,
):
    channels, length = inputs.shape
    assert length == medium_taps.shape[1]
    width = channels * lax.axis_size("tensor")
    source = inputs.astype(F32)
    values_medium = (key_medium.astype(F32) * source).astype(BF16)
    rim = shifted(values_medium, "context", 1)
    after_medium, partial = medium_call(inputs, gate_medium, key_medium, rim, medium_taps)
    totals = lax.psum(partial, "tensor")
    r = lax.rsqrt(totals / width + EPS)
    gain = norm_gain[:, None]
    a_t = to_tiles(log_decay)
    lam = jnp.exp(-a_t)
    w = to_tiles(residues * jnp.sqrt(2.0 * log_decay))
    finals, vt = final_state_call(after_medium, key_long, gain, r, lam)

    sent = finals
    carried = shifted(sent, "context", 1).astype(F32)
    distance = 1
    if lax.axis_size("context") > 2:
        decay = jnp.exp(-length * a_t)
        carried = carried + decay * shifted(sent, "context", 2).astype(F32)
        distance = 2
    decay = jnp.zeros_like(a_t)
    received = jnp.zeros(a_t.shape, BF16)
    while distance < lax.axis_size("context"):
        if distance * 2 < lax.axis_size("context"):
            decay = jnp.exp(-(length * distance) * a_t)
            carried = carried + decay * shifted(carried.astype(BF16), "context", distance).astype(F32)
        else:
            decay = jnp.exp(-(length * distance) * a_t)
            received = shifted(carried.astype(BF16), "context", distance)
        distance *= 2

    return output_call(after_medium, vt, gate_long, lam, w, carried, decay, received)


def solution(mesh):
    return jax.shard_map(
        on_device,
        mesh=mesh,
        in_specs=(
            P("tensor", ("groups", "context")),
            P("tensor", ("groups", "context")),
            P("tensor", ("groups", "context")),
            P("tensor", ("groups", "context")),
            P("tensor", ("groups", "context")),
            P("tensor", None),
            P("tensor", None),
            P("tensor", None),
            P("tensor"),
        ),
        out_specs=P("tensor", ("groups", "context")),
        check_vma=False,
    )
```

```python
import functools

import jax
import jax.numpy as jnp
from jax import lax
from jax.experimental import pallas as pl
from jax.experimental.pallas import tpu as pltpu
from jax.sharding import PartitionSpec as P

F32 = jnp.float32
BF16 = jnp.bfloat16
EPS = 1e-05
SUB, LANE = 8, 128
TILE = SUB * LANE


def shifted(block, axis, distance):
    devices = range(lax.axis_size(axis))
    route = [(i - distance, i) for i in devices if i - distance in devices]
    return lax.ppermute(block, axis, route)


def medium_kernel(x_ref, gm_ref, km_ref, rim_ref, taps_ref, am_ref, ss_ref):
    rows, length = x_ref.shape
    groups = taps_ref.shape[0]
    per_group = rows // groups
    row = lax.broadcasted_iota(jnp.int32, (length, length), 0)
    col = lax.broadcasted_iota(jnp.int32, (length, length), 1)
    upper = col >= row

    @pl.when(pl.program_id(0) == 0)
    def _():
        ss_ref[...] = jnp.zeros_like(ss_ref)

    acc = jnp.zeros((1, length), F32)
    for g in range(groups):
        lo, hi = g * per_group, (g + 1) * per_group
        taps = jnp.broadcast_to(taps_ref[g : g + 1, :].astype(F32), (length, length))
        rolled = pltpu.roll(taps, 0, 1, stride=1, stride_axis=0)
        t_cur = jnp.where(upper, rolled, 0.0).astype(BF16)
        t_rim = jnp.where(upper, 0.0, rolled).astype(BF16)
        x = x_ref[lo:hi, :].astype(F32)
        vm = (km_ref[lo:hi, :].astype(F32) * x).astype(BF16)
        ext = jnp.concatenate([rim_ref[lo:hi, :], vm], axis=1)
        conv = jnp.dot(ext, jnp.concatenate([t_rim, t_cur], axis=0), preferred_element_type=F32)
        am = x + gm_ref[lo:hi, :].astype(F32) * conv
        am_ref[lo:hi, :] = am
        acc = acc + jnp.sum(am * am, axis=0, keepdims=True)
    ss_ref[...] += acc


def medium_call(inputs, gate_medium, key_medium, rim, taps):
    channels, length = inputs.shape
    per_group = channels // taps.shape[0]
    block = 2048
    tap_block = block // per_group
    big = pl.BlockSpec((block, length), lambda b: (b, 0))
    return pl.pallas_call(
        medium_kernel,
        grid=(channels // block,),
        in_specs=[big, big, big, big, pl.BlockSpec((tap_block, length), lambda b: (b, 0))],
        out_specs=[big, pl.BlockSpec((1, length), lambda b: (0, 0))],
        out_shape=[
            jax.ShapeDtypeStruct((channels, length), F32),
            jax.ShapeDtypeStruct((1, length), F32),
        ],
        compiler_params=pltpu.CompilerParams(dimension_semantics=("arbitrary",)),
    )(inputs, gate_medium, key_medium, rim, taps)


def load_values(am_ref, kl_ref, g_ref, r_ref, vt_ref, width):
    r = lax.rsqrt(r_ref[...] / width + EPS)
    for i in range(SUB):
        rows = slice(i * LANE, (i + 1) * LANE)
        normed = am_ref[rows, :] * r * g_ref[rows, :]
        v = (kl_ref[rows, :].astype(F32) * normed).astype(BF16).astype(F32)
        vt_ref[pl.ds(i, LANE, stride=SUB), :] = v.T


def token_tile(ref, t):
    return ref[pl.ds(pl.multiple_of(t * SUB, SUB), SUB), :]


def final_state_kernel(width, am_ref, kl_ref, g_ref, r_ref, lam_ref, f_ref, vt_ref):
    modes = lam_ref.shape[0]
    length = am_ref.shape[1]
    load_values(am_ref, kl_ref, g_ref, r_ref, vt_ref, width)
    lam = [lam_ref[m] for m in range(modes)]

    def body(t, h):
        v = token_tile(vt_ref, t)
        return tuple(lam[m] * h[m] + v for m in range(modes))

    h = lax.fori_loop(0, length, body, tuple(jnp.zeros((SUB, LANE), F32) for _ in range(modes)), unroll=8)
    for m in range(modes):
        f_ref[m] = h[m].astype(f_ref.dtype)


def output_kernel(am_ref, vt_ref, gl_ref, lam_ref, w_ref, h0_ref, out_ref, yt_ref):
    modes = lam_ref.shape[0]
    length = am_ref.shape[1]
    lam = [lam_ref[m] for m in range(modes)]
    w = [w_ref[m] for m in range(modes)]

    def body(t, h):
        v = token_tile(vt_ref, t)
        h = tuple(lam[m] * h[m] + v for m in range(modes))
        y = w[0] * h[0]
        for m in range(1, modes):
            y = y + w[m] * h[m]
        yt_ref[pl.ds(pl.multiple_of(t * SUB, SUB), SUB), :] = y
        return h

    lax.fori_loop(0, length, body, tuple(h0_ref[m] for m in range(modes)), unroll=8)
    for i in range(SUB):
        rows = slice(i * LANE, (i + 1) * LANE)
        long_out = yt_ref[pl.ds(i, LANE, stride=SUB), :].T.astype(BF16).astype(F32)
        out_ref[rows, :] = (am_ref[rows, :] + gl_ref[rows, :].astype(F32) * long_out).astype(BF16)


def tiled_spec(lead):
    return pl.BlockSpec((lead, None, SUB, LANE), lambda b: (0, b, 0, 0))


def final_state_call(am, kl, gain, totals, lam, width):
    channels, length = am.shape
    modes = lam.shape[0]
    big = pl.BlockSpec((TILE, length), lambda b: (b, 0))
    return pl.pallas_call(
        functools.partial(final_state_kernel, float(width)),
        grid=(channels // TILE,),
        in_specs=[big, big, pl.BlockSpec((TILE, 1), lambda b: (b, 0)), pl.BlockSpec((1, length), lambda b: (0, 0)), tiled_spec(modes)],
        out_specs=[tiled_spec(modes), pl.BlockSpec((length * SUB, LANE), lambda b: (b, 0))],
        out_shape=[
            jax.ShapeDtypeStruct(lam.shape, BF16),
            jax.ShapeDtypeStruct((channels // TILE * length * SUB, LANE), F32),
        ],
    )(am, kl, gain, totals, lam)


def output_call(am, vt, gl, lam, w, h0):
    channels, length = am.shape
    modes = lam.shape[0]
    big = pl.BlockSpec((TILE, length), lambda b: (b, 0))
    return pl.pallas_call(
        output_kernel,
        grid=(channels // TILE,),
        in_specs=[big, pl.BlockSpec((length * SUB, LANE), lambda b: (b, 0)), big, tiled_spec(modes), tiled_spec(modes), tiled_spec(modes)],
        out_specs=big,
        out_shape=jax.ShapeDtypeStruct((channels, length), BF16),
        scratch_shapes=[pltpu.VMEM((length * SUB, LANE), F32)],
    )(am, vt, gl, lam, w, h0)


def to_tiles(a):
    channels, k = a.shape
    return a.T.reshape(k, channels // TILE, SUB, LANE)


def on_device(
    inputs,
    gate_medium,
    key_medium,
    gate_long,
    key_long,
    medium_taps,
    log_decay,
    residues,
    norm_gain,
):
    channels, length = inputs.shape
    assert length == medium_taps.shape[1]
    width = channels * lax.axis_size("tensor")
    source = inputs.astype(F32)
    values_medium = (key_medium.astype(F32) * source).astype(BF16)
    rim = shifted(values_medium, "context", 1)
    after_medium, partial = medium_call(inputs, gate_medium, key_medium, rim, medium_taps)
    totals = lax.psum(partial, "tensor")
    gain = norm_gain[:, None]
    a_t = to_tiles(log_decay)
    lam = jnp.exp(-a_t)
    w = to_tiles(residues * jnp.sqrt(2.0 * log_decay))
    finals, vt = final_state_call(after_medium, key_long, gain, totals, lam, width)

    sent = finals
    carried = shifted(sent, "context", 1).astype(F32)
    distance = 1
    if lax.axis_size("context") > 2:
        decay = jnp.exp(-length * a_t)
        carried = carried + decay * shifted(sent, "context", 2).astype(F32)
        distance = 2
    while distance < lax.axis_size("context"):
        decay = jnp.exp(-(length * distance) * a_t)
        carried = carried + decay * shifted(carried.astype(BF16), "context", distance).astype(F32)
        distance *= 2

    return output_call(after_medium, vt, gate_long, lam, w, carried)


def solution(mesh):
    return jax.shard_map(
        on_device,
        mesh=mesh,
        in_specs=(
            P("tensor", ("groups", "context")),
            P("tensor", ("groups", "context")),
            P("tensor", ("groups", "context")),
            P("tensor", ("groups", "context")),
            P("tensor", ("groups", "context")),
            P("tensor", None),
            P("tensor", None),
            P("tensor", None),
            P("tensor"),
        ),
        out_specs=P("tensor", ("groups", "context")),
        check_vma=False,
    )
```

```python
import functools

import jax
import jax.numpy as jnp
from jax import lax
from jax.experimental import pallas as pl
from jax.experimental.pallas import tpu as pltpu
from jax.sharding import PartitionSpec as P

F32 = jnp.float32
BF16 = jnp.bfloat16
EPS = 1e-05
SUB, LANE = 8, 128
TILE = SUB * LANE


def shifted(block, axis, distance):
    devices = range(lax.axis_size(axis))
    route = [(i - distance, i) for i in devices if i - distance in devices]
    return lax.ppermute(block, axis, route)


def medium_kernel(x_ref, gm_ref, km_ref, rim_ref, taps_ref, am_ref, ss_ref):
    rows, length = x_ref.shape
    groups = taps_ref.shape[0]
    per_group = rows // groups
    row = lax.broadcasted_iota(jnp.int32, (length, length), 0)
    col = lax.broadcasted_iota(jnp.int32, (length, length), 1)
    upper = col >= row

    @pl.when(pl.program_id(0) == 0)
    def _():
        ss_ref[...] = jnp.zeros_like(ss_ref)

    acc = jnp.zeros((1, length), F32)
    for g in range(groups):
        lo, hi = g * per_group, (g + 1) * per_group
        taps = jnp.broadcast_to(taps_ref[g : g + 1, :].astype(F32), (length, length))
        rolled = pltpu.roll(taps, 0, 1, stride=1, stride_axis=0)
        t_cur = jnp.where(upper, rolled, 0.0).astype(BF16)
        t_rim = jnp.where(upper, 0.0, rolled).astype(BF16)
        x = x_ref[lo:hi, :].astype(F32)
        vm = (km_ref[lo:hi, :].astype(F32) * x).astype(BF16)
        ext = jnp.concatenate([rim_ref[lo:hi, :], vm], axis=1)
        conv = jnp.dot(ext, jnp.concatenate([t_rim, t_cur], axis=0), preferred_element_type=F32)
        am = x + gm_ref[lo:hi, :].astype(F32) * conv
        am_ref[lo:hi, :] = am
        acc = acc + jnp.sum(am * am, axis=0, keepdims=True)
    ss_ref[...] += acc


def medium_call(inputs, gate_medium, key_medium, rim, taps):
    channels, length = inputs.shape
    per_group = channels // taps.shape[0]
    block = 2048
    tap_block = block // per_group
    big = pl.BlockSpec((block, length), lambda b: (b, 0))
    return pl.pallas_call(
        medium_kernel,
        grid=(channels // block,),
        in_specs=[big, big, big, big, pl.BlockSpec((tap_block, length), lambda b: (b, 0))],
        out_specs=[big, pl.BlockSpec((1, length), lambda b: (0, 0))],
        out_shape=[
            jax.ShapeDtypeStruct((channels, length), F32),
            jax.ShapeDtypeStruct((1, length), F32),
        ],
        compiler_params=pltpu.CompilerParams(dimension_semantics=("arbitrary",)),
    )(inputs, gate_medium, key_medium, rim, taps)


def load_values(am_ref, kl_ref, g_ref, r_ref, vt_ref):
    r = r_ref[...]
    for i in range(SUB):
        rows = slice(i * LANE, (i + 1) * LANE)
        normed = am_ref[rows, :] * r * g_ref[rows, :]
        v = (kl_ref[rows, :].astype(F32) * normed).astype(BF16).astype(F32)
        vt_ref[pl.ds(i, LANE, stride=SUB), :] = v.T


def token_tile(ref, t):
    return ref[pl.ds(pl.multiple_of(t * SUB, SUB), SUB), :]


def final_state_kernel(am_ref, kl_ref, g_ref, r_ref, lam_ref, f_ref, vt_ref):
    modes = lam_ref.shape[0]
    length = am_ref.shape[1]
    load_values(am_ref, kl_ref, g_ref, r_ref, vt_ref)
    lam = [lam_ref[m] for m in range(modes)]

    def body(t, h):
        v = token_tile(vt_ref, t)
        return tuple(lam[m] * h[m] + v for m in range(modes))

    h = lax.fori_loop(0, length, body, tuple(jnp.zeros((SUB, LANE), F32) for _ in range(modes)), unroll=8)
    for m in range(modes):
        f_ref[m] = h[m].astype(f_ref.dtype)


def output_kernel(am_ref, vt_ref, gl_ref, lam_ref, w_ref, h0_ref, out_ref, yt_ref):
    modes = lam_ref.shape[0]
    length = am_ref.shape[1]
    lam = [lam_ref[m] for m in range(modes)]
    w = [w_ref[m] for m in range(modes)]

    def body(t, h):
        v = token_tile(vt_ref, t)
        h = tuple(lam[m] * h[m] + v for m in range(modes))
        y = w[0] * h[0]
        for m in range(1, modes):
            y = y + w[m] * h[m]
        yt_ref[pl.ds(pl.multiple_of(t * SUB, SUB), SUB), :] = y
        return h

    lax.fori_loop(0, length, body, tuple(h0_ref[m] for m in range(modes)), unroll=8)
    for i in range(SUB):
        rows = slice(i * LANE, (i + 1) * LANE)
        long_out = yt_ref[pl.ds(i, LANE, stride=SUB), :].T.astype(BF16).astype(F32)
        out_ref[rows, :] = (am_ref[rows, :] + gl_ref[rows, :].astype(F32) * long_out).astype(BF16)


def tiled_spec(lead):
    return pl.BlockSpec((lead, None, SUB, LANE), lambda b: (0, b, 0, 0))


def final_state_call(am, kl, gain, r, lam):
    channels, length = am.shape
    modes = lam.shape[0]
    big = pl.BlockSpec((TILE, length), lambda b: (b, 0))
    return pl.pallas_call(
        final_state_kernel,
        grid=(channels // TILE,),
        in_specs=[big, big, pl.BlockSpec((TILE, 1), lambda b: (b, 0)), pl.BlockSpec((1, length), lambda b: (0, 0)), tiled_spec(modes)],
        out_specs=[tiled_spec(modes), pl.BlockSpec((length * SUB, LANE), lambda b: (b, 0))],
        out_shape=[
            jax.ShapeDtypeStruct(lam.shape, BF16),
            jax.ShapeDtypeStruct((channels // TILE * length * SUB, LANE), F32),
        ],
    )(am, kl, gain, r, lam)


def output_call(am, vt, gl, lam, w, h0):
    channels, length = am.shape
    modes = lam.shape[0]
    big = pl.BlockSpec((TILE, length), lambda b: (b, 0))
    return pl.pallas_call(
        output_kernel,
        grid=(channels // TILE,),
        in_specs=[big, pl.BlockSpec((length * SUB, LANE), lambda b: (b, 0)), big, tiled_spec(modes), tiled_spec(modes), tiled_spec(modes)],
        out_specs=big,
        out_shape=jax.ShapeDtypeStruct((channels, length), BF16),
        scratch_shapes=[pltpu.VMEM((length * SUB, LANE), F32)],
    )(am, vt, gl, lam, w, h0)


def to_tiles(a):
    channels, k = a.shape
    return a.T.reshape(k, channels // TILE, SUB, LANE)


def on_device(
    inputs,
    gate_medium,
    key_medium,
    gate_long,
    key_long,
    medium_taps,
    log_decay,
    residues,
    norm_gain,
):
    channels, length = inputs.shape
    assert length == medium_taps.shape[1]
    width = channels * lax.axis_size("tensor")
    source = inputs.astype(F32)
    values_medium = (key_medium.astype(F32) * source).astype(BF16)
    rim = shifted(values_medium, "context", 1)
    after_medium, partial = medium_call(inputs, gate_medium, key_medium, rim, medium_taps)
    if lax.axis_size("tensor") == 2:
        totals = partial + lax.ppermute(partial, "tensor", [(0, 1), (1, 0)])
    else:
        totals = lax.psum(partial, "tensor")
    r = lax.rsqrt(totals / width + EPS)
    gain = norm_gain[:, None]
    a_t = to_tiles(log_decay)
    lam = jnp.exp(-a_t)
    w = to_tiles(residues * jnp.sqrt(2.0 * log_decay))
    finals, vt = final_state_call(after_medium, key_long, gain, r, lam)

    sent = finals
    carried = shifted(sent, "context", 1).astype(F32)
    distance = 1
    if lax.axis_size("context") > 2:
        decay = jnp.exp(-length * a_t)
        carried = carried + decay * shifted(sent, "context", 2).astype(F32)
        distance = 2
    while distance < lax.axis_size("context"):
        decay = jnp.exp(-(length * distance) * a_t)
        carried = carried + decay * shifted(carried.astype(BF16), "context", distance).astype(F32)
        distance *= 2

    return output_call(after_medium, vt, gate_long, lam, w, carried)


def solution(mesh):
    return jax.shard_map(
        on_device,
        mesh=mesh,
        in_specs=(
            P("tensor", ("groups", "context")),
            P("tensor", ("groups", "context")),
            P("tensor", ("groups", "context")),
            P("tensor", ("groups", "context")),
            P("tensor", ("groups", "context")),
            P("tensor", None),
            P("tensor", None),
            P("tensor", None),
            P("tensor"),
        ),
        out_specs=P("tensor", ("groups", "context")),
        check_vma=False,
    )
```

```python
import functools

import jax
import jax.numpy as jnp
from jax import lax
from jax.experimental import pallas as pl
from jax.experimental.pallas import tpu as pltpu
from jax.sharding import PartitionSpec as P

F32 = jnp.float32
BF16 = jnp.bfloat16
EPS = 1e-05
SUB, LANE = 8, 128
TILE = SUB * LANE


def shifted(block, axis, distance):
    devices = range(lax.axis_size(axis))
    route = [(i - distance, i) for i in devices if i - distance in devices]
    return lax.ppermute(block, axis, route)


def medium_kernel(x_ref, gm_ref, km_ref, rim_ref, taps_ref, am_ref, ss_ref):
    rows, length = x_ref.shape
    groups = taps_ref.shape[0]
    per_group = rows // groups
    row = lax.broadcasted_iota(jnp.int32, (length, length), 0)
    col = lax.broadcasted_iota(jnp.int32, (length, length), 1)
    upper = col >= row

    @pl.when(pl.program_id(0) == 0)
    def _():
        ss_ref[...] = jnp.zeros_like(ss_ref)

    acc = jnp.zeros((1, length), F32)
    for g in range(groups):
        lo, hi = g * per_group, (g + 1) * per_group
        taps = jnp.broadcast_to(taps_ref[g : g + 1, :].astype(F32), (length, length))
        rolled = pltpu.roll(taps, 0, 1, stride=1, stride_axis=0)
        t_cur = jnp.where(upper, rolled, 0.0).astype(BF16)
        t_rim = jnp.where(upper, 0.0, rolled).astype(BF16)
        x = x_ref[lo:hi, :].astype(F32)
        vm = (km_ref[lo:hi, :].astype(F32) * x).astype(BF16)
        ext = jnp.concatenate([rim_ref[lo:hi, :], vm], axis=1)
        conv = jnp.dot(ext, jnp.concatenate([t_rim, t_cur], axis=0), preferred_element_type=F32)
        am = x + gm_ref[lo:hi, :].astype(F32) * conv
        am_ref[lo:hi, :] = am
        acc = acc + jnp.sum(am * am, axis=0, keepdims=True)
    ss_ref[...] += acc


def medium_call(inputs, gate_medium, key_medium, rim, taps):
    channels, length = inputs.shape
    per_group = channels // taps.shape[0]
    block = 2048
    tap_block = block // per_group
    big = pl.BlockSpec((block, length), lambda b: (b, 0))
    return pl.pallas_call(
        medium_kernel,
        grid=(channels // block,),
        in_specs=[big, big, big, big, pl.BlockSpec((tap_block, length), lambda b: (b, 0))],
        out_specs=[big, pl.BlockSpec((1, length), lambda b: (0, 0))],
        out_shape=[
            jax.ShapeDtypeStruct((channels, length), F32),
            jax.ShapeDtypeStruct((1, length), F32),
        ],
        compiler_params=pltpu.CompilerParams(dimension_semantics=("arbitrary",)),
    )(inputs, gate_medium, key_medium, rim, taps)


def load_values(am_ref, kl_ref, g_ref, r_ref, vt_ref):
    r = r_ref[...]
    for i in range(SUB):
        rows = slice(i * LANE, (i + 1) * LANE)
        normed = am_ref[rows, :] * r * g_ref[rows, :]
        v = (kl_ref[rows, :].astype(F32) * normed).astype(BF16).astype(F32)
        vt_ref[pl.ds(i, LANE, stride=SUB), :] = v.T


def token_tile(ref, t):
    return ref[pl.ds(pl.multiple_of(t * SUB, SUB), SUB), :]


def final_state_kernel(am_ref, kl_ref, g_ref, r_ref, lam_ref, f_ref, vt_ref):
    modes = lam_ref.shape[0]
    length = am_ref.shape[1]
    load_values(am_ref, kl_ref, g_ref, r_ref, vt_ref)
    lam = [lam_ref[m] for m in range(modes)]

    def body(t, h):
        v = token_tile(vt_ref, t)
        return tuple(lam[m] * h[m] + v for m in range(modes))

    h = lax.fori_loop(0, length, body, tuple(jnp.zeros((SUB, LANE), F32) for _ in range(modes)), unroll=8)
    for m in range(modes):
        f_ref[m] = h[m].astype(f_ref.dtype)


def output_kernel(am_ref, vt_ref, gl_ref, lam_ref, w_ref, h0_ref, out_ref, yt_ref):
    modes = lam_ref.shape[0]
    length = am_ref.shape[1]
    lam = [lam_ref[m] for m in range(modes)]
    w = [w_ref[m] for m in range(modes)]

    def body(t, h):
        v = token_tile(vt_ref, t)
        h = tuple(lam[m] * h[m] + v for m in range(modes))
        y = w[0] * h[0]
        for m in range(1, modes):
            y = y + w[m] * h[m]
        yt_ref[pl.ds(pl.multiple_of(t * SUB, SUB), SUB), :] = y
        return h

    lax.fori_loop(0, length, body, tuple(h0_ref[m] for m in range(modes)), unroll=8)
    for i in range(SUB):
        rows = slice(i * LANE, (i + 1) * LANE)
        long_out = yt_ref[pl.ds(i, LANE, stride=SUB), :].T.astype(BF16).astype(F32)
        out_ref[rows, :] = (am_ref[rows, :] + gl_ref[rows, :].astype(F32) * long_out).astype(BF16)


def tiled_spec(lead):
    return pl.BlockSpec((lead, None, SUB, LANE), lambda b: (0, b, 0, 0))


def final_state_call(am, kl, gain, r, lam):
    channels, length = am.shape
    modes = lam.shape[0]
    big = pl.BlockSpec((TILE, length), lambda b: (b, 0))
    return pl.pallas_call(
        final_state_kernel,
        grid=(channels // TILE,),
        in_specs=[big, big, big, pl.BlockSpec((1, length), lambda b: (0, 0)), tiled_spec(modes)],
        out_specs=[tiled_spec(modes), pl.BlockSpec((length * SUB, LANE), lambda b: (b, 0))],
        out_shape=[
            jax.ShapeDtypeStruct(lam.shape, BF16),
            jax.ShapeDtypeStruct((channels // TILE * length * SUB, LANE), F32),
        ],
    )(am, kl, gain, r, lam)


def output_call(am, vt, gl, lam, w, h0):
    channels, length = am.shape
    modes = lam.shape[0]
    big = pl.BlockSpec((TILE, length), lambda b: (b, 0))
    return pl.pallas_call(
        output_kernel,
        grid=(channels // TILE,),
        in_specs=[big, pl.BlockSpec((length * SUB, LANE), lambda b: (b, 0)), big, tiled_spec(modes), tiled_spec(modes), tiled_spec(modes)],
        out_specs=big,
        out_shape=jax.ShapeDtypeStruct((channels, length), BF16),
        scratch_shapes=[pltpu.VMEM((length * SUB, LANE), F32)],
    )(am, vt, gl, lam, w, h0)


def to_tiles(a):
    channels, k = a.shape
    return a.T.reshape(k, channels // TILE, SUB, LANE)


def on_device(
    inputs,
    gate_medium,
    key_medium,
    gate_long,
    key_long,
    medium_taps,
    log_decay,
    residues,
    norm_gain,
):
    channels, length = inputs.shape
    assert length == medium_taps.shape[1]
    width = channels * lax.axis_size("tensor")
    source = inputs.astype(F32)
    values_medium = (key_medium.astype(F32) * source).astype(BF16)
    rim = shifted(values_medium, "context", 1)
    gain = jnp.broadcast_to(norm_gain[:, None], inputs.shape)
    a_t = to_tiles(log_decay)
    lam = jnp.exp(-a_t)
    w = to_tiles(residues * jnp.sqrt(2.0 * log_decay))
    rim, gain, a_t, lam, w = lax.optimization_barrier((rim, gain, a_t, lam, w))
    after_medium, partial = medium_call(inputs, gate_medium, key_medium, rim, medium_taps)
    if lax.axis_size("tensor") == 2:
        totals = partial + lax.ppermute(partial, "tensor", [(0, 1), (1, 0)])
    else:
        totals = lax.psum(partial, "tensor")
    r = lax.rsqrt(totals / width + EPS)
    finals, vt = final_state_call(after_medium, key_long, gain, r, lam)

    sent = finals
    carried = shifted(sent, "context", 1).astype(F32)
    distance = 1
    if lax.axis_size("context") > 2:
        decay = jnp.exp(-length * a_t)
        carried = carried + decay * shifted(sent, "context", 2).astype(F32)
        distance = 2
    while distance < lax.axis_size("context"):
        decay = jnp.exp(-(length * distance) * a_t)
        carried = carried + decay * shifted(carried.astype(BF16), "context", distance).astype(F32)
        distance *= 2

    return output_call(after_medium, vt, gate_long, lam, w, carried)


def solution(mesh):
    return jax.shard_map(
        on_device,
        mesh=mesh,
        in_specs=(
            P("tensor", ("groups", "context")),
            P("tensor", ("groups", "context")),
            P("tensor", ("groups", "context")),
            P("tensor", ("groups", "context")),
            P("tensor", ("groups", "context")),
            P("tensor", None),
            P("tensor", None),
            P("tensor", None),
            P("tensor"),
        ),
        out_specs=P("tensor", ("groups", "context")),
        check_vma=False,
    )
```

```python
import functools

import jax
import jax.numpy as jnp
from jax import lax
from jax.experimental import pallas as pl
from jax.experimental.pallas import tpu as pltpu
from jax.sharding import PartitionSpec as P

F32 = jnp.float32
BF16 = jnp.bfloat16
EPS = 1e-05
SUB, LANE = 8, 128
TILE = SUB * LANE


def shifted(block, axis, distance):
    devices = range(lax.axis_size(axis))
    route = [(i - distance, i) for i in devices if i - distance in devices]
    return lax.ppermute(block, axis, route)


def medium_kernel(x_ref, gm_ref, km_ref, rim_ref, taps_ref, am_ref, ss_ref):
    rows, length = x_ref.shape
    groups = taps_ref.shape[0]
    per_group = rows // groups
    row = lax.broadcasted_iota(jnp.int32, (length, length), 0)
    col = lax.broadcasted_iota(jnp.int32, (length, length), 1)
    upper = col >= row

    @pl.when(pl.program_id(0) == 0)
    def _():
        ss_ref[...] = jnp.zeros_like(ss_ref)

    acc = jnp.zeros((1, length), F32)
    for g in range(groups):
        lo, hi = g * per_group, (g + 1) * per_group
        taps = jnp.broadcast_to(taps_ref[g : g + 1, :].astype(F32), (length, length))
        rolled = pltpu.roll(taps, 0, 1, stride=1, stride_axis=0)
        t_cur = jnp.where(upper, rolled, 0.0).astype(BF16)
        t_rim = jnp.where(upper, 0.0, rolled).astype(BF16)
        x = x_ref[lo:hi, :].astype(F32)
        vm = (km_ref[lo:hi, :].astype(F32) * x).astype(BF16)
        ext = jnp.concatenate([rim_ref[lo:hi, :], vm], axis=1)
        conv = jnp.dot(ext, jnp.concatenate([t_rim, t_cur], axis=0), preferred_element_type=F32)
        am = x + gm_ref[lo:hi, :].astype(F32) * conv
        am_ref[lo:hi, :] = am
        acc = acc + jnp.sum(am * am, axis=0, keepdims=True)
    ss_ref[...] += acc


def medium_call(inputs, gate_medium, key_medium, rim, taps):
    channels, length = inputs.shape
    per_group = channels // taps.shape[0]
    block = 2048
    tap_block = block // per_group
    big = pl.BlockSpec((block, length), lambda b: (b, 0))
    return pl.pallas_call(
        medium_kernel,
        grid=(channels // block,),
        in_specs=[big, big, big, big, pl.BlockSpec((tap_block, length), lambda b: (b, 0))],
        out_specs=[big, pl.BlockSpec((1, length), lambda b: (0, 0))],
        out_shape=[
            jax.ShapeDtypeStruct((channels, length), F32),
            jax.ShapeDtypeStruct((1, length), F32),
        ],
        compiler_params=pltpu.CompilerParams(dimension_semantics=("arbitrary",)),
    )(inputs, gate_medium, key_medium, rim, taps)


def load_values(am_ref, kl_ref, g_ref, r_ref, vt_ref):
    r = r_ref[...]
    for i in range(SUB):
        rows = slice(i * LANE, (i + 1) * LANE)
        gain = jnp.broadcast_to(g_ref[i : i + 1, :], (LANE, LANE)).T
        normed = am_ref[rows, :] * r * gain
        v = (kl_ref[rows, :].astype(F32) * normed).astype(BF16).astype(F32)
        vt_ref[pl.ds(i, LANE, stride=SUB), :] = v.T


def token_tile(ref, t):
    return ref[pl.ds(pl.multiple_of(t * SUB, SUB), SUB), :]


def final_state_kernel(am_ref, kl_ref, g_ref, r_ref, lam_ref, f_ref, vt_ref):
    modes = lam_ref.shape[0]
    length = am_ref.shape[1]
    load_values(am_ref, kl_ref, g_ref, r_ref, vt_ref)
    lam = [lam_ref[m] for m in range(modes)]

    def body(t, h):
        v = token_tile(vt_ref, t)
        return tuple(lam[m] * h[m] + v for m in range(modes))

    h = lax.fori_loop(0, length, body, tuple(jnp.zeros((SUB, LANE), F32) for _ in range(modes)), unroll=8)
    for m in range(modes):
        f_ref[m] = h[m].astype(f_ref.dtype)


def output_kernel(am_ref, vt_ref, gl_ref, lam_ref, w_ref, h0_ref, out_ref, yt_ref):
    modes = lam_ref.shape[0]
    length = am_ref.shape[1]
    lam = [lam_ref[m] for m in range(modes)]
    w = [w_ref[m] for m in range(modes)]

    def body(t, h):
        v = token_tile(vt_ref, t)
        h = tuple(lam[m] * h[m] + v for m in range(modes))
        y = w[0] * h[0]
        for m in range(1, modes):
            y = y + w[m] * h[m]
        yt_ref[pl.ds(pl.multiple_of(t * SUB, SUB), SUB), :] = y
        return h

    lax.fori_loop(0, length, body, tuple(h0_ref[m] for m in range(modes)), unroll=8)
    for i in range(SUB):
        rows = slice(i * LANE, (i + 1) * LANE)
        long_out = yt_ref[pl.ds(i, LANE, stride=SUB), :].T.astype(BF16).astype(F32)
        out_ref[rows, :] = (am_ref[rows, :] + gl_ref[rows, :].astype(F32) * long_out).astype(BF16)


def tiled_spec(lead):
    return pl.BlockSpec((lead, None, SUB, LANE), lambda b: (0, b, 0, 0))


def final_state_call(am, kl, gain, r, lam):
    channels, length = am.shape
    modes = lam.shape[0]
    big = pl.BlockSpec((TILE, length), lambda b: (b, 0))
    return pl.pallas_call(
        final_state_kernel,
        grid=(channels // TILE,),
        in_specs=[big, big, pl.BlockSpec((SUB, LANE), lambda b: (b, 0)), pl.BlockSpec((1, length), lambda b: (0, 0)), tiled_spec(modes)],
        out_specs=[tiled_spec(modes), pl.BlockSpec((length * SUB, LANE), lambda b: (b, 0))],
        out_shape=[
            jax.ShapeDtypeStruct(lam.shape, BF16),
            jax.ShapeDtypeStruct((channels // TILE * length * SUB, LANE), F32),
        ],
    )(am, kl, gain, r, lam)


def output_call(am, vt, gl, lam, w, h0):
    channels, length = am.shape
    modes = lam.shape[0]
    big = pl.BlockSpec((TILE, length), lambda b: (b, 0))
    return pl.pallas_call(
        output_kernel,
        grid=(channels // TILE,),
        in_specs=[big, pl.BlockSpec((length * SUB, LANE), lambda b: (b, 0)), big, tiled_spec(modes), tiled_spec(modes), tiled_spec(modes)],
        out_specs=big,
        out_shape=jax.ShapeDtypeStruct((channels, length), BF16),
        scratch_shapes=[pltpu.VMEM((length * SUB, LANE), F32)],
    )(am, vt, gl, lam, w, h0)


def to_tiles(a):
    channels, k = a.shape
    return a.T.reshape(k, channels // TILE, SUB, LANE)


def on_device(
    inputs,
    gate_medium,
    key_medium,
    gate_long,
    key_long,
    medium_taps,
    log_decay,
    residues,
    norm_gain,
):
    channels, length = inputs.shape
    assert length == medium_taps.shape[1]
    width = channels * lax.axis_size("tensor")
    source = inputs.astype(F32)
    values_medium = (key_medium.astype(F32) * source).astype(BF16)
    rim = shifted(values_medium, "context", 1)
    gain = norm_gain.reshape(channels // LANE, LANE)
    a_t = to_tiles(log_decay)
    lam = jnp.exp(-a_t)
    w = to_tiles(residues * jnp.sqrt(2.0 * log_decay))
    rim, a_t, lam, w = lax.optimization_barrier((rim, a_t, lam, w))
    after_medium, partial = medium_call(inputs, gate_medium, key_medium, rim, medium_taps)
    if lax.axis_size("tensor") == 2:
        totals = partial + lax.ppermute(partial, "tensor", [(0, 1), (1, 0)])
    else:
        totals = lax.psum(partial, "tensor")
    r = lax.rsqrt(totals / width + EPS)
    finals, vt = final_state_call(after_medium, key_long, gain, r, lam)

    sent = finals
    carried = shifted(sent, "context", 1).astype(F32)
    distance = 1
    if lax.axis_size("context") > 2:
        decay = jnp.exp(-length * a_t)
        carried = carried + decay * shifted(sent, "context", 2).astype(F32)
        distance = 2
    while distance < lax.axis_size("context"):
        decay = jnp.exp(-(length * distance) * a_t)
        carried = carried + decay * shifted(carried.astype(BF16), "context", distance).astype(F32)
        distance *= 2

    return output_call(after_medium, vt, gate_long, lam, w, carried)


def solution(mesh):
    return jax.shard_map(
        on_device,
        mesh=mesh,
        in_specs=(
            P("tensor", ("groups", "context")),
            P("tensor", ("groups", "context")),
            P("tensor", ("groups", "context")),
            P("tensor", ("groups", "context")),
            P("tensor", ("groups", "context")),
            P("tensor", None),
            P("tensor", None),
            P("tensor", None),
            P("tensor"),
        ),
        out_specs=P("tensor", ("groups", "context")),
        check_vma=False,
    )
```

```python
import functools

import jax
import jax.numpy as jnp
from jax import lax
from jax.experimental import pallas as pl
from jax.experimental.pallas import tpu as pltpu
from jax.sharding import PartitionSpec as P

F32 = jnp.float32
BF16 = jnp.bfloat16
EPS = 1e-05
SUB, LANE = 8, 128
TILE = SUB * LANE


def shifted(block, axis, distance):
    devices = range(lax.axis_size(axis))
    route = [(i - distance, i) for i in devices if i - distance in devices]
    return lax.ppermute(block, axis, route)


def medium_kernel(x_ref, gm_ref, km_ref, rim_ref, taps_ref, am_ref, ss_ref):
    rows, length = x_ref.shape
    groups = taps_ref.shape[0]
    per_group = rows // groups
    row = lax.broadcasted_iota(jnp.int32, (length, length), 0)
    col = lax.broadcasted_iota(jnp.int32, (length, length), 1)
    upper = col >= row

    @pl.when(pl.program_id(0) == 0)
    def _():
        ss_ref[...] = jnp.zeros_like(ss_ref)

    acc = jnp.zeros((1, length), F32)
    for g in range(groups):
        lo, hi = g * per_group, (g + 1) * per_group
        taps = jnp.broadcast_to(taps_ref[g : g + 1, :].astype(F32), (length, length))
        rolled = pltpu.roll(taps, 0, 1, stride=1, stride_axis=0)
        t_cur = jnp.where(upper, rolled, 0.0).astype(BF16)
        t_rim = jnp.where(upper, 0.0, rolled).astype(BF16)
        x = x_ref[lo:hi, :].astype(F32)
        vm = (km_ref[lo:hi, :].astype(F32) * x).astype(BF16)
        ext = jnp.concatenate([rim_ref[lo:hi, :], vm], axis=1)
        conv = jnp.dot(ext, jnp.concatenate([t_rim, t_cur], axis=0), preferred_element_type=F32)
        am = x + gm_ref[lo:hi, :].astype(F32) * conv
        am_ref[lo:hi, :] = am
        acc = acc + jnp.sum(am * am, axis=0, keepdims=True)
    ss_ref[...] += acc


def medium_call(inputs, gate_medium, key_medium, rim, taps):
    channels, length = inputs.shape
    per_group = channels // taps.shape[0]
    block = 2048
    tap_block = block // per_group
    big = pl.BlockSpec((block, length), lambda b: (b, 0))
    return pl.pallas_call(
        medium_kernel,
        grid=(channels // block,),
        in_specs=[big, big, big, big, pl.BlockSpec((tap_block, length), lambda b: (b, 0))],
        out_specs=[big, pl.BlockSpec((1, length), lambda b: (0, 0))],
        out_shape=[
            jax.ShapeDtypeStruct((channels, length), F32),
            jax.ShapeDtypeStruct((1, length), F32),
        ],
        compiler_params=pltpu.CompilerParams(dimension_semantics=("arbitrary",)),
    )(inputs, gate_medium, key_medium, rim, taps)


def load_values(am_ref, kl_ref, g_ref, p_ref, q_ref, vt_ref, width):
    r = lax.rsqrt((p_ref[...] + q_ref[...]) / width + EPS)
    for i in range(SUB):
        rows = slice(i * LANE, (i + 1) * LANE)
        gain = jnp.broadcast_to(g_ref[i : i + 1, :], (LANE, LANE)).T
        normed = am_ref[rows, :] * r * gain
        v = (kl_ref[rows, :].astype(F32) * normed).astype(BF16).astype(F32)
        vt_ref[pl.ds(i, LANE, stride=SUB), :] = v.T


def token_tile(ref, t):
    return ref[pl.ds(pl.multiple_of(t * SUB, SUB), SUB), :]


def final_state_kernel(width, am_ref, kl_ref, g_ref, p_ref, q_ref, lam_ref, f_ref, vt_ref):
    modes = lam_ref.shape[0]
    length = am_ref.shape[1]
    load_values(am_ref, kl_ref, g_ref, p_ref, q_ref, vt_ref, width)
    lam = [lam_ref[m] for m in range(modes)]

    def body(t, h):
        v = token_tile(vt_ref, t)
        return tuple(lam[m] * h[m] + v for m in range(modes))

    h = lax.fori_loop(0, length, body, tuple(jnp.zeros((SUB, LANE), F32) for _ in range(modes)), unroll=8)
    for m in range(modes):
        f_ref[m] = h[m].astype(f_ref.dtype)


def output_kernel(am_ref, vt_ref, gl_ref, lam_ref, w_ref, h0_ref, out_ref, yt_ref):
    modes = lam_ref.shape[0]
    length = am_ref.shape[1]
    lam = [lam_ref[m] for m in range(modes)]
    w = [w_ref[m] for m in range(modes)]

    def body(t, h):
        v = token_tile(vt_ref, t)
        h = tuple(lam[m] * h[m] + v for m in range(modes))
        y = w[0] * h[0]
        for m in range(1, modes):
            y = y + w[m] * h[m]
        yt_ref[pl.ds(pl.multiple_of(t * SUB, SUB), SUB), :] = y
        return h

    lax.fori_loop(0, length, body, tuple(h0_ref[m] for m in range(modes)), unroll=8)
    for i in range(SUB):
        rows = slice(i * LANE, (i + 1) * LANE)
        long_out = yt_ref[pl.ds(i, LANE, stride=SUB), :].T.astype(BF16).astype(F32)
        out_ref[rows, :] = (am_ref[rows, :] + gl_ref[rows, :].astype(F32) * long_out).astype(BF16)


def tiled_spec(lead):
    return pl.BlockSpec((lead, None, SUB, LANE), lambda b: (0, b, 0, 0))


def final_state_call(am, kl, gain, mine, other, lam, width):
    channels, length = am.shape
    modes = lam.shape[0]
    big = pl.BlockSpec((TILE, length), lambda b: (b, 0))
    row = pl.BlockSpec((1, length), lambda b: (0, 0))
    return pl.pallas_call(
        functools.partial(final_state_kernel, float(width)),
        grid=(channels // TILE,),
        in_specs=[big, big, pl.BlockSpec((SUB, LANE), lambda b: (b, 0)), row, row, tiled_spec(modes)],
        out_specs=[tiled_spec(modes), pl.BlockSpec((length * SUB, LANE), lambda b: (b, 0))],
        out_shape=[
            jax.ShapeDtypeStruct(lam.shape, BF16),
            jax.ShapeDtypeStruct((channels // TILE * length * SUB, LANE), F32),
        ],
    )(am, kl, gain, mine, other, lam)


def output_call(am, vt, gl, lam, w, h0):
    channels, length = am.shape
    modes = lam.shape[0]
    big = pl.BlockSpec((TILE, length), lambda b: (b, 0))
    return pl.pallas_call(
        output_kernel,
        grid=(channels // TILE,),
        in_specs=[big, pl.BlockSpec((length * SUB, LANE), lambda b: (b, 0)), big, tiled_spec(modes), tiled_spec(modes), tiled_spec(modes)],
        out_specs=big,
        out_shape=jax.ShapeDtypeStruct((channels, length), BF16),
        scratch_shapes=[pltpu.VMEM((length * SUB, LANE), F32)],
    )(am, vt, gl, lam, w, h0)


def to_tiles(a):
    channels, k = a.shape
    return a.T.reshape(k, channels // TILE, SUB, LANE)


def on_device(
    inputs,
    gate_medium,
    key_medium,
    gate_long,
    key_long,
    medium_taps,
    log_decay,
    residues,
    norm_gain,
):
    channels, length = inputs.shape
    assert length == medium_taps.shape[1]
    width = channels * lax.axis_size("tensor")
    source = inputs.astype(F32)
    values_medium = (key_medium.astype(F32) * source).astype(BF16)
    rim = shifted(values_medium, "context", 1)
    gain = norm_gain.reshape(channels // LANE, LANE)
    a_t = to_tiles(log_decay)
    lam = jnp.exp(-a_t)
    w = to_tiles(residues * jnp.sqrt(2.0 * log_decay))
    rim, a_t, lam, w = lax.optimization_barrier((rim, a_t, lam, w))
    after_medium, partial = medium_call(inputs, gate_medium, key_medium, rim, medium_taps)
    if lax.axis_size("tensor") == 2:
        other = lax.ppermute(partial, "tensor", [(0, 1), (1, 0)])
    else:
        partial, other = lax.psum(partial, "tensor"), jnp.zeros_like(partial)
    finals, vt = final_state_call(after_medium, key_long, gain, partial, other, lam, width)

    sent = finals
    carried = shifted(sent, "context", 1).astype(F32)
    distance = 1
    if lax.axis_size("context") > 2:
        decay = jnp.exp(-length * a_t)
        carried = carried + decay * shifted(sent, "context", 2).astype(F32)
        distance = 2
    while distance < lax.axis_size("context"):
        decay = jnp.exp(-(length * distance) * a_t)
        carried = carried + decay * shifted(carried.astype(BF16), "context", distance).astype(F32)
        distance *= 2

    return output_call(after_medium, vt, gate_long, lam, w, carried)


def solution(mesh):
    return jax.shard_map(
        on_device,
        mesh=mesh,
        in_specs=(
            P("tensor", ("groups", "context")),
            P("tensor", ("groups", "context")),
            P("tensor", ("groups", "context")),
            P("tensor", ("groups", "context")),
            P("tensor", ("groups", "context")),
            P("tensor", None),
            P("tensor", None),
            P("tensor", None),
            P("tensor"),
        ),
        out_specs=P("tensor", ("groups", "context")),
        check_vma=False,
    )
```

```python
import functools

import jax
import jax.numpy as jnp
from jax import lax
from jax.experimental import pallas as pl
from jax.experimental.pallas import tpu as pltpu
from jax.sharding import PartitionSpec as P

F32 = jnp.float32
BF16 = jnp.bfloat16
EPS = 1e-05
SUB, LANE = 8, 128
TILE = SUB * LANE


def shifted(block, axis, distance):
    devices = range(lax.axis_size(axis))
    route = [(i - distance, i) for i in devices if i - distance in devices]
    return lax.ppermute(block, axis, route)


def medium_kernel(x_ref, gm_ref, km_ref, rim_ref, taps_ref, am_ref, ss_ref):
    rows, length = x_ref.shape
    groups = taps_ref.shape[0]
    per_group = rows // groups
    row = lax.broadcasted_iota(jnp.int32, (length, length), 0)
    col = lax.broadcasted_iota(jnp.int32, (length, length), 1)
    upper = col >= row

    @pl.when(pl.program_id(0) == 0)
    def _():
        ss_ref[...] = jnp.zeros_like(ss_ref)

    acc = jnp.zeros((1, length), F32)
    for g in range(groups):
        lo, hi = g * per_group, (g + 1) * per_group
        taps = jnp.broadcast_to(taps_ref[g : g + 1, :].astype(F32), (length, length))
        rolled = pltpu.roll(taps, 0, 1, stride=1, stride_axis=0)
        t_cur = jnp.where(upper, rolled, 0.0).astype(BF16)
        t_rim = jnp.where(upper, 0.0, rolled).astype(BF16)
        x = x_ref[lo:hi, :].astype(F32)
        vm = (km_ref[lo:hi, :].astype(F32) * x).astype(BF16)
        ext = jnp.concatenate([rim_ref[lo:hi, :], vm], axis=1)
        conv = jnp.dot(ext, jnp.concatenate([t_rim, t_cur], axis=0), preferred_element_type=F32)
        am = x + gm_ref[lo:hi, :].astype(F32) * conv
        am_ref[lo:hi, :] = am
        acc = acc + jnp.sum(am * am, axis=0, keepdims=True)
    ss_ref[...] += acc


def medium_call(inputs, gate_medium, key_medium, rim, taps):
    channels, length = inputs.shape
    per_group = channels // taps.shape[0]
    block = 2048
    tap_block = block // per_group
    big = pl.BlockSpec((block, length), lambda b: (b, 0))
    return pl.pallas_call(
        medium_kernel,
        grid=(channels // block,),
        in_specs=[big, big, big, big, pl.BlockSpec((tap_block, length), lambda b: (b, 0))],
        out_specs=[big, pl.BlockSpec((1, length), lambda b: (0, 0))],
        out_shape=[
            jax.ShapeDtypeStruct((channels, length), F32),
            jax.ShapeDtypeStruct((1, length), F32),
        ],
        compiler_params=pltpu.CompilerParams(dimension_semantics=("arbitrary",)),
    )(inputs, gate_medium, key_medium, rim, taps)


def load_values(am_ref, kl_ref, g_ref, p_ref, q_ref, vt_ref, width):
    r = lax.rsqrt((p_ref[...] + q_ref[...]) / width + EPS)
    columns = g_ref[...].T
    for i in range(SUB):
        rows = slice(i * LANE, (i + 1) * LANE)
        gain = jnp.broadcast_to(columns[:, i : i + 1], (LANE, LANE))
        normed = am_ref[rows, :] * r * gain
        v = (kl_ref[rows, :].astype(F32) * normed).astype(BF16).astype(F32)
        vt_ref[pl.ds(i, LANE, stride=SUB), :] = v.T


def token_tile(ref, t):
    return ref[pl.ds(pl.multiple_of(t * SUB, SUB), SUB), :]


def final_state_kernel(width, am_ref, kl_ref, g_ref, p_ref, q_ref, lam_ref, f_ref, vt_ref):
    modes = lam_ref.shape[0]
    length = am_ref.shape[1]
    load_values(am_ref, kl_ref, g_ref, p_ref, q_ref, vt_ref, width)
    lam = [lam_ref[m] for m in range(modes)]

    def body(t, h):
        v = token_tile(vt_ref, t)
        return tuple(lam[m] * h[m] + v for m in range(modes))

    h = lax.fori_loop(0, length, body, tuple(jnp.zeros((SUB, LANE), F32) for _ in range(modes)), unroll=8)
    for m in range(modes):
        f_ref[m] = h[m].astype(f_ref.dtype)


def output_kernel(am_ref, vt_ref, gl_ref, lam_ref, w_ref, h0_ref, out_ref, yt_ref):
    modes = lam_ref.shape[0]
    length = am_ref.shape[1]
    lam = [lam_ref[m] for m in range(modes)]
    w = [w_ref[m] for m in range(modes)]

    def body(t, h):
        v = token_tile(vt_ref, t)
        h = tuple(lam[m] * h[m] + v for m in range(modes))
        y = w[0] * h[0]
        for m in range(1, modes):
            y = y + w[m] * h[m]
        yt_ref[pl.ds(pl.multiple_of(t * SUB, SUB), SUB), :] = y
        return h

    lax.fori_loop(0, length, body, tuple(h0_ref[m] for m in range(modes)), unroll=8)
    for i in range(SUB):
        rows = slice(i * LANE, (i + 1) * LANE)
        long_out = yt_ref[pl.ds(i, LANE, stride=SUB), :].T.astype(BF16).astype(F32)
        out_ref[rows, :] = (am_ref[rows, :] + gl_ref[rows, :].astype(F32) * long_out).astype(BF16)


def tiled_spec(lead):
    return pl.BlockSpec((lead, None, SUB, LANE), lambda b: (0, b, 0, 0))


def final_state_call(am, kl, gain, mine, other, lam, width):
    channels, length = am.shape
    modes = lam.shape[0]
    big = pl.BlockSpec((TILE, length), lambda b: (b, 0))
    row = pl.BlockSpec((1, length), lambda b: (0, 0))
    return pl.pallas_call(
        functools.partial(final_state_kernel, float(width)),
        grid=(channels // TILE,),
        in_specs=[big, big, pl.BlockSpec((SUB, LANE), lambda b: (b, 0)), row, row, tiled_spec(modes)],
        out_specs=[tiled_spec(modes), pl.BlockSpec((length * SUB, LANE), lambda b: (b, 0))],
        out_shape=[
            jax.ShapeDtypeStruct(lam.shape, BF16),
            jax.ShapeDtypeStruct((channels // TILE * length * SUB, LANE), F32),
        ],
    )(am, kl, gain, mine, other, lam)


def output_call(am, vt, gl, lam, w, h0):
    channels, length = am.shape
    modes = lam.shape[0]
    big = pl.BlockSpec((TILE, length), lambda b: (b, 0))
    return pl.pallas_call(
        output_kernel,
        grid=(channels // TILE,),
        in_specs=[big, pl.BlockSpec((length * SUB, LANE), lambda b: (b, 0)), big, tiled_spec(modes), tiled_spec(modes), tiled_spec(modes)],
        out_specs=big,
        out_shape=jax.ShapeDtypeStruct((channels, length), BF16),
        scratch_shapes=[pltpu.VMEM((length * SUB, LANE), F32)],
    )(am, vt, gl, lam, w, h0)


def to_tiles(a):
    channels, k = a.shape
    return a.T.reshape(k, channels // TILE, SUB, LANE)


def on_device(
    inputs,
    gate_medium,
    key_medium,
    gate_long,
    key_long,
    medium_taps,
    log_decay,
    residues,
    norm_gain,
):
    channels, length = inputs.shape
    assert length == medium_taps.shape[1]
    width = channels * lax.axis_size("tensor")
    source = inputs.astype(F32)
    values_medium = (key_medium.astype(F32) * source).astype(BF16)
    rim = shifted(values_medium, "context", 1)
    gain = norm_gain.reshape(channels // LANE, LANE)
    a_t = to_tiles(log_decay)
    lam = jnp.exp(-a_t)
    w = to_tiles(residues * jnp.sqrt(2.0 * log_decay))
    rim, a_t, lam, w = lax.optimization_barrier((rim, a_t, lam, w))
    after_medium, partial = medium_call(inputs, gate_medium, key_medium, rim, medium_taps)
    if lax.axis_size("tensor") == 2:
        other = lax.ppermute(partial, "tensor", [(0, 1), (1, 0)])
    else:
        partial, other = lax.psum(partial, "tensor"), jnp.zeros_like(partial)
    finals, vt = final_state_call(after_medium, key_long, gain, partial, other, lam, width)

    sent = finals
    carried = shifted(sent, "context", 1).astype(F32)
    distance = 1
    if lax.axis_size("context") > 2:
        decay = jnp.exp(-length * a_t)
        carried = carried + decay * shifted(sent, "context", 2).astype(F32)
        distance = 2
    while distance < lax.axis_size("context"):
        decay = jnp.exp(-(length * distance) * a_t)
        carried = carried + decay * shifted(carried.astype(BF16), "context", distance).astype(F32)
        distance *= 2

    return output_call(after_medium, vt, gate_long, lam, w, carried)


def solution(mesh):
    return jax.shard_map(
        on_device,
        mesh=mesh,
        in_specs=(
            P("tensor", ("groups", "context")),
            P("tensor", ("groups", "context")),
            P("tensor", ("groups", "context")),
            P("tensor", ("groups", "context")),
            P("tensor", ("groups", "context")),
            P("tensor", None),
            P("tensor", None),
            P("tensor", None),
            P("tensor"),
        ),
        out_specs=P("tensor", ("groups", "context")),
        check_vma=False,
    )
```

```python
import functools

import jax
import jax.numpy as jnp
from jax import lax
from jax.experimental import pallas as pl
from jax.experimental.pallas import tpu as pltpu
from jax.sharding import PartitionSpec as P

F32 = jnp.float32
BF16 = jnp.bfloat16
EPS = 1e-05
SUB, LANE = 8, 128
TILE = SUB * LANE


def shifted(block, axis, distance):
    devices = range(lax.axis_size(axis))
    route = [(i - distance, i) for i in devices if i - distance in devices]
    return lax.ppermute(block, axis, route)


def medium_kernel(x_ref, gm_ref, km_ref, rim_ref, taps_ref, am_ref, ss_ref):
    rows, length = x_ref.shape
    groups = taps_ref.shape[0]
    per_group = rows // groups
    row = lax.broadcasted_iota(jnp.int32, (length, length), 0)
    col = lax.broadcasted_iota(jnp.int32, (length, length), 1)
    upper = col >= row

    @pl.when(pl.program_id(0) == 0)
    def _():
        ss_ref[...] = jnp.zeros_like(ss_ref)

    acc = jnp.zeros((1, length), F32)
    for g in range(groups):
        lo, hi = g * per_group, (g + 1) * per_group
        taps = jnp.broadcast_to(taps_ref[g : g + 1, :].astype(F32), (length, length))
        rolled = pltpu.roll(taps, 0, 1, stride=1, stride_axis=0)
        t_cur = jnp.where(upper, rolled, 0.0).astype(BF16)
        t_rim = jnp.where(upper, 0.0, rolled).astype(BF16)
        x = x_ref[lo:hi, :].astype(F32)
        vm = (km_ref[lo:hi, :].astype(F32) * x).astype(BF16)
        ext = jnp.concatenate([rim_ref[lo:hi, :], vm], axis=1)
        conv = jnp.dot(ext, jnp.concatenate([t_rim, t_cur], axis=0), preferred_element_type=F32)
        am = x + gm_ref[lo:hi, :].astype(F32) * conv
        am_ref[lo:hi, :] = am
        acc = acc + jnp.sum(am * am, axis=0, keepdims=True)
    ss_ref[...] += acc


def medium_call(inputs, gate_medium, key_medium, rim, taps):
    channels, length = inputs.shape
    per_group = channels // taps.shape[0]
    block = 4096
    tap_block = block // per_group
    big = pl.BlockSpec((block, length), lambda b: (b, 0))
    return pl.pallas_call(
        medium_kernel,
        grid=(channels // block,),
        in_specs=[big, big, big, big, pl.BlockSpec((tap_block, length), lambda b: (b, 0))],
        out_specs=[big, pl.BlockSpec((1, length), lambda b: (0, 0))],
        out_shape=[
            jax.ShapeDtypeStruct((channels, length), F32),
            jax.ShapeDtypeStruct((1, length), F32),
        ],
        compiler_params=pltpu.CompilerParams(dimension_semantics=("arbitrary",)),
    )(inputs, gate_medium, key_medium, rim, taps)


def load_values(am_ref, kl_ref, g_ref, p_ref, q_ref, vt_ref, width):
    r = lax.rsqrt((p_ref[...] + q_ref[...]) / width + EPS)
    for i in range(SUB):
        rows = slice(i * LANE, (i + 1) * LANE)
        gain = jnp.broadcast_to(g_ref[i : i + 1, :], (LANE, LANE)).T
        normed = am_ref[rows, :] * r * gain
        v = (kl_ref[rows, :].astype(F32) * normed).astype(BF16).astype(F32)
        vt_ref[pl.ds(i, LANE, stride=SUB), :] = v.T


def token_tile(ref, t):
    return ref[pl.ds(pl.multiple_of(t * SUB, SUB), SUB), :]


def final_state_kernel(width, am_ref, kl_ref, g_ref, p_ref, q_ref, lam_ref, f_ref, vt_ref):
    modes = lam_ref.shape[0]
    length = am_ref.shape[1]
    load_values(am_ref, kl_ref, g_ref, p_ref, q_ref, vt_ref, width)
    lam = [lam_ref[m] for m in range(modes)]

    def body(t, h):
        v = token_tile(vt_ref, t)
        return tuple(lam[m] * h[m] + v for m in range(modes))

    h = lax.fori_loop(0, length, body, tuple(jnp.zeros((SUB, LANE), F32) for _ in range(modes)), unroll=8)
    for m in range(modes):
        f_ref[m] = h[m].astype(f_ref.dtype)


def output_kernel(am_ref, vt_ref, gl_ref, lam_ref, w_ref, h0_ref, out_ref, yt_ref):
    modes = lam_ref.shape[0]
    length = am_ref.shape[1]
    lam = [lam_ref[m] for m in range(modes)]
    w = [w_ref[m] for m in range(modes)]

    def body(t, h):
        v = token_tile(vt_ref, t)
        h = tuple(lam[m] * h[m] + v for m in range(modes))
        y = w[0] * h[0]
        for m in range(1, modes):
            y = y + w[m] * h[m]
        yt_ref[pl.ds(pl.multiple_of(t * SUB, SUB), SUB), :] = y
        return h

    lax.fori_loop(0, length, body, tuple(h0_ref[m] for m in range(modes)), unroll=8)
    for i in range(SUB):
        rows = slice(i * LANE, (i + 1) * LANE)
        long_out = yt_ref[pl.ds(i, LANE, stride=SUB), :].T.astype(BF16).astype(F32)
        out_ref[rows, :] = (am_ref[rows, :] + gl_ref[rows, :].astype(F32) * long_out).astype(BF16)


def tiled_spec(lead):
    return pl.BlockSpec((lead, None, SUB, LANE), lambda b: (0, b, 0, 0))


def final_state_call(am, kl, gain, mine, other, lam, width):
    channels, length = am.shape
    modes = lam.shape[0]
    big = pl.BlockSpec((TILE, length), lambda b: (b, 0))
    row = pl.BlockSpec((1, length), lambda b: (0, 0))
    return pl.pallas_call(
        functools.partial(final_state_kernel, float(width)),
        grid=(channels // TILE,),
        in_specs=[big, big, pl.BlockSpec((SUB, LANE), lambda b: (b, 0)), row, row, tiled_spec(modes)],
        out_specs=[tiled_spec(modes), pl.BlockSpec((length * SUB, LANE), lambda b: (b, 0))],
        out_shape=[
            jax.ShapeDtypeStruct(lam.shape, BF16),
            jax.ShapeDtypeStruct((channels // TILE * length * SUB, LANE), F32),
        ],
    )(am, kl, gain, mine, other, lam)


def output_call(am, vt, gl, lam, w, h0):
    channels, length = am.shape
    modes = lam.shape[0]
    big = pl.BlockSpec((TILE, length), lambda b: (b, 0))
    return pl.pallas_call(
        output_kernel,
        grid=(channels // TILE,),
        in_specs=[big, pl.BlockSpec((length * SUB, LANE), lambda b: (b, 0)), big, tiled_spec(modes), tiled_spec(modes), tiled_spec(modes)],
        out_specs=big,
        out_shape=jax.ShapeDtypeStruct((channels, length), BF16),
        scratch_shapes=[pltpu.VMEM((length * SUB, LANE), F32)],
    )(am, vt, gl, lam, w, h0)


def to_tiles(a):
    channels, k = a.shape
    return a.T.reshape(k, channels // TILE, SUB, LANE)


def on_device(
    inputs,
    gate_medium,
    key_medium,
    gate_long,
    key_long,
    medium_taps,
    log_decay,
    residues,
    norm_gain,
):
    channels, length = inputs.shape
    assert length == medium_taps.shape[1]
    width = channels * lax.axis_size("tensor")
    source = inputs.astype(F32)
    values_medium = (key_medium.astype(F32) * source).astype(BF16)
    rim = shifted(values_medium, "context", 1)
    gain = norm_gain.reshape(channels // LANE, LANE)
    a_t = to_tiles(log_decay)
    lam = jnp.exp(-a_t)
    w = to_tiles(residues * jnp.sqrt(2.0 * log_decay))
    rim, a_t, lam, w = lax.optimization_barrier((rim, a_t, lam, w))
    after_medium, partial = medium_call(inputs, gate_medium, key_medium, rim, medium_taps)
    if lax.axis_size("tensor") == 2:
        other = lax.ppermute(partial, "tensor", [(0, 1), (1, 0)])
    else:
        partial, other = lax.psum(partial, "tensor"), jnp.zeros_like(partial)
    finals, vt = final_state_call(after_medium, key_long, gain, partial, other, lam, width)

    sent = finals
    carried = shifted(sent, "context", 1).astype(F32)
    distance = 1
    if lax.axis_size("context") > 2:
        decay = jnp.exp(-length * a_t)
        carried = carried + decay * shifted(sent, "context", 2).astype(F32)
        distance = 2
    while distance < lax.axis_size("context"):
        decay = jnp.exp(-(length * distance) * a_t)
        carried = carried + decay * shifted(carried.astype(BF16), "context", distance).astype(F32)
        distance *= 2

    return output_call(after_medium, vt, gate_long, lam, w, carried)


def solution(mesh):
    return jax.shard_map(
        on_device,
        mesh=mesh,
        in_specs=(
            P("tensor", ("groups", "context")),
            P("tensor", ("groups", "context")),
            P("tensor", ("groups", "context")),
            P("tensor", ("groups", "context")),
            P("tensor", ("groups", "context")),
            P("tensor", None),
            P("tensor", None),
            P("tensor", None),
            P("tensor"),
        ),
        out_specs=P("tensor", ("groups", "context")),
        check_vma=False,
    )
```

```python
import functools

import jax
import jax.numpy as jnp
from jax import lax
from jax.experimental import pallas as pl
from jax.experimental.pallas import tpu as pltpu
from jax.sharding import PartitionSpec as P

F32 = jnp.float32
BF16 = jnp.bfloat16
EPS = 1e-05
SUB, LANE = 8, 128
TILE = SUB * LANE


def shifted(block, axis, distance):
    devices = range(lax.axis_size(axis))
    route = [(i - distance, i) for i in devices if i - distance in devices]
    return lax.ppermute(block, axis, route)


def medium_kernel(x_ref, gm_ref, km_ref, rim_ref, taps_ref, am_ref, ss_ref):
    rows, length = x_ref.shape
    groups = taps_ref.shape[0]
    per_group = rows // groups
    row = lax.broadcasted_iota(jnp.int32, (length, length), 0)
    col = lax.broadcasted_iota(jnp.int32, (length, length), 1)
    upper = col >= row

    @pl.when(pl.program_id(0) == 0)
    def _():
        ss_ref[...] = jnp.zeros_like(ss_ref)

    acc = jnp.zeros((1, length), F32)
    for g in range(groups):
        lo, hi = g * per_group, (g + 1) * per_group
        taps = jnp.broadcast_to(taps_ref[g : g + 1, :].astype(F32), (length, length))
        rolled = pltpu.roll(taps, 0, 1, stride=1, stride_axis=0)
        t_cur = jnp.where(upper, rolled, 0.0).astype(BF16)
        t_rim = jnp.where(upper, 0.0, rolled).astype(BF16)
        x = x_ref[lo:hi, :].astype(F32)
        vm = (km_ref[lo:hi, :].astype(F32) * x).astype(BF16)
        ext = jnp.concatenate([rim_ref[lo:hi, :], vm], axis=1)
        conv = jnp.dot(ext, jnp.concatenate([t_rim, t_cur], axis=0), preferred_element_type=F32)
        am = x + gm_ref[lo:hi, :].astype(F32) * conv
        am_ref[lo:hi, :] = am
        acc = acc + jnp.sum(am * am, axis=0, keepdims=True)
    ss_ref[...] += acc


def medium_call(inputs, gate_medium, key_medium, rim, taps):
    channels, length = inputs.shape
    per_group = channels // taps.shape[0]
    block = 2048
    tap_block = block // per_group
    big = pl.BlockSpec((block, length), lambda b: (b, 0))
    return pl.pallas_call(
        medium_kernel,
        grid=(channels // block,),
        in_specs=[big, big, big, big, pl.BlockSpec((tap_block, length), lambda b: (b, 0))],
        out_specs=[big, pl.BlockSpec((1, length), lambda b: (0, 0))],
        out_shape=[
            jax.ShapeDtypeStruct((channels, length), F32),
            jax.ShapeDtypeStruct((1, length), F32),
        ],
        compiler_params=pltpu.CompilerParams(dimension_semantics=("arbitrary",)),
    )(inputs, gate_medium, key_medium, rim, taps)


def load_values(am_ref, kl_ref, g_ref, p_ref, q_ref, vt_ref, width):
    r = lax.rsqrt((p_ref[...] + q_ref[...]) / width + EPS)
    for i in range(SUB):
        rows = slice(i * LANE, (i + 1) * LANE)
        gain = jnp.broadcast_to(g_ref[i : i + 1, :], (LANE, LANE)).T
        normed = am_ref[rows, :] * r * gain
        v = (kl_ref[rows, :].astype(F32) * normed).astype(BF16).astype(F32)
        vt_ref[pl.ds(i, LANE, stride=SUB), :] = v.T


def token_tile(ref, t):
    return ref[pl.ds(pl.multiple_of(t * SUB, SUB), SUB), :]


def final_state_kernel(width, am_ref, kl_ref, g_ref, p_ref, q_ref, lam_ref, f_ref, vt_ref):
    modes = lam_ref.shape[0]
    length = am_ref.shape[1]
    load_values(am_ref, kl_ref, g_ref, p_ref, q_ref, vt_ref, width)
    lam = [lam_ref[m] for m in range(modes)]

    def body(t, h):
        v = token_tile(vt_ref, t)
        return tuple(lam[m] * h[m] + v for m in range(modes))

    h = lax.fori_loop(0, length, body, tuple(jnp.zeros((SUB, LANE), F32) for _ in range(modes)), unroll=16)
    for m in range(modes):
        f_ref[m] = h[m].astype(f_ref.dtype)


def output_kernel(am_ref, vt_ref, gl_ref, lam_ref, w_ref, h0_ref, out_ref, yt_ref):
    modes = lam_ref.shape[0]
    length = am_ref.shape[1]
    lam = [lam_ref[m] for m in range(modes)]
    w = [w_ref[m] for m in range(modes)]

    def body(t, h):
        v = token_tile(vt_ref, t)
        h = tuple(lam[m] * h[m] + v for m in range(modes))
        y = w[0] * h[0]
        for m in range(1, modes):
            y = y + w[m] * h[m]
        yt_ref[pl.ds(pl.multiple_of(t * SUB, SUB), SUB), :] = y
        return h

    lax.fori_loop(0, length, body, tuple(h0_ref[m] for m in range(modes)), unroll=16)
    for i in range(SUB):
        rows = slice(i * LANE, (i + 1) * LANE)
        long_out = yt_ref[pl.ds(i, LANE, stride=SUB), :].T.astype(BF16).astype(F32)
        out_ref[rows, :] = (am_ref[rows, :] + gl_ref[rows, :].astype(F32) * long_out).astype(BF16)


def tiled_spec(lead):
    return pl.BlockSpec((lead, None, SUB, LANE), lambda b: (0, b, 0, 0))


def final_state_call(am, kl, gain, mine, other, lam, width):
    channels, length = am.shape
    modes = lam.shape[0]
    big = pl.BlockSpec((TILE, length), lambda b: (b, 0))
    row = pl.BlockSpec((1, length), lambda b: (0, 0))
    return pl.pallas_call(
        functools.partial(final_state_kernel, float(width)),
        grid=(channels // TILE,),
        in_specs=[big, big, pl.BlockSpec((SUB, LANE), lambda b: (b, 0)), row, row, tiled_spec(modes)],
        out_specs=[tiled_spec(modes), pl.BlockSpec((length * SUB, LANE), lambda b: (b, 0))],
        out_shape=[
            jax.ShapeDtypeStruct(lam.shape, BF16),
            jax.ShapeDtypeStruct((channels // TILE * length * SUB, LANE), F32),
        ],
    )(am, kl, gain, mine, other, lam)


def output_call(am, vt, gl, lam, w, h0):
    channels, length = am.shape
    modes = lam.shape[0]
    big = pl.BlockSpec((TILE, length), lambda b: (b, 0))
    return pl.pallas_call(
        output_kernel,
        grid=(channels // TILE,),
        in_specs=[big, pl.BlockSpec((length * SUB, LANE), lambda b: (b, 0)), big, tiled_spec(modes), tiled_spec(modes), tiled_spec(modes)],
        out_specs=big,
        out_shape=jax.ShapeDtypeStruct((channels, length), BF16),
        scratch_shapes=[pltpu.VMEM((length * SUB, LANE), F32)],
    )(am, vt, gl, lam, w, h0)


def to_tiles(a):
    channels, k = a.shape
    return a.T.reshape(k, channels // TILE, SUB, LANE)


def on_device(
    inputs,
    gate_medium,
    key_medium,
    gate_long,
    key_long,
    medium_taps,
    log_decay,
    residues,
    norm_gain,
):
    channels, length = inputs.shape
    assert length == medium_taps.shape[1]
    width = channels * lax.axis_size("tensor")
    source = inputs.astype(F32)
    values_medium = (key_medium.astype(F32) * source).astype(BF16)
    rim = shifted(values_medium, "context", 1)
    gain = norm_gain.reshape(channels // LANE, LANE)
    a_t = to_tiles(log_decay)
    lam = jnp.exp(-a_t)
    w = to_tiles(residues * jnp.sqrt(2.0 * log_decay))
    rim, a_t, lam, w = lax.optimization_barrier((rim, a_t, lam, w))
    after_medium, partial = medium_call(inputs, gate_medium, key_medium, rim, medium_taps)
    if lax.axis_size("tensor") == 2:
        other = lax.ppermute(partial, "tensor", [(0, 1), (1, 0)])
    else:
        partial, other = lax.psum(partial, "tensor"), jnp.zeros_like(partial)
    finals, vt = final_state_call(after_medium, key_long, gain, partial, other, lam, width)

    sent = finals
    carried = shifted(sent, "context", 1).astype(F32)
    distance = 1
    if lax.axis_size("context") > 2:
        decay = jnp.exp(-length * a_t)
        carried = carried + decay * shifted(sent, "context", 2).astype(F32)
        distance = 2
    while distance < lax.axis_size("context"):
        decay = jnp.exp(-(length * distance) * a_t)
        carried = carried + decay * shifted(carried.astype(BF16), "context", distance).astype(F32)
        distance *= 2

    return output_call(after_medium, vt, gate_long, lam, w, carried)


def solution(mesh):
    return jax.shard_map(
        on_device,
        mesh=mesh,
        in_specs=(
            P("tensor", ("groups", "context")),
            P("tensor", ("groups", "context")),
            P("tensor", ("groups", "context")),
            P("tensor", ("groups", "context")),
            P("tensor", ("groups", "context")),
            P("tensor", None),
            P("tensor", None),
            P("tensor", None),
            P("tensor"),
        ),
        out_specs=P("tensor", ("groups", "context")),
        check_vma=False,
    )
```

```python
import functools

import jax
import jax.numpy as jnp
from jax import lax
from jax.experimental import pallas as pl
from jax.experimental.pallas import tpu as pltpu
from jax.sharding import PartitionSpec as P

F32 = jnp.float32
BF16 = jnp.bfloat16
EPS = 1e-05
SUB, LANE = 8, 128
TILE = SUB * LANE


def shifted(block, axis, distance):
    devices = range(lax.axis_size(axis))
    route = [(i - distance, i) for i in devices if i - distance in devices]
    return lax.ppermute(block, axis, route)


def medium_kernel(x_ref, gm_ref, km_ref, rim_ref, taps_ref, am_ref, ss_ref):
    rows, length = x_ref.shape
    groups = taps_ref.shape[0]
    per_group = rows // groups
    row = lax.broadcasted_iota(jnp.int32, (length, length), 0)
    col = lax.broadcasted_iota(jnp.int32, (length, length), 1)
    upper = col >= row

    @pl.when(pl.program_id(0) == 0)
    def _():
        ss_ref[...] = jnp.zeros_like(ss_ref)

    acc = jnp.zeros((1, length), F32)
    for g in range(groups):
        lo, hi = g * per_group, (g + 1) * per_group
        taps = jnp.broadcast_to(taps_ref[g : g + 1, :].astype(F32), (length, length))
        rolled = pltpu.roll(taps, 0, 1, stride=1, stride_axis=0)
        t_cur = jnp.where(upper, rolled, 0.0).astype(BF16)
        t_rim = jnp.where(upper, 0.0, rolled).astype(BF16)
        x = x_ref[lo:hi, :].astype(F32)
        vm = (km_ref[lo:hi, :].astype(F32) * x).astype(BF16)
        ext = jnp.concatenate([rim_ref[lo:hi, :], vm], axis=1)
        conv = jnp.dot(ext, jnp.concatenate([t_rim, t_cur], axis=0), preferred_element_type=F32)
        am = x + gm_ref[lo:hi, :].astype(F32) * conv
        am_ref[lo:hi, :] = am
        acc = acc + jnp.sum(am * am, axis=0, keepdims=True)
    ss_ref[...] += acc


def medium_call(inputs, gate_medium, key_medium, rim, taps):
    channels, length = inputs.shape
    per_group = channels // taps.shape[0]
    block = 2048
    tap_block = block // per_group
    big = pl.BlockSpec((block, length), lambda b: (b, 0))
    return pl.pallas_call(
        medium_kernel,
        grid=(channels // block,),
        in_specs=[big, big, big, big, pl.BlockSpec((tap_block, length), lambda b: (b, 0))],
        out_specs=[big, pl.BlockSpec((1, length), lambda b: (0, 0))],
        out_shape=[
            jax.ShapeDtypeStruct((channels, length), F32),
            jax.ShapeDtypeStruct((1, length), F32),
        ],
        compiler_params=pltpu.CompilerParams(dimension_semantics=("arbitrary",)),
    )(inputs, gate_medium, key_medium, rim, taps)


def load_values(am_ref, kl_ref, g_ref, p_ref, q_ref, vt_ref, width):
    r = lax.rsqrt((p_ref[...] + q_ref[...]) / width + EPS)
    for i in range(SUB):
        rows = slice(i * LANE, (i + 1) * LANE)
        gain = jnp.broadcast_to(g_ref[i : i + 1, :], (LANE, LANE)).T
        normed = am_ref[rows, :] * r * gain
        v = (kl_ref[rows, :].astype(F32) * normed).astype(BF16).astype(F32)
        vt_ref[pl.ds(i, LANE, stride=SUB), :] = v.T


def token_tile(ref, t):
    return ref[pl.ds(pl.multiple_of(t * SUB, SUB), SUB), :]


def final_state_kernel(width, am_ref, kl_ref, g_ref, p_ref, q_ref, lam_ref, f_ref, vt_ref):
    modes = lam_ref.shape[0]
    length = am_ref.shape[1]
    load_values(am_ref, kl_ref, g_ref, p_ref, q_ref, vt_ref, width)
    lam = [lam_ref[m] for m in range(modes)]

    def body(t, h):
        v = token_tile(vt_ref, t)
        return tuple(lam[m] * h[m] + v for m in range(modes))

    h = lax.fori_loop(0, length, body, tuple(jnp.zeros((SUB, LANE), F32) for _ in range(modes)), unroll=32)
    for m in range(modes):
        f_ref[m] = h[m].astype(f_ref.dtype)


def output_kernel(am_ref, vt_ref, gl_ref, lam_ref, w_ref, h0_ref, out_ref, yt_ref):
    modes = lam_ref.shape[0]
    length = am_ref.shape[1]
    lam = [lam_ref[m] for m in range(modes)]
    w = [w_ref[m] for m in range(modes)]

    def body(t, h):
        v = token_tile(vt_ref, t)
        h = tuple(lam[m] * h[m] + v for m in range(modes))
        y = w[0] * h[0]
        for m in range(1, modes):
            y = y + w[m] * h[m]
        yt_ref[pl.ds(pl.multiple_of(t * SUB, SUB), SUB), :] = y
        return h

    lax.fori_loop(0, length, body, tuple(h0_ref[m] for m in range(modes)), unroll=32)
    for i in range(SUB):
        rows = slice(i * LANE, (i + 1) * LANE)
        long_out = yt_ref[pl.ds(i, LANE, stride=SUB), :].T.astype(BF16).astype(F32)
        out_ref[rows, :] = (am_ref[rows, :] + gl_ref[rows, :].astype(F32) * long_out).astype(BF16)


def tiled_spec(lead):
    return pl.BlockSpec((lead, None, SUB, LANE), lambda b: (0, b, 0, 0))


def final_state_call(am, kl, gain, mine, other, lam, width):
    channels, length = am.shape
    modes = lam.shape[0]
    big = pl.BlockSpec((TILE, length), lambda b: (b, 0))
    row = pl.BlockSpec((1, length), lambda b: (0, 0))
    return pl.pallas_call(
        functools.partial(final_state_kernel, float(width)),
        grid=(channels // TILE,),
        in_specs=[big, big, pl.BlockSpec((SUB, LANE), lambda b: (b, 0)), row, row, tiled_spec(modes)],
        out_specs=[tiled_spec(modes), pl.BlockSpec((length * SUB, LANE), lambda b: (b, 0))],
        out_shape=[
            jax.ShapeDtypeStruct(lam.shape, BF16),
            jax.ShapeDtypeStruct((channels // TILE * length * SUB, LANE), F32),
        ],
    )(am, kl, gain, mine, other, lam)


def output_call(am, vt, gl, lam, w, h0):
    channels, length = am.shape
    modes = lam.shape[0]
    big = pl.BlockSpec((TILE, length), lambda b: (b, 0))
    return pl.pallas_call(
        output_kernel,
        grid=(channels // TILE,),
        in_specs=[big, pl.BlockSpec((length * SUB, LANE), lambda b: (b, 0)), big, tiled_spec(modes), tiled_spec(modes), tiled_spec(modes)],
        out_specs=big,
        out_shape=jax.ShapeDtypeStruct((channels, length), BF16),
        scratch_shapes=[pltpu.VMEM((length * SUB, LANE), F32)],
    )(am, vt, gl, lam, w, h0)


def to_tiles(a):
    channels, k = a.shape
    return a.T.reshape(k, channels // TILE, SUB, LANE)


def on_device(
    inputs,
    gate_medium,
    key_medium,
    gate_long,
    key_long,
    medium_taps,
    log_decay,
    residues,
    norm_gain,
):
    channels, length = inputs.shape
    assert length == medium_taps.shape[1]
    width = channels * lax.axis_size("tensor")
    source = inputs.astype(F32)
    values_medium = (key_medium.astype(F32) * source).astype(BF16)
    rim = shifted(values_medium, "context", 1)
    gain = norm_gain.reshape(channels // LANE, LANE)
    a_t = to_tiles(log_decay)
    lam = jnp.exp(-a_t)
    w = to_tiles(residues * jnp.sqrt(2.0 * log_decay))
    rim, a_t, lam, w = lax.optimization_barrier((rim, a_t, lam, w))
    after_medium, partial = medium_call(inputs, gate_medium, key_medium, rim, medium_taps)
    if lax.axis_size("tensor") == 2:
        other = lax.ppermute(partial, "tensor", [(0, 1), (1, 0)])
    else:
        partial, other = lax.psum(partial, "tensor"), jnp.zeros_like(partial)
    finals, vt = final_state_call(after_medium, key_long, gain, partial, other, lam, width)

    sent = finals
    carried = shifted(sent, "context", 1).astype(F32)
    distance = 1
    if lax.axis_size("context") > 2:
        decay = jnp.exp(-length * a_t)
        carried = carried + decay * shifted(sent, "context", 2).astype(F32)
        distance = 2
    while distance < lax.axis_size("context"):
        decay = jnp.exp(-(length * distance) * a_t)
        carried = carried + decay * shifted(carried.astype(BF16), "context", distance).astype(F32)
        distance *= 2

    return output_call(after_medium, vt, gate_long, lam, w, carried)


def solution(mesh):
    return jax.shard_map(
        on_device,
        mesh=mesh,
        in_specs=(
            P("tensor", ("groups", "context")),
            P("tensor", ("groups", "context")),
            P("tensor", ("groups", "context")),
            P("tensor", ("groups", "context")),
            P("tensor", ("groups", "context")),
            P("tensor", None),
            P("tensor", None),
            P("tensor", None),
            P("tensor"),
        ),
        out_specs=P("tensor", ("groups", "context")),
        check_vma=False,
    )
```

```python
import functools

import jax
import jax.numpy as jnp
from jax import lax
from jax.experimental import pallas as pl
from jax.experimental.pallas import tpu as pltpu
from jax.sharding import PartitionSpec as P

F32 = jnp.float32
BF16 = jnp.bfloat16
EPS = 1e-05
SUB, LANE = 8, 128
TILE = SUB * LANE


def shifted(block, axis, distance):
    devices = range(lax.axis_size(axis))
    route = [(i - distance, i) for i in devices if i - distance in devices]
    return lax.ppermute(block, axis, route)


def medium_kernel(x_ref, gm_ref, km_ref, rim_ref, taps_ref, am_ref, ss_ref):
    rows, length = x_ref.shape
    groups = taps_ref.shape[0]
    per_group = rows // groups
    row = lax.broadcasted_iota(jnp.int32, (length, length), 0)
    col = lax.broadcasted_iota(jnp.int32, (length, length), 1)
    upper = col >= row

    @pl.when(pl.program_id(0) == 0)
    def _():
        ss_ref[...] = jnp.zeros_like(ss_ref)

    acc = jnp.zeros((1, length), F32)
    for g in range(groups):
        lo, hi = g * per_group, (g + 1) * per_group
        taps = jnp.broadcast_to(taps_ref[g : g + 1, :].astype(F32), (length, length))
        rolled = pltpu.roll(taps, 0, 1, stride=1, stride_axis=0)
        t_cur = jnp.where(upper, rolled, 0.0).astype(BF16)
        t_rim = jnp.where(upper, 0.0, rolled).astype(BF16)
        x = x_ref[lo:hi, :].astype(F32)
        vm = (km_ref[lo:hi, :].astype(F32) * x).astype(BF16)
        ext = jnp.concatenate([rim_ref[lo:hi, :], vm], axis=1)
        conv = jnp.dot(ext, jnp.concatenate([t_rim, t_cur], axis=0), preferred_element_type=F32)
        am = x + gm_ref[lo:hi, :].astype(F32) * conv
        am_ref[lo:hi, :] = am
        acc = acc + jnp.sum(am * am, axis=0, keepdims=True)
    ss_ref[...] += acc


def medium_call(inputs, gate_medium, key_medium, rim, taps):
    channels, length = inputs.shape
    per_group = channels // taps.shape[0]
    block = 2048
    tap_block = block // per_group
    big = pl.BlockSpec((block, length), lambda b: (b, 0))
    return pl.pallas_call(
        medium_kernel,
        grid=(channels // block,),
        in_specs=[big, big, big, big, pl.BlockSpec((tap_block, length), lambda b: (b, 0))],
        out_specs=[big, pl.BlockSpec((1, length), lambda b: (0, 0))],
        out_shape=[
            jax.ShapeDtypeStruct((channels, length), F32),
            jax.ShapeDtypeStruct((1, length), F32),
        ],
        compiler_params=pltpu.CompilerParams(dimension_semantics=("arbitrary",)),
    )(inputs, gate_medium, key_medium, rim, taps)


def load_values(am_ref, kl_ref, g_ref, p_ref, q_ref, vt_ref, width):
    r = lax.rsqrt((p_ref[...] + q_ref[...]) / width + EPS)
    for i in range(SUB):
        rows = slice(i * LANE, (i + 1) * LANE)
        gain = jnp.broadcast_to(g_ref[i : i + 1, :], (LANE, LANE)).T
        normed = am_ref[rows, :] * r * gain
        v = (kl_ref[rows, :].astype(F32) * normed).astype(BF16).astype(F32)
        vt_ref[pl.ds(i, LANE, stride=SUB), :] = v.T


def token_tile(ref, t):
    return ref[pl.ds(pl.multiple_of(t * SUB, SUB), SUB), :]


def final_state_kernel(width, am_ref, kl_ref, g_ref, p_ref, q_ref, lam_ref, f_ref, vt_ref):
    modes = lam_ref.shape[0]
    length = am_ref.shape[1]
    load_values(am_ref, kl_ref, g_ref, p_ref, q_ref, vt_ref, width)
    lam = [lam_ref[m] for m in range(modes)]

    def body(t, h):
        v = token_tile(vt_ref, t)
        return tuple(lam[m] * h[m] + v for m in range(modes))

    h = lax.fori_loop(0, length, body, tuple(jnp.zeros((SUB, LANE), F32) for _ in range(modes)), unroll=64)
    for m in range(modes):
        f_ref[m] = h[m].astype(f_ref.dtype)


def output_kernel(am_ref, vt_ref, gl_ref, lam_ref, w_ref, h0_ref, out_ref, yt_ref):
    modes = lam_ref.shape[0]
    length = am_ref.shape[1]
    lam = [lam_ref[m] for m in range(modes)]
    w = [w_ref[m] for m in range(modes)]

    def body(t, h):
        v = token_tile(vt_ref, t)
        h = tuple(lam[m] * h[m] + v for m in range(modes))
        y = w[0] * h[0]
        for m in range(1, modes):
            y = y + w[m] * h[m]
        yt_ref[pl.ds(pl.multiple_of(t * SUB, SUB), SUB), :] = y
        return h

    lax.fori_loop(0, length, body, tuple(h0_ref[m] for m in range(modes)), unroll=64)
    for i in range(SUB):
        rows = slice(i * LANE, (i + 1) * LANE)
        long_out = yt_ref[pl.ds(i, LANE, stride=SUB), :].T.astype(BF16).astype(F32)
        out_ref[rows, :] = (am_ref[rows, :] + gl_ref[rows, :].astype(F32) * long_out).astype(BF16)


def tiled_spec(lead):
    return pl.BlockSpec((lead, None, SUB, LANE), lambda b: (0, b, 0, 0))


def final_state_call(am, kl, gain, mine, other, lam, width):
    channels, length = am.shape
    modes = lam.shape[0]
    big = pl.BlockSpec((TILE, length), lambda b: (b, 0))
    row = pl.BlockSpec((1, length), lambda b: (0, 0))
    return pl.pallas_call(
        functools.partial(final_state_kernel, float(width)),
        grid=(channels // TILE,),
        in_specs=[big, big, pl.BlockSpec((SUB, LANE), lambda b: (b, 0)), row, row, tiled_spec(modes)],
        out_specs=[tiled_spec(modes), pl.BlockSpec((length * SUB, LANE), lambda b: (b, 0))],
        out_shape=[
            jax.ShapeDtypeStruct(lam.shape, BF16),
            jax.ShapeDtypeStruct((channels // TILE * length * SUB, LANE), F32),
        ],
    )(am, kl, gain, mine, other, lam)


def output_call(am, vt, gl, lam, w, h0):
    channels, length = am.shape
    modes = lam.shape[0]
    big = pl.BlockSpec((TILE, length), lambda b: (b, 0))
    return pl.pallas_call(
        output_kernel,
        grid=(channels // TILE,),
        in_specs=[big, pl.BlockSpec((length * SUB, LANE), lambda b: (b, 0)), big, tiled_spec(modes), tiled_spec(modes), tiled_spec(modes)],
        out_specs=big,
        out_shape=jax.ShapeDtypeStruct((channels, length), BF16),
        scratch_shapes=[pltpu.VMEM((length * SUB, LANE), F32)],
    )(am, vt, gl, lam, w, h0)


def to_tiles(a):
    channels, k = a.shape
    return a.T.reshape(k, channels // TILE, SUB, LANE)


def on_device(
    inputs,
    gate_medium,
    key_medium,
    gate_long,
    key_long,
    medium_taps,
    log_decay,
    residues,
    norm_gain,
):
    channels, length = inputs.shape
    assert length == medium_taps.shape[1]
    width = channels * lax.axis_size("tensor")
    source = inputs.astype(F32)
    values_medium = (key_medium.astype(F32) * source).astype(BF16)
    rim = shifted(values_medium, "context", 1)
    gain = norm_gain.reshape(channels // LANE, LANE)
    a_t = to_tiles(log_decay)
    lam = jnp.exp(-a_t)
    w = to_tiles(residues * jnp.sqrt(2.0 * log_decay))
    rim, a_t, lam, w = lax.optimization_barrier((rim, a_t, lam, w))
    after_medium, partial = medium_call(inputs, gate_medium, key_medium, rim, medium_taps)
    if lax.axis_size("tensor") == 2:
        other = lax.ppermute(partial, "tensor", [(0, 1), (1, 0)])
    else:
        partial, other = lax.psum(partial, "tensor"), jnp.zeros_like(partial)
    finals, vt = final_state_call(after_medium, key_long, gain, partial, other, lam, width)

    sent = finals
    carried = shifted(sent, "context", 1).astype(F32)
    distance = 1
    if lax.axis_size("context") > 2:
        decay = jnp.exp(-length * a_t)
        carried = carried + decay * shifted(sent, "context", 2).astype(F32)
        distance = 2
    while distance < lax.axis_size("context"):
        decay = jnp.exp(-(length * distance) * a_t)
        carried = carried + decay * shifted(carried.astype(BF16), "context", distance).astype(F32)
        distance *= 2

    return output_call(after_medium, vt, gate_long, lam, w, carried)


def solution(mesh):
    return jax.shard_map(
        on_device,
        mesh=mesh,
        in_specs=(
            P("tensor", ("groups", "context")),
            P("tensor", ("groups", "context")),
            P("tensor", ("groups", "context")),
            P("tensor", ("groups", "context")),
            P("tensor", ("groups", "context")),
            P("tensor", None),
            P("tensor", None),
            P("tensor", None),
            P("tensor"),
        ),
        out_specs=P("tensor", ("groups", "context")),
        check_vma=False,
    )
```
